32 devices in a mesh: ctx: 4 (over y, x), tp: 8 (over z, core).
Axes of the slice: x: 2, y: 2, z: 4, core: 2. Of those that a mesh axis runs over, the one named last changes fastest.
Arguments:
- resid: bfloat16 [1024, 4096], P('ctx', 'tp'), may hold values from -6 to 6
- attn_gain: bfloat16 [4096], replicated, may hold values from 0.5 to 1.5
- mlp_gain: bfloat16 [4096], replicated, may hold values from 0.5 to 1.5
- w_query: bfloat16 [4096, 4096], P(None, 'tp'), may hold values from -0.09375 to 0.09375
- w_kv: bfloat16 [4096, 1024], P(None, 'tp'), may hold values from -0.09375 to 0.09375
- w_out: bfloat16 [4096, 4096], P('tp'), may hold values from -0.09375 to 0.09375
- w_gate: bfloat16 [4096, 11008], P(None, 'tp'), may hold values from -0.09375 to 0.09375
- w_up: bfloat16 [4096, 11008], P(None, 'tp'), may hold values from -0.09375 to 0.09375
- w_down: bfloat16 [11008, 4096], P('tp'), may hold values from -0.0546875 to 0.0546875
- kv_cache: bfloat16 [32, 128, 1024], P('ctx'), may hold values from -70 to 70
- cache_len: int32 [4], replicated, may hold values from 1 to 2048
- span_len: int32 [4], replicated, may hold values from 1 to 256
- slot_req: int32 [32], P('ctx'), may hold values from 0 to 4, as said below
- slot_blk: int32 [32], P('ctx'), may hold values from 0 to 15, as said below
Outputs:
- layer_out: bfloat16 [1024, 4096], P('ctx', 'tp')
- new_kv: bfloat16 [1024, 1024], P('ctx', 'tp')
The draws below stay inside these ranges and needn't reach their ends.
Inputs may be any that keep to these rules, and one draw needn't show every extreme that they name: `slot_req`: each request r holds ceil(cache_len[r] / 128) blocks, and each of its blocks stands in exactly one slot; every other slot is empty. `slot_blk`: block numbers of live slots are below their request's block count; empty slots carry 0.
All inputs are finite; a program needn't handle non-finite values.
Results may differ from the reference program's by a relative error of at most 0.035.
Values may be sent and summed in bfloat16 or wider, within the bound.
No kernel may reach another device: no remote copies, remote signals or barrier semaphores. Data moves between devices by JAX's collectives and lax.ppermute only.
A program may use at most 128 MiB of HBM per device.

```python
import jax
import jax.numpy as jnp
from jax import lax

D = 4096
HQ = 32
KVH = 4
HD = 128
FF = 11008
SPAN = 256
BLK = 128
SLOTS = 8
REQS = 4
TOKENS = 1024
SLOTS_ALL = 32
N_CTX = 4
N_TP = 8


def slot_layout(key):
    total_slots = SLOTS * N_CTX
    requests = N_CTX
    longest = total_slots // 2
    others = total_slots - longest - total_slots // 8
    pick_key, weight_key, tail_key, perm_key = jax.random.split(jax.random.fold_in(key, 7), 4)
    req_ids = jnp.arange(requests, dtype=jnp.int32)
    long_req = jax.random.randint(pick_key, (), 0, requests)
    weights = jax.random.randint(weight_key, (requests,), 1, 9)
    weights = jnp.where(req_ids == long_req, 0, weights)
    spare = others - (requests - 1)
    blocks = 1 + weights * spare // jnp.maximum(jnp.sum(weights), 1)
    blocks = jnp.where(req_ids == long_req, longest, blocks).astype(jnp.int32)
    tails = jax.random.randint(tail_key, (requests,), 1, BLK + 1)
    tails = jnp.where(req_ids == long_req, BLK, tails)
    lengths = ((blocks - 1) * BLK + tails).astype(jnp.int32)
    perm = jax.random.permutation(perm_key, total_slots)
    rank = jnp.argsort(perm, stable=True).astype(jnp.int32)
    ends = jnp.cumsum(blocks).astype(jnp.int32)
    live_count = ends[requests - 1]
    owner = jnp.sum((rank[:, None] >= ends[None, :]).astype(jnp.int32), axis=1)
    live = rank < live_count
    safe_owner = jnp.minimum(owner, requests - 1)
    number = rank - (ends[safe_owner] - blocks[safe_owner])
    slot_owner = jnp.where(live, safe_owner, requests).astype(jnp.int32)
    slot_number = jnp.where(live, number, 0).astype(jnp.int32)
    return (lengths, slot_owner, slot_number)


def draw_cache_len(key, part):
    return slot_layout(key)[0]


def draw_slot_req(key, part):
    return slot_layout(key)[1]


def draw_slot_blk(key, part):
    return slot_layout(key)[2]


def draw_span_len(key, part):
    pick_key, len_key = jax.random.split(jax.random.fold_in(key, 11), 2)
    full_req = jax.random.randint(pick_key, (), 0, N_CTX)
    counts = jax.random.randint(len_key, (N_CTX,), 1, SPAN + 1)
    return jnp.where(jnp.arange(N_CTX, dtype=jnp.int32) == full_req, SPAN, counts).astype(jnp.int32)


def draw_kv_cache(key, part):
    base_key = jax.random.fold_in(jax.random.fold_in(key, 13), 0)
    shape = (SLOTS * N_CTX, BLK, 2 * KVH * HD)
    values = jnp.clip(jax.random.normal(base_key, shape, jnp.float32), -6.0, 6.0)
    return values.astype(jnp.bfloat16)


def level_of(stream_key, dims, shards, low, largest):
    loudness = 1.0
    for axis_at, parts in shards:
        heights = jax.random.uniform(jax.random.fold_in(jax.random.fold_in(stream_key, 6), axis_at), (parts,), jnp.float32, low / len(shards), largest / len(shards))
        loudness = loudness * jnp.repeat(jnp.exp(heights), dims[axis_at] // parts).reshape((-1,) + (1,) * (len(dims) - 1 - axis_at))
    return loudness


def centred(rng, shape, scale, bound, shards=(), held_as=jnp.bfloat16):
    entries = jax.random.normal(rng, shape, jnp.float32) * scale
    if len(shards) > 0:
        entries = level_of(rng, shape, shards, -0.22, 0.18) * entries
    return jnp.clip(entries, min=-bound, max=bound).astype(held_as)


def setup_inputs(seed: int = 0) -> dict:
    key_list = jax.random.split(jax.random.key(seed), 15)
    resid = centred(key_list[0], (TOKENS, D), 1.0, 6.0, ((0, 4), (1, 8)))
    attn_gain = jnp.clip(1.0 + 0.1 * jax.random.normal(key_list[1], (D,), jnp.float32), 0.5, 1.5).astype(jnp.bfloat16)
    mlp_gain = jnp.clip(1.0 + 0.1 * jax.random.normal(key_list[2], (D,), jnp.float32), 0.5, 1.5).astype(jnp.bfloat16)
    w_query = centred(key_list[3], (D, HQ * HD), D ** -0.5, 0.09375, ((1, 8),))
    w_kv = centred(key_list[4], (D, 2 * KVH * HD), D ** -0.5, 0.09375, ((1, 8),))
    w_out = centred(key_list[5], (HQ * HD, D), (HQ * HD) ** -0.5, 0.09375, ((0, 8),))
    w_gate = centred(key_list[6], (D, FF), D ** -0.5, 0.09375, ((1, 8),))
    w_up = centred(key_list[7], (D, FF), D ** -0.5, 0.09375, ((1, 8),))
    w_down = centred(key_list[8], (FF, D), FF ** -0.5, 0.0546875, ((0, 8),))
    kv_cache = draw_kv_cache(jax.random.fold_in(key_list[14], 71), 0)
    cache_len = draw_cache_len(jax.random.fold_in(key_list[14], 71), 0)
    span_len = draw_span_len(jax.random.fold_in(key_list[14], 71), 0)
    slot_req = draw_slot_req(jax.random.fold_in(key_list[14], 71), 0)
    slot_blk = draw_slot_blk(jax.random.fold_in(key_list[14], 71), 0)
    return dict(resid=resid, attn_gain=attn_gain, mlp_gain=mlp_gain, w_query=w_query, w_kv=w_kv, w_out=w_out, w_gate=w_gate, w_up=w_up, w_down=w_down, kv_cache=kv_cache, cache_len=cache_len, span_len=span_len, slot_req=slot_req, slot_blk=slot_blk)


THETA = 5000000.0
EPS = 1e-05
NEG = -1e+30

def rms_norm(values, gain):
    wide = values.astype(jnp.float32)
    factor = lax.rsqrt(lax.optimization_barrier(jnp.mean(wide * wide, axis=-1, keepdims=True)) + EPS)
    return (wide * factor * gain.astype(jnp.float32)).astype(jnp.bfloat16)

def rotate(vectors, positions):
    width = vectors.shape[-1]
    half = width // 2
    freqs = THETA ** (-(jnp.arange(half, dtype=jnp.float32) * 2.0 / width))
    angles = positions.astype(jnp.float32)[:, None] * freqs[None, :]
    cosine = jnp.cos(angles)[:, None, :]
    sine = jnp.sin(angles)[:, None, :]
    first = vectors[..., :half]
    second = vectors[..., half:]
    return jnp.concatenate([first * cosine - second * sine, second * cosine + first * sine], axis=-1)

def block_sum(left, right, pieces):
    width = left.shape[1] // pieces

    def add_block(index, total):
        start = (index * width).astype(jnp.int32)
        left_cols = lax.dynamic_slice_in_dim(left, start, width, 1)
        right_rows = lax.dynamic_slice_in_dim(right, start, width, 0)
        partial_value = jnp.dot(left_cols, right_rows, preferred_element_type=jnp.float32).astype(jnp.bfloat16)
        partial_value = lax.optimization_barrier(partial_value)
        return total + partial_value.astype(jnp.float32)
    return lax.fori_loop(jnp.int32(0), jnp.int32(pieces), add_block, jnp.zeros((left.shape[0], right.shape[1]), jnp.float32))

def reference(resid, attn_gain, mlp_gain, w_query, w_kv, w_out, w_gate, w_up, w_down, kv_cache, cache_len, span_len, slot_req, slot_blk):
    tokens = resid.shape[0]
    x_norm = rms_norm(resid, attn_gain)
    query_raw = jnp.dot(x_norm, w_query, preferred_element_type=jnp.float32)
    kv_raw = jnp.dot(x_norm, w_kv, preferred_element_type=jnp.float32).astype(jnp.bfloat16)
    token_ids = jnp.arange(tokens, dtype=jnp.int32)
    token_req = token_ids // SPAN
    token_off = token_ids % SPAN
    positions = cache_len[token_req] + token_off
    live_tok = token_off < span_len[token_req]
    query = rotate(query_raw.reshape(tokens, HQ, HD), positions).astype(jnp.bfloat16)
    new_keys = rotate(kv_raw[:, :KVH * HD].astype(jnp.float32).reshape(tokens, KVH, HD), positions).astype(jnp.bfloat16)
    new_vals = kv_raw[:, KVH * HD:].reshape(tokens, KVH, HD)
    joined = jnp.concatenate([new_keys.reshape(tokens, KVH * HD), new_vals.reshape(tokens, KVH * HD)], axis=1)
    new_kv = jnp.where(live_tok[:, None], joined, jnp.zeros_like(joined))
    cache_keys = kv_cache[:, :, :KVH * HD].reshape(SLOTS_ALL * BLK, KVH, HD)
    cache_vals = kv_cache[:, :, KVH * HD:].reshape(SLOTS_ALL * BLK, KVH, HD)
    key_req = jnp.repeat(slot_req, BLK)
    key_pos = (slot_blk[:, None] * BLK + jnp.arange(BLK, dtype=jnp.int32)[None, :]).reshape(-1)
    offsets = jnp.arange(SPAN, dtype=jnp.int32)
    scale = HD ** (-0.5)
    group_size = HQ // KVH

    def one_head(pair):
        request = pair // HQ
        head = pair % HQ
        group = head // group_size
        start = (request * SPAN).astype(jnp.int32)
        rows = lax.dynamic_index_in_dim(lax.dynamic_slice_in_dim(query, start, SPAN, 0), head, 1, keepdims=False)
        req_keys = lax.dynamic_slice_in_dim(new_keys, start, SPAN, 0)
        req_vals = lax.dynamic_slice_in_dim(new_vals, start, SPAN, 0)
        keys = jnp.concatenate([lax.dynamic_index_in_dim(cache_keys, group, 1, keepdims=False), lax.dynamic_index_in_dim(req_keys, group, 1, keepdims=False)], axis=0)
        vals = jnp.concatenate([lax.dynamic_index_in_dim(cache_vals, group, 1, keepdims=False), lax.dynamic_index_in_dim(req_vals, group, 1, keepdims=False)], axis=0)
        cache_ok = (key_req == request) & (key_pos < cache_len[request])
        new_ok = (offsets[None, :] <= offsets[:, None]) & (offsets[None, :] < span_len[request])
        valid = jnp.concatenate([jnp.broadcast_to(cache_ok[None, :], (SPAN, cache_ok.shape[0])), new_ok], axis=1)
        scores = jnp.dot(rows, keys.T, preferred_element_type=jnp.float32) * scale
        peak = lax.optimization_barrier(jnp.max(jnp.where(valid, scores, NEG), axis=1, keepdims=True))
        weights = jnp.where(valid, jnp.exp(scores - peak), 0.0)
        total = lax.optimization_barrier(jnp.sum(weights, axis=1, keepdims=True))
        summed = jnp.dot(weights.astype(jnp.bfloat16), vals, preferred_element_type=jnp.float32)
        return summed / total
    heads_out = lax.map(one_head, jnp.arange(REQS * HQ, dtype=jnp.int32))
    attn = heads_out.reshape(REQS, HQ, SPAN, HD).transpose(0, 2, 1, 3).reshape(tokens, HQ * HD).astype(jnp.bfloat16)
    mid = (resid.astype(jnp.float32) + block_sum(attn, w_out, N_TP)).astype(jnp.bfloat16)
    x_two = rms_norm(mid, mlp_gain)
    gate = jnp.dot(x_two, w_gate, preferred_element_type=jnp.float32)
    up_part = jnp.dot(x_two, w_up, preferred_element_type=jnp.float32)
    hidden = (jax.nn.silu(gate) * up_part).astype(jnp.bfloat16)
    layer_out = (mid.astype(jnp.float32) + block_sum(hidden, w_down, N_TP)).astype(jnp.bfloat16)
    layer_out = jnp.where(live_tok[:, None], layer_out, jnp.zeros_like(layer_out))
    return (layer_out, new_kv)
```

```python
import jax
import jax.numpy as jnp
from jax import lax
from jax.sharding import PartitionSpec as P

HQ = 32
KVH = 4
HD = 128
BLK = 128


THETA = 5000000.0
EPS = 1e-05
NEG = -1e30


def rms_norm(values, gain):
    wide = values.astype(jnp.float32)
    factor = lax.rsqrt(jnp.mean(wide * wide, axis=-1, keepdims=True) + EPS)
    return (wide * factor * gain.astype(jnp.float32)).astype(jnp.bfloat16)


def rotate(vectors, positions):
    width = vectors.shape[-1]
    half = width // 2
    freqs = THETA ** (-(jnp.arange(half, dtype=jnp.float32) * 2.0 / width))
    angles = positions.astype(jnp.float32)[:, None] * freqs[None, :]
    cosine = jnp.cos(angles)[:, None, :]
    sine = jnp.sin(angles)[:, None, :]
    first = vectors[..., :half]
    second = vectors[..., half:]
    return jnp.concatenate(
        [first * cosine - second * sine, second * cosine + first * sine], axis=-1
    )


def column_term(rows, weight):
    return lax.dot_general(
        weight, rows, (((0,), (1,)), ((), ())), preferred_element_type=jnp.float32
    )


def gather_ctx(value, count):
    parts = [value]
    for shift in range(1, count):
        pairs = [(i, (i + shift) % count) for i in range(count)]
        parts.append(lax.ppermute(value, "ctx", pairs))
    return parts


def per_device(
    resid,
    attn_gain,
    mlp_gain,
    w_query,
    w_kv,
    w_out,
    w_gate,
    w_up,
    w_down,
    kv_cache,
    cache_len,
    span_len,
    slot_req,
    slot_blk,
):
    span_size = resid.shape[0]
    ctx_count = lax.axis_size("ctx")
    q_cols = w_query.shape[1]
    heads_dev = q_cols // HD
    ctx_rank = lax.axis_index("ctx")
    tp_rank = lax.axis_index("tp")
    group = tp_rank * heads_dev // (HQ // KVH)
    my_len = cache_len[ctx_rank]
    my_span = span_len[ctx_rank]
    offsets = jnp.arange(span_size, dtype=jnp.int32)
    positions = my_len + offsets
    live_rows = offsets < my_span

    own_cache = jnp.concatenate(
        [
            lax.dynamic_slice_in_dim(kv_cache, group * HD, HD, 2),
            lax.dynamic_slice_in_dim(kv_cache, KVH * HD + group * HD, HD, 2),
        ],
        axis=2,
    )
    own_meta = jnp.stack([slot_req, slot_blk])
    cache_all = jnp.concatenate(gather_ctx(own_cache, ctx_count), axis=0)
    meta_all = jnp.concatenate(gather_ctx(own_meta, ctx_count), axis=1)

    full_resid = lax.all_gather(resid, "tp", axis=1, tiled=True)
    x_norm = rms_norm(full_resid, attn_gain)
    query = rotate(
        jnp.dot(x_norm, w_query, preferred_element_type=jnp.float32).reshape(
            span_size, heads_dev, HD
        ),
        positions,
    ).astype(jnp.bfloat16)
    kv_piece = jnp.dot(x_norm, w_kv, preferred_element_type=jnp.float32).astype(jnp.bfloat16)
    kv_width = kv_piece.shape[1]
    kv_all = lax.all_gather(kv_piece, "tp", axis=1, tiled=True)
    all_keys = rotate(
        kv_all[:, : KVH * HD].astype(jnp.float32).reshape(span_size, KVH, HD), positions
    ).astype(jnp.bfloat16)
    joined = jnp.concatenate([all_keys.reshape(span_size, KVH * HD), kv_all[:, KVH * HD :]], axis=1)
    mine = lax.dynamic_slice_in_dim(joined, tp_rank * kv_width, kv_width, 1)
    new_kv = jnp.where(live_rows[:, None], mine, jnp.zeros_like(mine))
    new_keys = lax.dynamic_index_in_dim(all_keys, group, 1, keepdims=False)
    new_vals = lax.dynamic_slice_in_dim(kv_all, KVH * HD + group * HD, HD, 1)

    cache_rows = cache_all.shape[0] * BLK
    keys = jnp.concatenate([cache_all[..., :HD].reshape(cache_rows, HD), new_keys], axis=0)
    vals = jnp.concatenate([cache_all[..., HD:].reshape(cache_rows, HD), new_vals], axis=0)
    key_pos = meta_all[1][:, None] * BLK + jnp.arange(BLK, dtype=jnp.int32)[None, :]
    cache_ok = ((meta_all[0][:, None] == ctx_rank) & (key_pos < my_len)).reshape(cache_rows)
    new_ok = (offsets[None, :] <= offsets[:, None]) & (offsets[None, :] < my_span)
    valid = jnp.concatenate(
        [jnp.broadcast_to(cache_ok[None, :], (span_size, cache_rows)), new_ok], axis=1
    )
    scores = jnp.einsum(
        "chd,kd->hck", query, keys, preferred_element_type=jnp.float32
    ) * HD ** (-0.5)
    peak = jnp.max(jnp.where(valid[None], scores, NEG), axis=2)
    weights = jnp.where(valid[None], jnp.exp(scores - peak[..., None]), 0.0)
    total = jnp.sum(weights, axis=2)
    summed = jnp.einsum(
        "hck,kd->hcd", weights.astype(jnp.bfloat16), vals, preferred_element_type=jnp.float32
    )
    attn_rows = (
        (summed / total[..., None])
        .transpose(1, 0, 2)
        .reshape(span_size, q_cols)
        .astype(jnp.bfloat16)
    )
    head_sum = lax.psum_scatter(
        column_term(attn_rows, w_out).astype(jnp.bfloat16), "tp", scatter_dimension=0, tiled=True
    ).astype(jnp.float32)
    mid = (resid.astype(jnp.float32) + head_sum.T).astype(jnp.bfloat16)
    full_mid = lax.all_gather(mid, "tp", axis=1, tiled=True)
    x_two = rms_norm(full_mid, mlp_gain)
    gate = jnp.dot(x_two, w_gate, preferred_element_type=jnp.float32)
    up_part = jnp.dot(x_two, w_up, preferred_element_type=jnp.float32)
    hidden = (jax.nn.silu(gate) * up_part).astype(jnp.bfloat16)
    down_sum = lax.psum_scatter(
        column_term(hidden, w_down).astype(jnp.bfloat16), "tp", scatter_dimension=0, tiled=True
    ).astype(jnp.float32)
    layer_out = (mid.astype(jnp.float32) + down_sum.T).astype(jnp.bfloat16)
    layer_out = jnp.where(live_rows[:, None], layer_out, jnp.zeros_like(layer_out))
    return (layer_out, new_kv)


def solution(mesh):
    return jax.shard_map(
        per_device,
        mesh=mesh,
        in_specs=(
            P("ctx", "tp"),
            P(),
            P(),
            P(None, "tp"),
            P(None, "tp"),
            P("tp", None),
            P(None, "tp"),
            P(None, "tp"),
            P("tp", None),
            P("ctx", None, None),
            P(),
            P(),
            P("ctx"),
            P("ctx"),
        ),
        out_specs=(P("ctx", "tp"), P("ctx", "tp")),
        check_vma=False,
    )
```

```python
import jax
import jax.numpy as jnp
from jax import lax
from jax.sharding import PartitionSpec as P

HQ = 32
KVH = 4
HD = 128
BLK = 128


THETA = 5000000.0
EPS = 1e-05
NEG = -1e30


def rms_norm(values, gain):
    wide = values.astype(jnp.float32)
    factor = lax.rsqrt(jnp.mean(wide * wide, axis=-1, keepdims=True) + EPS)
    return (wide * factor * gain.astype(jnp.float32)).astype(jnp.bfloat16)


def rotate(vectors, positions):
    width = vectors.shape[-1]
    half = width // 2
    freqs = THETA ** (-(jnp.arange(half, dtype=jnp.float32) * 2.0 / width))
    angles = positions.astype(jnp.float32)[:, None] * freqs[None, :]
    cosine = jnp.cos(angles)[:, None, :]
    sine = jnp.sin(angles)[:, None, :]
    first = vectors[..., :half]
    second = vectors[..., half:]
    return jnp.concatenate(
        [first * cosine - second * sine, second * cosine + first * sine], axis=-1
    )


def column_term(rows, weight):
    return lax.dot_general(
        weight, rows, (((0,), (1,)), ((), ())), preferred_element_type=jnp.float32
    )


def gather_ctx(value, count):
    parts = [value]
    for shift in range(1, count):
        pairs = [(i, (i + shift) % count) for i in range(count)]
        parts.append(lax.ppermute(value, "ctx", pairs))
    return parts


def per_device(
    resid,
    attn_gain,
    mlp_gain,
    w_query,
    w_kv,
    w_out,
    w_gate,
    w_up,
    w_down,
    kv_cache,
    cache_len,
    span_len,
    slot_req,
    slot_blk,
):
    span_size = resid.shape[0]
    ctx_count = lax.axis_size("ctx")
    q_cols = w_query.shape[1]
    heads_dev = q_cols // HD
    ctx_rank = lax.axis_index("ctx")
    tp_rank = lax.axis_index("tp")
    group = tp_rank * heads_dev // (HQ // KVH)
    my_len = cache_len[ctx_rank]
    my_span = span_len[ctx_rank]
    offsets = jnp.arange(span_size, dtype=jnp.int32)
    positions = my_len + offsets
    live_rows = offsets < my_span

    own_cache = jnp.concatenate(
        [
            lax.dynamic_slice_in_dim(kv_cache, group * HD, HD, 2),
            lax.dynamic_slice_in_dim(kv_cache, KVH * HD + group * HD, HD, 2),
        ],
        axis=2,
    )
    own_meta = jnp.stack([slot_req, slot_blk])
    cache_all = jnp.concatenate(gather_ctx(own_cache, ctx_count), axis=0)
    meta_all = jnp.concatenate(gather_ctx(own_meta, ctx_count), axis=1)

    full_resid = lax.all_gather(resid, "tp", axis=1, tiled=True)
    x_norm = rms_norm(full_resid, attn_gain)
    query = rotate(
        jnp.dot(x_norm, w_query, preferred_element_type=jnp.float32).reshape(
            span_size, heads_dev, HD
        ),
        positions,
    ).astype(jnp.bfloat16)
    kv_piece = jnp.dot(x_norm, w_kv, preferred_element_type=jnp.float32).astype(jnp.bfloat16)
    kv_width = kv_piece.shape[1]
    kv_all = lax.all_gather(kv_piece, "tp", axis=1, tiled=True)
    all_keys = rotate(
        kv_all[:, : KVH * HD].astype(jnp.float32).reshape(span_size, KVH, HD), positions
    ).astype(jnp.bfloat16)
    joined = jnp.concatenate([all_keys.reshape(span_size, KVH * HD), kv_all[:, KVH * HD :]], axis=1)
    mine = lax.dynamic_slice_in_dim(joined, tp_rank * kv_width, kv_width, 1)
    new_kv = jnp.where(live_rows[:, None], mine, jnp.zeros_like(mine))
    new_keys = lax.dynamic_index_in_dim(all_keys, group, 1, keepdims=False)
    new_vals = lax.dynamic_slice_in_dim(kv_all, KVH * HD + group * HD, HD, 1)

    cache_rows = cache_all.shape[0] * BLK
    keys = jnp.concatenate([cache_all[..., :HD].reshape(cache_rows, HD), new_keys], axis=0)
    vals = jnp.concatenate([cache_all[..., HD:].reshape(cache_rows, HD), new_vals], axis=0)
    key_pos = meta_all[1][:, None] * BLK + jnp.arange(BLK, dtype=jnp.int32)[None, :]
    cache_ok = ((meta_all[0][:, None] == ctx_rank) & (key_pos < my_len)).reshape(cache_rows)
    new_ok = (offsets[None, :] <= offsets[:, None]) & (offsets[None, :] < my_span)
    valid = jnp.concatenate(
        [jnp.broadcast_to(cache_ok[None, :], (span_size, cache_rows)), new_ok], axis=1
    )
    scores = jnp.einsum(
        "chd,kd->hck", query, keys, preferred_element_type=jnp.float32
    ) * HD ** (-0.5)
    peak = jnp.max(jnp.where(valid[None], scores, NEG), axis=2)
    weights = jnp.where(valid[None], jnp.exp(scores - peak[..., None]), 0.0)
    total = jnp.sum(weights, axis=2)
    summed = jnp.einsum(
        "hck,kd->hcd", weights.astype(jnp.bfloat16), vals, preferred_element_type=jnp.float32
    )
    attn_rows = (
        (summed / total[..., None])
        .transpose(1, 0, 2)
        .reshape(span_size, q_cols)
        .astype(jnp.bfloat16)
    )
    head_sum = lax.psum(
        jnp.dot(attn_rows, w_out, preferred_element_type=jnp.float32).astype(jnp.bfloat16), "tp"
    )
    full_mid = (full_resid.astype(jnp.float32) + head_sum.astype(jnp.float32)).astype(jnp.bfloat16)
    mid = lax.dynamic_slice_in_dim(full_mid, tp_rank * resid.shape[1], resid.shape[1], 1)
    x_two = rms_norm(full_mid, mlp_gain)
    gate = jnp.dot(x_two, w_gate, preferred_element_type=jnp.float32)
    up_part = jnp.dot(x_two, w_up, preferred_element_type=jnp.float32)
    hidden = (jax.nn.silu(gate) * up_part).astype(jnp.bfloat16)
    down_sum = lax.psum_scatter(
        column_term(hidden, w_down).astype(jnp.bfloat16), "tp", scatter_dimension=0, tiled=True
    ).astype(jnp.float32)
    layer_out = (mid.astype(jnp.float32) + down_sum.T).astype(jnp.bfloat16)
    layer_out = jnp.where(live_rows[:, None], layer_out, jnp.zeros_like(layer_out))
    return (layer_out, new_kv)


def solution(mesh):
    return jax.shard_map(
        per_device,
        mesh=mesh,
        in_specs=(
            P("ctx", "tp"),
            P(),
            P(),
            P(None, "tp"),
            P(None, "tp"),
            P("tp", None),
            P(None, "tp"),
            P(None, "tp"),
            P("tp", None),
            P("ctx", None, None),
            P(),
            P(),
            P("ctx"),
            P("ctx"),
        ),
        out_specs=(P("ctx", "tp"), P("ctx", "tp")),
        check_vma=False,
    )
```

```python
import jax
import jax.numpy as jnp
from jax import lax
from jax.sharding import PartitionSpec as P
from jax.experimental import pallas as pl
from jax.experimental.pallas import tpu as pltpu

HQ = 32
KVH = 4
HD = 128
BLK = 128


THETA = 5000000.0
EPS = 1e-05
NEG = -1e30


def rms_norm(values, gain):
    wide = values.astype(jnp.float32)
    factor = lax.rsqrt(jnp.mean(wide * wide, axis=-1, keepdims=True) + EPS)
    return (wide * factor * gain.astype(jnp.float32)).astype(jnp.bfloat16)


def rotate(vectors, positions):
    width = vectors.shape[-1]
    half = width // 2
    freqs = THETA ** (-(jnp.arange(half, dtype=jnp.float32) * 2.0 / width))
    angles = positions.astype(jnp.float32)[:, None] * freqs[None, :]
    cosine = jnp.cos(angles)[:, None, :]
    sine = jnp.sin(angles)[:, None, :]
    first = vectors[..., :half]
    second = vectors[..., half:]
    return jnp.concatenate(
        [first * cosine - second * sine, second * cosine + first * sine], axis=-1
    )


def column_term(rows, weight):
    return lax.dot_general(
        weight, rows, (((0,), (1,)), ((), ())), preferred_element_type=jnp.float32
    )


def attn_kernel(limit_ref, span_ref, q_ref, cache_ref, nk_ref, nv_ref, o_ref, m_scr, t_scr, acc_scr):
    slots = cache_ref.shape[0]
    span_size = nk_ref.shape[0]
    heads = q_ref.shape[0] // span_size
    scale = HD ** (-0.5)
    q_all = q_ref[...]
    col = lax.broadcasted_iota(jnp.int32, (1, BLK), 1)
    row_i = lax.broadcasted_iota(jnp.int32, (span_size, span_size), 0)
    col_j = lax.broadcasted_iota(jnp.int32, (span_size, span_size), 1)
    new_ok = (col_j <= row_i) & (col_j < span_ref[0])
    dims = (((1,), (1,)), ((), ()))

    def cache_scores(s):
        keys = cache_ref[s, :, :HD]
        return lax.dot_general(q_all, keys, dims, preferred_element_type=jnp.float32) * scale

    def new_scores(h):
        rows = q_ref[h * span_size : (h + 1) * span_size, :]
        return lax.dot_general(rows, nk_ref[...], dims, preferred_element_type=jnp.float32) * scale

    m_scr[...] = jnp.full(m_scr.shape, NEG, jnp.float32)

    def max_step(s, carry):
        lim = limit_ref[s]

        @pl.when(lim > 0)
        def _():
            sc = jnp.where(col < lim, cache_scores(s), NEG)
            m_scr[...] = jnp.maximum(m_scr[...], jnp.max(sc, axis=1, keepdims=True))

        return carry

    lax.fori_loop(0, slots, max_step, 0)
    for h in range(heads):
        part = slice(h * span_size, (h + 1) * span_size)
        sc = jnp.where(new_ok, new_scores(h), NEG)
        m_scr[part, :] = jnp.maximum(m_scr[part, :], jnp.max(sc, axis=1, keepdims=True))

    t_scr[...] = jnp.zeros(t_scr.shape, jnp.float32)
    acc_scr[...] = jnp.zeros(acc_scr.shape, jnp.float32)

    def sum_step(s, carry):
        lim = limit_ref[s]

        @pl.when(lim > 0)
        def _():
            w = jnp.where(col < lim, jnp.exp(cache_scores(s) - m_scr[...]), 0.0)
            t_scr[...] += jnp.sum(w, axis=1, keepdims=True)
            acc_scr[...] += jnp.dot(
                w.astype(jnp.bfloat16), cache_ref[s, :, HD:], preferred_element_type=jnp.float32
            )

        return carry

    lax.fori_loop(0, slots, sum_step, 0)
    for h in range(heads):
        part = slice(h * span_size, (h + 1) * span_size)
        w = jnp.where(new_ok, jnp.exp(new_scores(h) - m_scr[part, :]), 0.0)
        t_scr[part, :] += jnp.sum(w, axis=1, keepdims=True)
        acc_scr[part, :] += jnp.dot(
            w.astype(jnp.bfloat16), nv_ref[...], preferred_element_type=jnp.float32
        )
    o_ref[...] = (acc_scr[...] / t_scr[...]).astype(o_ref.dtype)


def local_attention(limit, span, q_rows, cache_all, new_keys, new_vals):
    rows = q_rows.shape[0]

    def whole(shape):
        return pl.BlockSpec(shape, lambda i, *_: (0,) * len(shape))

    return pl.pallas_call(
        attn_kernel,
        out_shape=jax.ShapeDtypeStruct((rows, HD), jnp.bfloat16),
        grid_spec=pltpu.PrefetchScalarGridSpec(
            num_scalar_prefetch=2,
            grid=(1,),
            in_specs=[
                whole(q_rows.shape),
                whole(cache_all.shape),
                whole(new_keys.shape),
                whole(new_vals.shape),
            ],
            out_specs=whole((rows, HD)),
            scratch_shapes=[
                pltpu.VMEM((rows, 1), jnp.float32),
                pltpu.VMEM((rows, 1), jnp.float32),
                pltpu.VMEM((rows, HD), jnp.float32),
            ],
        ),
    )(limit, span, q_rows, cache_all, new_keys, new_vals)


def gather_ctx(value, count):
    parts = [value]
    for shift in range(1, count):
        pairs = [(i, (i + shift) % count) for i in range(count)]
        parts.append(lax.ppermute(value, "ctx", pairs))
    return parts


def per_device(
    resid,
    attn_gain,
    mlp_gain,
    w_query,
    w_kv,
    w_out,
    w_gate,
    w_up,
    w_down,
    kv_cache,
    cache_len,
    span_len,
    slot_req,
    slot_blk,
):
    span_size = resid.shape[0]
    ctx_count = lax.axis_size("ctx")
    q_cols = w_query.shape[1]
    heads_dev = q_cols // HD
    ctx_rank = lax.axis_index("ctx")
    tp_rank = lax.axis_index("tp")
    group = tp_rank * heads_dev // (HQ // KVH)
    my_len = cache_len[ctx_rank]
    my_span = span_len[ctx_rank]
    offsets = jnp.arange(span_size, dtype=jnp.int32)
    positions = my_len + offsets
    live_rows = offsets < my_span

    own_cache = jnp.concatenate(
        [
            lax.dynamic_slice_in_dim(kv_cache, group * HD, HD, 2),
            lax.dynamic_slice_in_dim(kv_cache, KVH * HD + group * HD, HD, 2),
        ],
        axis=2,
    )
    own_meta = jnp.stack([slot_req, slot_blk])
    cache_all = jnp.concatenate(gather_ctx(own_cache, ctx_count), axis=0)
    meta_all = jnp.concatenate(gather_ctx(own_meta, ctx_count), axis=1)

    full_resid = lax.all_gather(resid, "tp", axis=1, tiled=True)
    x_norm = rms_norm(full_resid, attn_gain)
    query = rotate(
        jnp.dot(x_norm, w_query, preferred_element_type=jnp.float32).reshape(
            span_size, heads_dev, HD
        ),
        positions,
    ).astype(jnp.bfloat16)
    kv_piece = jnp.dot(x_norm, w_kv, preferred_element_type=jnp.float32).astype(jnp.bfloat16)
    kv_width = kv_piece.shape[1]
    kv_all = lax.all_gather(kv_piece, "tp", axis=1, tiled=True)
    all_keys = rotate(
        kv_all[:, : KVH * HD].astype(jnp.float32).reshape(span_size, KVH, HD), positions
    ).astype(jnp.bfloat16)
    joined = jnp.concatenate([all_keys.reshape(span_size, KVH * HD), kv_all[:, KVH * HD :]], axis=1)
    mine = lax.dynamic_slice_in_dim(joined, tp_rank * kv_width, kv_width, 1)
    new_kv = jnp.where(live_rows[:, None], mine, jnp.zeros_like(mine))
    new_keys = lax.dynamic_index_in_dim(all_keys, group, 1, keepdims=False)
    new_vals = lax.dynamic_slice_in_dim(kv_all, KVH * HD + group * HD, HD, 1)

    limit = jnp.where(
        meta_all[0] == ctx_rank, jnp.clip(my_len - meta_all[1] * BLK, 0, BLK), 0
    ).astype(jnp.int32)
    q_rows = query.transpose(1, 0, 2).reshape(heads_dev * span_size, HD)
    attn_heads = local_attention(
        limit, my_span.reshape(1).astype(jnp.int32), q_rows, cache_all, new_keys, new_vals
    )
    attn_rows = (
        attn_heads.reshape(heads_dev, span_size, HD).transpose(1, 0, 2).reshape(span_size, q_cols)
    )
    head_sum = lax.psum_scatter(
        column_term(attn_rows, w_out).astype(jnp.bfloat16), "tp", scatter_dimension=0, tiled=True
    ).astype(jnp.float32)
    mid = (resid.astype(jnp.float32) + head_sum.T).astype(jnp.bfloat16)
    full_mid = lax.all_gather(mid, "tp", axis=1, tiled=True)
    x_two = rms_norm(full_mid, mlp_gain)
    gate = jnp.dot(x_two, w_gate, preferred_element_type=jnp.float32)
    up_part = jnp.dot(x_two, w_up, preferred_element_type=jnp.float32)
    hidden = (jax.nn.silu(gate) * up_part).astype(jnp.bfloat16)
    down_sum = lax.psum_scatter(
        column_term(hidden, w_down).astype(jnp.bfloat16), "tp", scatter_dimension=0, tiled=True
    ).astype(jnp.float32)
    layer_out = (mid.astype(jnp.float32) + down_sum.T).astype(jnp.bfloat16)
    layer_out = jnp.where(live_rows[:, None], layer_out, jnp.zeros_like(layer_out))
    return (layer_out, new_kv)


def solution(mesh):
    return jax.shard_map(
        per_device,
        mesh=mesh,
        in_specs=(
            P("ctx", "tp"),
            P(),
            P(),
            P(None, "tp"),
            P(None, "tp"),
            P("tp", None),
            P(None, "tp"),
            P(None, "tp"),
            P("tp", None),
            P("ctx", None, None),
            P(),
            P(),
            P("ctx"),
            P("ctx"),
        ),
        out_specs=(P("ctx", "tp"), P("ctx", "tp")),
        check_vma=False,
    )
```

```python
import jax
import jax.numpy as jnp
from jax import lax
from jax.sharding import PartitionSpec as P
from jax.experimental import pallas as pl
from jax.experimental.pallas import tpu as pltpu

HQ = 32
KVH = 4
HD = 128
BLK = 128


THETA = 5000000.0
EPS = 1e-05
NEG = -1e30


def rms_norm(values, gain):
    wide = values.astype(jnp.float32)
    factor = lax.rsqrt(jnp.mean(wide * wide, axis=-1, keepdims=True) + EPS)
    return (wide * factor * gain.astype(jnp.float32)).astype(jnp.bfloat16)


def rotate(vectors, positions):
    width = vectors.shape[-1]
    half = width // 2
    freqs = THETA ** (-(jnp.arange(half, dtype=jnp.float32) * 2.0 / width))
    angles = positions.astype(jnp.float32)[:, None] * freqs[None, :]
    cosine = jnp.cos(angles)[:, None, :]
    sine = jnp.sin(angles)[:, None, :]
    first = vectors[..., :half]
    second = vectors[..., half:]
    return jnp.concatenate(
        [first * cosine - second * sine, second * cosine + first * sine], axis=-1
    )


def column_term(rows, weight):
    return lax.dot_general(
        weight, rows, (((0,), (1,)), ((), ())), preferred_element_type=jnp.float32
    )


def attn_kernel(
    idx_ref, cnt_ref, span_ref, q_ref, cache_ref, bias_ref, nk_ref, nv_ref, o_ref
):
    span_size = nk_ref.shape[0]
    chunk = BLK
    scale = HD ** (-0.5)
    dims = (((1,), (1,)), ((), ()))
    count = cnt_ref[0]
    span = span_ref[0]
    row = lax.broadcasted_iota(jnp.int32, (chunk, BLK), 0)
    col = lax.broadcasted_iota(jnp.int32, (chunk, BLK), 1)

    def raw(q, keys):
        return lax.dot_general(q, keys, dims, preferred_element_type=jnp.float32)

    def one_chunk(c, carry):
        start = pl.multiple_of(c * chunk, chunk)
        q = q_ref[pl.ds(start, chunk), :]
        first = lax.rem(start, span_size)

        def new_ok(jb):
            j = jb * BLK + col
            return (j <= first + row) & (j < span)

        def max_step(i, top):
            slot = idx_ref[i]
            return jnp.maximum(top, raw(q, cache_ref[slot, :, :HD]) + bias_ref[pl.ds(slot, 1), :])

        top = lax.fori_loop(0, count, max_step, jnp.full((chunk, BLK), NEG, jnp.float32))
        for jb in range(span_size // BLK):
            sc = raw(q, nk_ref[jb * BLK : (jb + 1) * BLK, :])
            top = jnp.maximum(top, jnp.where(new_ok(jb), sc, NEG))
        peak = jnp.max(top, axis=1, keepdims=True) * scale

        def sum_step(i, acc):
            slot = idx_ref[i]
            sc = raw(q, cache_ref[slot, :, :HD]) * scale + bias_ref[pl.ds(slot, 1), :]
            w = jnp.exp(sc - peak)
            pv = jnp.dot(w.astype(jnp.bfloat16), cache_ref[slot, :, HD:], preferred_element_type=jnp.float32)
            return (acc[0] + w, acc[1] + pv)

        zeros = jnp.zeros((chunk, BLK), jnp.float32)
        total, summed = lax.fori_loop(0, count, sum_step, (zeros, jnp.zeros((chunk, HD), jnp.float32)))
        for jb in range(span_size // BLK):
            sc = raw(q, nk_ref[jb * BLK : (jb + 1) * BLK, :]) * scale
            w = jnp.where(new_ok(jb), jnp.exp(sc - peak), 0.0)
            total = total + w
            summed = summed + jnp.dot(
                w.astype(jnp.bfloat16), nv_ref[jb * BLK : (jb + 1) * BLK, :], preferred_element_type=jnp.float32
            )
        o_ref[pl.ds(start, chunk), :] = (summed / jnp.sum(total, axis=1, keepdims=True)).astype(o_ref.dtype)
        return carry

    lax.fori_loop(0, q_ref.shape[0] // chunk, one_chunk, 0)


def local_attention(limit, span, q_rows, cache_all, new_keys, new_vals):
    rows = q_rows.shape[0]
    slots = limit.shape[0]
    live = limit > 0
    place = jnp.where(live, jnp.cumsum(live.astype(jnp.int32)) - 1, slots)
    order = jnp.zeros((slots,), jnp.int32).at[place].set(
        jnp.arange(slots, dtype=jnp.int32), mode="drop"
    )
    count = jnp.sum(live.astype(jnp.int32)).reshape(1)
    bias = jnp.where(
        jnp.arange(BLK, dtype=jnp.int32)[None, :] < limit[:, None], 0.0, NEG
    ).astype(jnp.float32)

    def whole(shape):
        return pl.BlockSpec(shape, lambda i, *_: (0,) * len(shape))

    return pl.pallas_call(
        attn_kernel,
        out_shape=jax.ShapeDtypeStruct((rows, HD), jnp.bfloat16),
        grid_spec=pltpu.PrefetchScalarGridSpec(
            num_scalar_prefetch=3,
            grid=(1,),
            in_specs=[
                whole(q_rows.shape),
                whole(cache_all.shape),
                whole(bias.shape),
                whole(new_keys.shape),
                whole(new_vals.shape),
            ],
            out_specs=whole((rows, HD)),
        ),
    )(order, count, span, q_rows, cache_all, bias, new_keys, new_vals)


def gather_ctx(value, count):
    parts = [value]
    for shift in range(1, count):
        pairs = [(i, (i + shift) % count) for i in range(count)]
        parts.append(lax.ppermute(value, "ctx", pairs))
    return parts


def per_device(
    resid,
    attn_gain,
    mlp_gain,
    w_query,
    w_kv,
    w_out,
    w_gate,
    w_up,
    w_down,
    kv_cache,
    cache_len,
    span_len,
    slot_req,
    slot_blk,
):
    span_size = resid.shape[0]
    ctx_count = lax.axis_size("ctx")
    q_cols = w_query.shape[1]
    heads_dev = q_cols // HD
    ctx_rank = lax.axis_index("ctx")
    tp_rank = lax.axis_index("tp")
    group = tp_rank * heads_dev // (HQ // KVH)
    my_len = cache_len[ctx_rank]
    my_span = span_len[ctx_rank]
    offsets = jnp.arange(span_size, dtype=jnp.int32)
    positions = my_len + offsets
    live_rows = offsets < my_span

    own_cache = jnp.concatenate(
        [
            lax.dynamic_slice_in_dim(kv_cache, group * HD, HD, 2),
            lax.dynamic_slice_in_dim(kv_cache, KVH * HD + group * HD, HD, 2),
        ],
        axis=2,
    )
    own_meta = jnp.stack([slot_req, slot_blk])
    cache_all = jnp.concatenate(gather_ctx(own_cache, ctx_count), axis=0)
    meta_all = jnp.concatenate(gather_ctx(own_meta, ctx_count), axis=1)

    full_resid = lax.all_gather(resid, "tp", axis=1, tiled=True)
    x_norm = rms_norm(full_resid, attn_gain)
    query = rotate(
        jnp.dot(x_norm, w_query, preferred_element_type=jnp.float32).reshape(
            span_size, heads_dev, HD
        ),
        positions,
    ).astype(jnp.bfloat16)
    kv_piece = jnp.dot(x_norm, w_kv, preferred_element_type=jnp.float32).astype(jnp.bfloat16)
    kv_width = kv_piece.shape[1]
    kv_all = lax.all_gather(kv_piece, "tp", axis=1, tiled=True)
    all_keys = rotate(
        kv_all[:, : KVH * HD].astype(jnp.float32).reshape(span_size, KVH, HD), positions
    ).astype(jnp.bfloat16)
    joined = jnp.concatenate([all_keys.reshape(span_size, KVH * HD), kv_all[:, KVH * HD :]], axis=1)
    mine = lax.dynamic_slice_in_dim(joined, tp_rank * kv_width, kv_width, 1)
    new_kv = jnp.where(live_rows[:, None], mine, jnp.zeros_like(mine))
    new_keys = lax.dynamic_index_in_dim(all_keys, group, 1, keepdims=False)
    new_vals = lax.dynamic_slice_in_dim(kv_all, KVH * HD + group * HD, HD, 1)

    limit = jnp.where(
        meta_all[0] == ctx_rank, jnp.clip(my_len - meta_all[1] * BLK, 0, BLK), 0
    ).astype(jnp.int32)
    q_rows = query.transpose(1, 0, 2).reshape(heads_dev * span_size, HD)
    attn_heads = local_attention(
        limit, my_span.reshape(1).astype(jnp.int32), q_rows, cache_all, new_keys, new_vals
    )
    attn_rows = (
        attn_heads.reshape(heads_dev, span_size, HD).transpose(1, 0, 2).reshape(span_size, q_cols)
    )
    head_sum = lax.psum_scatter(
        column_term(attn_rows, w_out).astype(jnp.bfloat16), "tp", scatter_dimension=0, tiled=True
    ).astype(jnp.float32)
    mid = (resid.astype(jnp.float32) + head_sum.T).astype(jnp.bfloat16)
    full_mid = lax.all_gather(mid, "tp", axis=1, tiled=True)
    x_two = rms_norm(full_mid, mlp_gain)
    gate = jnp.dot(x_two, w_gate, preferred_element_type=jnp.float32)
    up_part = jnp.dot(x_two, w_up, preferred_element_type=jnp.float32)
    hidden = (jax.nn.silu(gate) * up_part).astype(jnp.bfloat16)
    down_sum = lax.psum_scatter(
        column_term(hidden, w_down).astype(jnp.bfloat16), "tp", scatter_dimension=0, tiled=True
    ).astype(jnp.float32)
    layer_out = (mid.astype(jnp.float32) + down_sum.T).astype(jnp.bfloat16)
    layer_out = jnp.where(live_rows[:, None], layer_out, jnp.zeros_like(layer_out))
    return (layer_out, new_kv)


def solution(mesh):
    return jax.shard_map(
        per_device,
        mesh=mesh,
        in_specs=(
            P("ctx", "tp"),
            P(),
            P(),
            P(None, "tp"),
            P(None, "tp"),
            P("tp", None),
            P(None, "tp"),
            P(None, "tp"),
            P("tp", None),
            P("ctx", None, None),
            P(),
            P(),
            P("ctx"),
            P("ctx"),
        ),
        out_specs=(P("ctx", "tp"), P("ctx", "tp")),
        check_vma=False,
    )
```

```python
import jax
import jax.numpy as jnp
from jax import lax
from jax.sharding import PartitionSpec as P
from jax.experimental import pallas as pl
from jax.experimental.pallas import tpu as pltpu

HQ = 32
KVH = 4
HD = 128
BLK = 128


THETA = 5000000.0
EPS = 1e-05
NEG = -1e30


def rms_norm(values, gain):
    wide = values.astype(jnp.float32)
    factor = lax.rsqrt(jnp.mean(wide * wide, axis=-1, keepdims=True) + EPS)
    return (wide * factor * gain.astype(jnp.float32)).astype(jnp.bfloat16)


def rotate(vectors, positions):
    width = vectors.shape[-1]
    half = width // 2
    freqs = THETA ** (-(jnp.arange(half, dtype=jnp.float32) * 2.0 / width))
    angles = positions.astype(jnp.float32)[:, None] * freqs[None, :]
    cosine = jnp.cos(angles)[:, None, :]
    sine = jnp.sin(angles)[:, None, :]
    first = vectors[..., :half]
    second = vectors[..., half:]
    return jnp.concatenate(
        [first * cosine - second * sine, second * cosine + first * sine], axis=-1
    )


def column_term(rows, weight):
    return lax.dot_general(
        weight, rows, (((0,), (1,)), ((), ())), preferred_element_type=jnp.float32
    )


def attn_kernel(limit_ref, span_ref, q_ref, cache_ref, nk_ref, nv_ref, o_ref, m_scr, t_scr, acc_scr):
    slots = cache_ref.shape[0]
    span_size = nk_ref.shape[0]
    heads = q_ref.shape[0] // span_size
    scale = HD ** (-0.5)
    q_all = q_ref[...]
    col = lax.broadcasted_iota(jnp.int32, (1, BLK), 1)
    row_i = lax.broadcasted_iota(jnp.int32, (span_size, span_size), 0)
    col_j = lax.broadcasted_iota(jnp.int32, (span_size, span_size), 1)
    new_ok = (col_j <= row_i) & (col_j < span_ref[0])
    dims = (((1,), (1,)), ((), ()))

    def cache_scores(s):
        keys = cache_ref[s, :, :HD]
        return lax.dot_general(q_all, keys, dims, preferred_element_type=jnp.float32) * scale

    def new_scores(h):
        rows = q_ref[h * span_size : (h + 1) * span_size, :]
        return lax.dot_general(rows, nk_ref[...], dims, preferred_element_type=jnp.float32) * scale

    m_scr[...] = jnp.full(m_scr.shape, NEG, jnp.float32)

    def max_step(s, carry):
        lim = limit_ref[s]

        @pl.when(lim > 0)
        def _():
            sc = jnp.where(col < lim, cache_scores(s), NEG)
            m_scr[...] = jnp.maximum(m_scr[...], jnp.max(sc, axis=1, keepdims=True))

        return carry

    lax.fori_loop(0, slots, max_step, 0)
    for h in range(heads):
        part = slice(h * span_size, (h + 1) * span_size)
        sc = jnp.where(new_ok, new_scores(h), NEG)
        m_scr[part, :] = jnp.maximum(m_scr[part, :], jnp.max(sc, axis=1, keepdims=True))

    t_scr[...] = jnp.zeros(t_scr.shape, jnp.float32)
    acc_scr[...] = jnp.zeros(acc_scr.shape, jnp.float32)

    def sum_step(s, carry):
        lim = limit_ref[s]

        @pl.when(lim > 0)
        def _():
            w = jnp.where(col < lim, jnp.exp(cache_scores(s) - m_scr[...]), 0.0)
            t_scr[...] += jnp.sum(w, axis=1, keepdims=True)
            acc_scr[...] += jnp.dot(
                w.astype(jnp.bfloat16), cache_ref[s, :, HD:], preferred_element_type=jnp.float32
            )

        return carry

    lax.fori_loop(0, slots, sum_step, 0)
    for h in range(heads):
        part = slice(h * span_size, (h + 1) * span_size)
        w = jnp.where(new_ok, jnp.exp(new_scores(h) - m_scr[part, :]), 0.0)
        t_scr[part, :] += jnp.sum(w, axis=1, keepdims=True)
        acc_scr[part, :] += jnp.dot(
            w.astype(jnp.bfloat16), nv_ref[...], preferred_element_type=jnp.float32
        )
    o_ref[...] = (acc_scr[...] / t_scr[...]).astype(o_ref.dtype)


def local_attention(limit, span, q_rows, cache_all, new_keys, new_vals):
    rows = q_rows.shape[0]

    def whole(shape):
        return pl.BlockSpec(shape, lambda i, *_: (0,) * len(shape))

    return pl.pallas_call(
        attn_kernel,
        out_shape=jax.ShapeDtypeStruct((rows, HD), jnp.bfloat16),
        grid_spec=pltpu.PrefetchScalarGridSpec(
            num_scalar_prefetch=2,
            grid=(1,),
            in_specs=[
                whole(q_rows.shape),
                whole(cache_all.shape),
                whole(new_keys.shape),
                whole(new_vals.shape),
            ],
            out_specs=whole((rows, HD)),
            scratch_shapes=[
                pltpu.VMEM((rows, 1), jnp.float32),
                pltpu.VMEM((rows, 1), jnp.float32),
                pltpu.VMEM((rows, HD), jnp.float32),
            ],
        ),
    )(limit, span, q_rows, cache_all, new_keys, new_vals)


def kv_routes(tp_count, kv_width):
    per_head = HD // kv_width
    heads_dev = HQ // tp_count
    needs = []
    for dev in range(tp_count):
        group = dev * heads_dev // (HQ // KVH)
        keys = [group * per_head + u for u in range(per_head)]
        vals = [KVH * per_head + group * per_head + u for u in range(per_head)]
        own_head = dev * kv_width // HD
        own = [own_head * per_head + u for u in range(per_head)] if own_head < KVH else [dev] * per_head
        needs.append(keys + vals + own)
    rounds = []
    for entry in range(len(needs[0])):
        sets = []
        for dev in range(tp_count):
            src = needs[dev][entry]
            if src == dev:
                continue
            for pairs in sets:
                if all(a != src for a, _ in pairs):
                    pairs.append((src, dev))
                    break
            else:
                sets.append([(src, dev)])
        rounds.append(sets)
    selfs = [[needs[dev][entry] == dev for dev in range(tp_count)] for entry in range(len(needs[0]))]
    return per_head, rounds, selfs


def gather_ctx(value, count):
    parts = [value]
    for shift in range(1, count):
        pairs = [(i, (i + shift) % count) for i in range(count)]
        parts.append(lax.ppermute(value, "ctx", pairs))
    return parts


def per_device(
    resid,
    attn_gain,
    mlp_gain,
    w_query,
    w_kv,
    w_out,
    w_gate,
    w_up,
    w_down,
    kv_cache,
    cache_len,
    span_len,
    slot_req,
    slot_blk,
):
    span_size = resid.shape[0]
    ctx_count = lax.axis_size("ctx")
    q_cols = w_query.shape[1]
    heads_dev = q_cols // HD
    ctx_rank = lax.axis_index("ctx")
    tp_rank = lax.axis_index("tp")
    group = tp_rank * heads_dev // (HQ // KVH)
    my_len = cache_len[ctx_rank]
    my_span = span_len[ctx_rank]
    offsets = jnp.arange(span_size, dtype=jnp.int32)
    positions = my_len + offsets
    live_rows = offsets < my_span

    own_cache = jnp.concatenate(
        [
            lax.dynamic_slice_in_dim(kv_cache, group * HD, HD, 2),
            lax.dynamic_slice_in_dim(kv_cache, KVH * HD + group * HD, HD, 2),
        ],
        axis=2,
    )
    own_meta = jnp.stack([slot_req, slot_blk])
    cache_all = jnp.concatenate(gather_ctx(own_cache, ctx_count), axis=0)
    meta_all = jnp.concatenate(gather_ctx(own_meta, ctx_count), axis=1)

    full_resid = lax.all_gather(resid, "tp", axis=1, tiled=True)
    x_norm = rms_norm(full_resid, attn_gain)
    kv_piece = jnp.dot(x_norm, w_kv, preferred_element_type=jnp.float32).astype(jnp.bfloat16)
    kv_width = kv_piece.shape[1]
    tp_count = lax.axis_size("tp")
    per_head, rounds, selfs = kv_routes(tp_count, kv_width)
    blocks = []
    for entry, sets in enumerate(rounds):
        is_self = jnp.asarray(selfs[entry])[tp_rank]
        got = jnp.where(is_self, kv_piece, jnp.zeros_like(kv_piece))
        for pairs in sets:
            got = got + lax.ppermute(kv_piece, "tp", pairs)
        blocks.append(got)

    def head_of(parts):
        return jnp.concatenate(parts, axis=1) if len(parts) > 1 else parts[0]

    def rotated(raw):
        return (
            rotate(raw.astype(jnp.float32).reshape(span_size, 1, HD), positions)
            .astype(jnp.bfloat16)
            .reshape(span_size, HD)
        )

    new_keys = rotated(head_of(blocks[:per_head]))
    new_vals = head_of(blocks[per_head : 2 * per_head])
    own_rot = lax.dynamic_slice_in_dim(
        rotated(head_of(blocks[2 * per_head :])), (tp_rank * kv_width) % HD, kv_width, 1
    )
    mine = jnp.where(tp_rank * kv_width < KVH * HD, own_rot, kv_piece)
    new_kv = jnp.where(live_rows[:, None], mine, jnp.zeros_like(mine))
    query = rotate(
        jnp.dot(x_norm, w_query, preferred_element_type=jnp.float32).reshape(
            span_size, heads_dev, HD
        ),
        positions,
    ).astype(jnp.bfloat16)

    limit = jnp.where(
        meta_all[0] == ctx_rank, jnp.clip(my_len - meta_all[1] * BLK, 0, BLK), 0
    ).astype(jnp.int32)
    q_rows = query.transpose(1, 0, 2).reshape(heads_dev * span_size, HD)
    attn_heads = local_attention(
        limit, my_span.reshape(1).astype(jnp.int32), q_rows, cache_all, new_keys, new_vals
    )
    attn_rows = (
        attn_heads.reshape(heads_dev, span_size, HD).transpose(1, 0, 2).reshape(span_size, q_cols)
    )
    head_sum = lax.psum_scatter(
        column_term(attn_rows, w_out).astype(jnp.bfloat16), "tp", scatter_dimension=0, tiled=True
    ).astype(jnp.float32)
    mid = (resid.astype(jnp.float32) + head_sum.T).astype(jnp.bfloat16)
    full_mid = lax.all_gather(mid, "tp", axis=1, tiled=True)
    x_two = rms_norm(full_mid, mlp_gain)
    gate = jnp.dot(x_two, w_gate, preferred_element_type=jnp.float32)
    up_part = jnp.dot(x_two, w_up, preferred_element_type=jnp.float32)
    hidden = (jax.nn.silu(gate) * up_part).astype(jnp.bfloat16)
    down_sum = lax.psum_scatter(
        column_term(hidden, w_down).astype(jnp.bfloat16), "tp", scatter_dimension=0, tiled=True
    ).astype(jnp.float32)
    layer_out = (mid.astype(jnp.float32) + down_sum.T).astype(jnp.bfloat16)
    layer_out = jnp.where(live_rows[:, None], layer_out, jnp.zeros_like(layer_out))
    return (layer_out, new_kv)


def solution(mesh):
    return jax.shard_map(
        per_device,
        mesh=mesh,
        in_specs=(
            P("ctx", "tp"),
            P(),
            P(),
            P(None, "tp"),
            P(None, "tp"),
            P("tp", None),
            P(None, "tp"),
            P(None, "tp"),
            P("tp", None),
            P("ctx", None, None),
            P(),
            P(),
            P("ctx"),
            P("ctx"),
        ),
        out_specs=(P("ctx", "tp"), P("ctx", "tp")),
        check_vma=False,
    )
```

```python
import jax
import jax.numpy as jnp
from jax import lax
from jax.sharding import PartitionSpec as P
from jax.experimental import pallas as pl
from jax.experimental.pallas import tpu as pltpu

HQ = 32
KVH = 4
HD = 128
BLK = 128


THETA = 5000000.0
EPS = 1e-05
NEG = -1e30


def rms_norm(values, gain):
    wide = values.astype(jnp.float32)
    factor = lax.rsqrt(jnp.mean(wide * wide, axis=-1, keepdims=True) + EPS)
    return (wide * factor * gain.astype(jnp.float32)).astype(jnp.bfloat16)


def rotate(vectors, positions):
    width = vectors.shape[-1]
    half = width // 2
    freqs = THETA ** (-(jnp.arange(half, dtype=jnp.float32) * 2.0 / width))
    angles = positions.astype(jnp.float32)[:, None] * freqs[None, :]
    cosine = jnp.cos(angles)[:, None, :]
    sine = jnp.sin(angles)[:, None, :]
    first = vectors[..., :half]
    second = vectors[..., half:]
    return jnp.concatenate(
        [first * cosine - second * sine, second * cosine + first * sine], axis=-1
    )


def column_term(rows, weight):
    return lax.dot_general(
        weight, rows, (((0,), (1,)), ((), ())), preferred_element_type=jnp.float32
    )


def attn_kernel(limit_ref, span_ref, q_ref, cache_ref, bias_ref, nk_ref, nv_ref, o_ref, top_scr, tot_scr, acc_scr):
    slots = cache_ref.shape[0]
    span_size = nk_ref.shape[0]
    heads = q_ref.shape[0] // span_size
    scale = HD ** (-0.5)
    q_all = q_ref[...]
    row_i = lax.broadcasted_iota(jnp.int32, (span_size, span_size), 0)
    col_j = lax.broadcasted_iota(jnp.int32, (span_size, span_size), 1)
    new_ok = (col_j <= row_i) & (col_j < span_ref[0])
    dims = (((1,), (1,)), ((), ()))

    def cache_raw(s):
        return lax.dot_general(q_all, cache_ref[s, :, :HD], dims, preferred_element_type=jnp.float32)

    def new_raw(h):
        rows = q_ref[h * span_size : (h + 1) * span_size, :]
        return lax.dot_general(rows, nk_ref[...], dims, preferred_element_type=jnp.float32)

    top_scr[...] = jnp.full(top_scr.shape, NEG, jnp.float32)

    def max_step(s, carry):
        @pl.when(limit_ref[s] > 0)
        def _():
            top_scr[...] = jnp.maximum(top_scr[...], cache_raw(s) + bias_ref[pl.ds(s, 1), :])

        return carry

    lax.fori_loop(0, slots, max_step, 0)
    peaks = []
    for h in range(heads):
        part = slice(h * span_size, (h + 1) * span_size)
        raw_top = jnp.maximum(
            jnp.max(top_scr[part, :], axis=1, keepdims=True),
            jnp.max(jnp.where(new_ok, new_raw(h), NEG), axis=1, keepdims=True),
        )
        peaks.append(raw_top * scale)
    peak = jnp.concatenate(peaks, axis=0)

    tot_scr[...] = jnp.zeros(tot_scr.shape, jnp.float32)
    acc_scr[...] = jnp.zeros(acc_scr.shape, jnp.float32)

    def sum_step(s, carry):
        @pl.when(limit_ref[s] > 0)
        def _():
            w = jnp.exp(cache_raw(s) * scale + bias_ref[pl.ds(s, 1), :] - peak)
            tot_scr[...] += w
            acc_scr[...] += jnp.dot(
                w.astype(jnp.bfloat16), cache_ref[s, :, HD:], preferred_element_type=jnp.float32
            )

        return carry

    lax.fori_loop(0, slots, sum_step, 0)
    for h in range(heads):
        part = slice(h * span_size, (h + 1) * span_size)
        w = jnp.where(new_ok, jnp.exp(new_raw(h) * scale - peak[part, :]), 0.0)
        total = jnp.sum(tot_scr[part, :], axis=1, keepdims=True) + jnp.sum(w, axis=1, keepdims=True)
        summed = acc_scr[part, :] + jnp.dot(
            w.astype(jnp.bfloat16), nv_ref[...], preferred_element_type=jnp.float32
        )
        o_ref[part, :] = (summed / total).astype(o_ref.dtype)


def local_attention(limit, span, q_rows, cache_all, new_keys, new_vals):
    rows = q_rows.shape[0]
    bias = jnp.where(
        jnp.arange(BLK, dtype=jnp.int32)[None, :] < limit[:, None], 0.0, NEG
    ).astype(jnp.float32)

    def whole(shape):
        return pl.BlockSpec(shape, lambda i, *_: (0,) * len(shape))

    return pl.pallas_call(
        attn_kernel,
        out_shape=jax.ShapeDtypeStruct((rows, HD), jnp.bfloat16),
        grid_spec=pltpu.PrefetchScalarGridSpec(
            num_scalar_prefetch=2,
            grid=(1,),
            in_specs=[
                whole(q_rows.shape),
                whole(cache_all.shape),
                whole(bias.shape),
                whole(new_keys.shape),
                whole(new_vals.shape),
            ],
            out_specs=whole((rows, HD)),
            scratch_shapes=[
                pltpu.VMEM((rows, BLK), jnp.float32),
                pltpu.VMEM((rows, BLK), jnp.float32),
                pltpu.VMEM((rows, HD), jnp.float32),
            ],
        ),
    )(limit, span, q_rows, cache_all, bias, new_keys, new_vals)


def kv_routes(tp_count, kv_width):
    per_head = HD // kv_width
    heads_dev = HQ // tp_count
    needs = []
    for dev in range(tp_count):
        group = dev * heads_dev // (HQ // KVH)
        keys = [group * per_head + u for u in range(per_head)]
        vals = [KVH * per_head + group * per_head + u for u in range(per_head)]
        own_head = dev * kv_width // HD
        own = [own_head * per_head + u for u in range(per_head)] if own_head < KVH else [dev] * per_head
        needs.append(keys + vals + own)
    rounds = []
    for entry in range(len(needs[0])):
        sets = []
        for dev in range(tp_count):
            src = needs[dev][entry]
            if src == dev:
                continue
            for pairs in sets:
                if all(a != src for a, _ in pairs):
                    pairs.append((src, dev))
                    break
            else:
                sets.append([(src, dev)])
        rounds.append(sets)
    selfs = [[needs[dev][entry] == dev for dev in range(tp_count)] for entry in range(len(needs[0]))]
    return per_head, rounds, selfs


def gather_ctx(value, count):
    parts = [value]
    for shift in range(1, count):
        pairs = [(i, (i + shift) % count) for i in range(count)]
        parts.append(lax.ppermute(value, "ctx", pairs))
    return parts


def per_device(
    resid,
    attn_gain,
    mlp_gain,
    w_query,
    w_kv,
    w_out,
    w_gate,
    w_up,
    w_down,
    kv_cache,
    cache_len,
    span_len,
    slot_req,
    slot_blk,
):
    span_size = resid.shape[0]
    ctx_count = lax.axis_size("ctx")
    q_cols = w_query.shape[1]
    heads_dev = q_cols // HD
    ctx_rank = lax.axis_index("ctx")
    tp_rank = lax.axis_index("tp")
    group = tp_rank * heads_dev // (HQ // KVH)
    my_len = cache_len[ctx_rank]
    my_span = span_len[ctx_rank]
    offsets = jnp.arange(span_size, dtype=jnp.int32)
    positions = my_len + offsets
    live_rows = offsets < my_span

    own_cache = jnp.concatenate(
        [
            lax.dynamic_slice_in_dim(kv_cache, group * HD, HD, 2),
            lax.dynamic_slice_in_dim(kv_cache, KVH * HD + group * HD, HD, 2),
        ],
        axis=2,
    )
    own_meta = jnp.stack([slot_req, slot_blk])
    cache_all = jnp.concatenate(gather_ctx(own_cache, ctx_count), axis=0)
    meta_all = jnp.concatenate(gather_ctx(own_meta, ctx_count), axis=1)

    full_resid = lax.all_gather(resid, "tp", axis=1, tiled=True)
    x_norm = rms_norm(full_resid, attn_gain)
    kv_piece = jnp.dot(x_norm, w_kv, preferred_element_type=jnp.float32).astype(jnp.bfloat16)
    kv_width = kv_piece.shape[1]
    tp_count = lax.axis_size("tp")
    per_head, rounds, selfs = kv_routes(tp_count, kv_width)
    blocks = []
    for entry, sets in enumerate(rounds):
        is_self = jnp.asarray(selfs[entry])[tp_rank]
        got = jnp.where(is_self, kv_piece, jnp.zeros_like(kv_piece))
        for pairs in sets:
            got = got + lax.ppermute(kv_piece, "tp", pairs)
        blocks.append(got)

    def head_of(parts):
        return jnp.concatenate(parts, axis=1) if len(parts) > 1 else parts[0]

    def rotated(raw):
        return (
            rotate(raw.astype(jnp.float32).reshape(span_size, 1, HD), positions)
            .astype(jnp.bfloat16)
            .reshape(span_size, HD)
        )

    new_keys = rotated(head_of(blocks[:per_head]))
    new_vals = head_of(blocks[per_head : 2 * per_head])
    own_rot = lax.dynamic_slice_in_dim(
        rotated(head_of(blocks[2 * per_head :])), (tp_rank * kv_width) % HD, kv_width, 1
    )
    mine = jnp.where(tp_rank * kv_width < KVH * HD, own_rot, kv_piece)
    new_kv = jnp.where(live_rows[:, None], mine, jnp.zeros_like(mine))
    query = rotate(
        jnp.dot(x_norm, w_query, preferred_element_type=jnp.float32).reshape(
            span_size, heads_dev, HD
        ),
        positions,
    ).astype(jnp.bfloat16)

    limit = jnp.where(
        meta_all[0] == ctx_rank, jnp.clip(my_len - meta_all[1] * BLK, 0, BLK), 0
    ).astype(jnp.int32)
    q_rows = query.transpose(1, 0, 2).reshape(heads_dev * span_size, HD)
    attn_heads = local_attention(
        limit, my_span.reshape(1).astype(jnp.int32), q_rows, cache_all, new_keys, new_vals
    )
    attn_rows = (
        attn_heads.reshape(heads_dev, span_size, HD).transpose(1, 0, 2).reshape(span_size, q_cols)
    )
    head_sum = lax.psum_scatter(
        column_term(attn_rows, w_out).astype(jnp.bfloat16), "tp", scatter_dimension=0, tiled=True
    ).astype(jnp.float32)
    mid = (resid.astype(jnp.float32) + head_sum.T).astype(jnp.bfloat16)
    full_mid = lax.all_gather(mid, "tp", axis=1, tiled=True)
    x_two = rms_norm(full_mid, mlp_gain)
    gate = jnp.dot(x_two, w_gate, preferred_element_type=jnp.float32)
    up_part = jnp.dot(x_two, w_up, preferred_element_type=jnp.float32)
    hidden = (jax.nn.silu(gate) * up_part).astype(jnp.bfloat16)
    down_sum = lax.psum_scatter(
        column_term(hidden, w_down).astype(jnp.bfloat16), "tp", scatter_dimension=0, tiled=True
    ).astype(jnp.float32)
    layer_out = (mid.astype(jnp.float32) + down_sum.T).astype(jnp.bfloat16)
    layer_out = jnp.where(live_rows[:, None], layer_out, jnp.zeros_like(layer_out))
    return (layer_out, new_kv)


def solution(mesh):
    return jax.shard_map(
        per_device,
        mesh=mesh,
        in_specs=(
            P("ctx", "tp"),
            P(),
            P(),
            P(None, "tp"),
            P(None, "tp"),
            P("tp", None),
            P(None, "tp"),
            P(None, "tp"),
            P("tp", None),
            P("ctx", None, None),
            P(),
            P(),
            P("ctx"),
            P("ctx"),
        ),
        out_specs=(P("ctx", "tp"), P("ctx", "tp")),
        check_vma=False,
    )
```

```python
import functools

import jax
import jax.numpy as jnp
from jax import lax
from jax.sharding import PartitionSpec as P
from jax.experimental import pallas as pl
from jax.experimental.pallas import tpu as pltpu

HQ = 32
KVH = 4
HD = 128
BLK = 128


THETA = 5000000.0
EPS = 1e-05
NEG = -1e30


def rms_norm(values, gain):
    wide = values.astype(jnp.float32)
    factor = lax.rsqrt(jnp.mean(wide * wide, axis=-1, keepdims=True) + EPS)
    return (wide * factor * gain.astype(jnp.float32)).astype(jnp.bfloat16)


def rotate(vectors, positions):
    width = vectors.shape[-1]
    half = width // 2
    freqs = THETA ** (-(jnp.arange(half, dtype=jnp.float32) * 2.0 / width))
    angles = positions.astype(jnp.float32)[:, None] * freqs[None, :]
    cosine = jnp.cos(angles)[:, None, :]
    sine = jnp.sin(angles)[:, None, :]
    first = vectors[..., :half]
    second = vectors[..., half:]
    return jnp.concatenate(
        [first * cosine - second * sine, second * cosine + first * sine], axis=-1
    )


def column_term(rows, weight):
    return lax.dot_general(
        weight, rows, (((0,), (1,)), ((), ())), preferred_element_type=jnp.float32
    )


def attn_kernel(limit_ref, span_ref, q_ref, cache_ref, bias_ref, nk_ref, nv_ref, o_ref, top_scr, tot_scr, acc_scr):
    slots = cache_ref.shape[0]
    span_size = nk_ref.shape[0]
    heads = q_ref.shape[0] // span_size
    scale = HD ** (-0.5)
    q_all = q_ref[...]
    row_i = lax.broadcasted_iota(jnp.int32, (span_size, span_size), 0)
    col_j = lax.broadcasted_iota(jnp.int32, (span_size, span_size), 1)
    new_ok = (col_j <= row_i) & (col_j < span_ref[0])
    dims = (((1,), (1,)), ((), ()))

    def cache_raw(s):
        return lax.dot_general(q_all, cache_ref[s, :, :HD], dims, preferred_element_type=jnp.float32)

    def new_raw(h):
        rows = q_ref[h * span_size : (h + 1) * span_size, :]
        return lax.dot_general(rows, nk_ref[...], dims, preferred_element_type=jnp.float32)

    top_scr[...] = jnp.full(top_scr.shape, NEG, jnp.float32)

    def max_step(s, carry):
        @pl.when(limit_ref[s] > 0)
        def _():
            top_scr[...] = jnp.maximum(top_scr[...], cache_raw(s) + bias_ref[pl.ds(s, 1), :])

        return carry

    lax.fori_loop(0, slots, max_step, 0)
    peaks = []
    for h in range(heads):
        part = slice(h * span_size, (h + 1) * span_size)
        raw_top = jnp.maximum(
            jnp.max(top_scr[part, :], axis=1, keepdims=True),
            jnp.max(jnp.where(new_ok, new_raw(h), NEG), axis=1, keepdims=True),
        )
        peaks.append(raw_top * scale)
    peak = jnp.concatenate(peaks, axis=0)

    tot_scr[...] = jnp.zeros(tot_scr.shape, jnp.float32)
    acc_scr[...] = jnp.zeros(acc_scr.shape, jnp.float32)

    def sum_step(s, carry):
        @pl.when(limit_ref[s] > 0)
        def _():
            w = jnp.exp(cache_raw(s) * scale + bias_ref[pl.ds(s, 1), :] - peak)
            tot_scr[...] += w
            acc_scr[...] += jnp.dot(
                w.astype(jnp.bfloat16), cache_ref[s, :, HD:], preferred_element_type=jnp.float32
            )

        return carry

    lax.fori_loop(0, slots, sum_step, 0)
    for h in range(heads):
        part = slice(h * span_size, (h + 1) * span_size)
        w = jnp.where(new_ok, jnp.exp(new_raw(h) * scale - peak[part, :]), 0.0)
        total = jnp.sum(tot_scr[part, :], axis=1, keepdims=True) + jnp.sum(w, axis=1, keepdims=True)
        summed = acc_scr[part, :] + jnp.dot(
            w.astype(jnp.bfloat16), nv_ref[...], preferred_element_type=jnp.float32
        )
        o_ref[part, :] = (summed / total).astype(o_ref.dtype)


def local_attention(limit, span, q_rows, cache_all, new_keys, new_vals):
    rows = q_rows.shape[0]
    bias = jnp.where(
        jnp.arange(BLK, dtype=jnp.int32)[None, :] < limit[:, None], 0.0, NEG
    ).astype(jnp.float32)

    def whole(shape):
        return pl.BlockSpec(shape, lambda i, *_: (0,) * len(shape))

    return pl.pallas_call(
        attn_kernel,
        out_shape=jax.ShapeDtypeStruct((rows, HD), jnp.bfloat16),
        grid_spec=pltpu.PrefetchScalarGridSpec(
            num_scalar_prefetch=2,
            grid=(1,),
            in_specs=[
                whole(q_rows.shape),
                whole(cache_all.shape),
                whole(bias.shape),
                whole(new_keys.shape),
                whole(new_vals.shape),
            ],
            out_specs=whole((rows, HD)),
            scratch_shapes=[
                pltpu.VMEM((rows, BLK), jnp.float32),
                pltpu.VMEM((rows, BLK), jnp.float32),
                pltpu.VMEM((rows, HD), jnp.float32),
            ],
        ),
    )(limit, span, q_rows, cache_all, bias, new_keys, new_vals)


def ffn_kernel(first, x_ref, wg_ref, wu_ref, wd_ref, o_ref, g_acc, u_acc, h_scr):
    step = pl.program_id(0)

    @pl.when(step == 0)
    def _():
        g_acc[...] = jnp.zeros(g_acc.shape, jnp.float32)
        u_acc[...] = jnp.zeros(u_acc.shape, jnp.float32)

    @pl.when(step < first)
    def _():
        x = x_ref[...]
        dims = (((1,), (1,)), ((), ()))
        g_acc[...] += lax.dot_general(x, wg_ref[...], dims, preferred_element_type=jnp.float32)
        u_acc[...] += lax.dot_general(x, wu_ref[...], dims, preferred_element_type=jnp.float32)

    @pl.when(step == first - 1)
    def _():
        g = g_acc[...]
        h_scr[...] = (g / (1.0 + jnp.exp(-g)) * u_acc[...]).astype(h_scr.dtype)

    @pl.when(step >= first)
    def _():
        o_ref[...] = jnp.dot(h_scr[...], wd_ref[...], preferred_element_type=jnp.float32).astype(
            o_ref.dtype
        )


def feed_forward(x_two, w_gate, w_up, w_down):
    rows, width = x_two.shape
    units = w_gate.shape[1]
    chunk = 1024 if width % 1024 == 0 else width
    first = width // chunk
    outs = w_down.shape[1] // chunk
    last = first - 1
    return pl.pallas_call(
        functools.partial(ffn_kernel, first),
        out_shape=jax.ShapeDtypeStruct((rows, w_down.shape[1]), jnp.bfloat16),
        grid=(first + outs,),
        in_specs=[
            pl.BlockSpec((rows, chunk), lambda i: (0, jnp.minimum(i, last))),
            pl.BlockSpec((units, chunk), lambda i: (0, jnp.minimum(i, last))),
            pl.BlockSpec((units, chunk), lambda i: (0, jnp.minimum(i, last))),
            pl.BlockSpec((units, chunk), lambda i: (0, jnp.maximum(i - first, 0))),
        ],
        out_specs=pl.BlockSpec((rows, chunk), lambda i: (0, jnp.maximum(i - first, 0))),
        scratch_shapes=[
            pltpu.VMEM((rows, units), jnp.float32),
            pltpu.VMEM((rows, units), jnp.float32),
            pltpu.VMEM((rows, units), jnp.bfloat16),
        ],
        compiler_params=pltpu.CompilerParams(dimension_semantics=("arbitrary",)),
    )(x_two, w_gate.T, w_up.T, w_down)


def kv_routes(tp_count, kv_width):
    per_head = HD // kv_width
    heads_dev = HQ // tp_count
    needs = []
    for dev in range(tp_count):
        group = dev * heads_dev // (HQ // KVH)
        keys = [group * per_head + u for u in range(per_head)]
        vals = [KVH * per_head + group * per_head + u for u in range(per_head)]
        own_head = dev * kv_width // HD
        own = [own_head * per_head + u for u in range(per_head)] if own_head < KVH else [dev] * per_head
        needs.append(keys + vals + own)
    rounds = []
    for entry in range(len(needs[0])):
        sets = []
        for dev in range(tp_count):
            src = needs[dev][entry]
            if src == dev:
                continue
            for pairs in sets:
                if all(a != src for a, _ in pairs):
                    pairs.append((src, dev))
                    break
            else:
                sets.append([(src, dev)])
        rounds.append(sets)
    selfs = [[needs[dev][entry] == dev for dev in range(tp_count)] for entry in range(len(needs[0]))]
    return per_head, rounds, selfs


def gather_ctx(value, count):
    parts = [value]
    for shift in range(1, count):
        pairs = [(i, (i + shift) % count) for i in range(count)]
        parts.append(lax.ppermute(value, "ctx", pairs))
    return parts


def per_device(
    resid,
    attn_gain,
    mlp_gain,
    w_query,
    w_kv,
    w_out,
    w_gate,
    w_up,
    w_down,
    kv_cache,
    cache_len,
    span_len,
    slot_req,
    slot_blk,
):
    span_size = resid.shape[0]
    ctx_count = lax.axis_size("ctx")
    q_cols = w_query.shape[1]
    heads_dev = q_cols // HD
    ctx_rank = lax.axis_index("ctx")
    tp_rank = lax.axis_index("tp")
    group = tp_rank * heads_dev // (HQ // KVH)
    my_len = cache_len[ctx_rank]
    my_span = span_len[ctx_rank]
    offsets = jnp.arange(span_size, dtype=jnp.int32)
    positions = my_len + offsets
    live_rows = offsets < my_span

    own_cache = jnp.concatenate(
        [
            lax.dynamic_slice_in_dim(kv_cache, group * HD, HD, 2),
            lax.dynamic_slice_in_dim(kv_cache, KVH * HD + group * HD, HD, 2),
        ],
        axis=2,
    )
    own_meta = jnp.stack([slot_req, slot_blk])
    cache_all = jnp.concatenate(gather_ctx(own_cache, ctx_count), axis=0)
    meta_all = jnp.concatenate(gather_ctx(own_meta, ctx_count), axis=1)

    full_resid = lax.all_gather(resid, "tp", axis=1, tiled=True)
    x_norm = rms_norm(full_resid, attn_gain)
    kv_piece = jnp.dot(x_norm, w_kv, preferred_element_type=jnp.float32).astype(jnp.bfloat16)
    kv_width = kv_piece.shape[1]
    tp_count = lax.axis_size("tp")
    per_head, rounds, selfs = kv_routes(tp_count, kv_width)
    blocks = []
    for entry, sets in enumerate(rounds):
        is_self = jnp.asarray(selfs[entry])[tp_rank]
        got = jnp.where(is_self, kv_piece, jnp.zeros_like(kv_piece))
        for pairs in sets:
            got = got + lax.ppermute(kv_piece, "tp", pairs)
        blocks.append(got)

    def head_of(parts):
        return jnp.concatenate(parts, axis=1) if len(parts) > 1 else parts[0]

    def rotated(raw):
        return (
            rotate(raw.astype(jnp.float32).reshape(span_size, 1, HD), positions)
            .astype(jnp.bfloat16)
            .reshape(span_size, HD)
        )

    new_keys = rotated(head_of(blocks[:per_head]))
    new_vals = head_of(blocks[per_head : 2 * per_head])
    own_rot = lax.dynamic_slice_in_dim(
        rotated(head_of(blocks[2 * per_head :])), (tp_rank * kv_width) % HD, kv_width, 1
    )
    mine = jnp.where(tp_rank * kv_width < KVH * HD, own_rot, kv_piece)
    new_kv = jnp.where(live_rows[:, None], mine, jnp.zeros_like(mine))
    query = rotate(
        jnp.dot(x_norm, w_query, preferred_element_type=jnp.float32).reshape(
            span_size, heads_dev, HD
        ),
        positions,
    ).astype(jnp.bfloat16)

    limit = jnp.where(
        meta_all[0] == ctx_rank, jnp.clip(my_len - meta_all[1] * BLK, 0, BLK), 0
    ).astype(jnp.int32)
    q_rows = query.transpose(1, 0, 2).reshape(heads_dev * span_size, HD)
    attn_heads = local_attention(
        limit, my_span.reshape(1).astype(jnp.int32), q_rows, cache_all, new_keys, new_vals
    )
    attn_rows = (
        attn_heads.reshape(heads_dev, span_size, HD).transpose(1, 0, 2).reshape(span_size, q_cols)
    )
    head_sum = lax.psum_scatter(
        column_term(attn_rows, w_out).astype(jnp.bfloat16), "tp", scatter_dimension=0, tiled=True
    ).astype(jnp.float32)
    mid = (resid.astype(jnp.float32) + head_sum.T).astype(jnp.bfloat16)
    full_mid = lax.all_gather(mid, "tp", axis=1, tiled=True)
    x_two = rms_norm(full_mid, mlp_gain)
    down_sum = lax.psum_scatter(
        feed_forward(x_two, w_gate, w_up, w_down), "tp", scatter_dimension=1, tiled=True
    ).astype(jnp.float32)
    layer_out = (mid.astype(jnp.float32) + down_sum).astype(jnp.bfloat16)
    layer_out = jnp.where(live_rows[:, None], layer_out, jnp.zeros_like(layer_out))
    return (layer_out, new_kv)


def solution(mesh):
    return jax.shard_map(
        per_device,
        mesh=mesh,
        in_specs=(
            P("ctx", "tp"),
            P(),
            P(),
            P(None, "tp"),
            P(None, "tp"),
            P("tp", None),
            P(None, "tp"),
            P(None, "tp"),
            P("tp", None),
            P("ctx", None, None),
            P(),
            P(),
            P("ctx"),
            P("ctx"),
        ),
        out_specs=(P("ctx", "tp"), P("ctx", "tp")),
        check_vma=False,
    )
```

```python
import functools

import jax
import jax.numpy as jnp
from jax import lax
from jax.sharding import PartitionSpec as P
from jax.experimental import pallas as pl
from jax.experimental.pallas import tpu as pltpu

HQ = 32
KVH = 4
HD = 128
BLK = 128


THETA = 5000000.0
EPS = 1e-05
NEG = -1e30


def rms_norm(values, gain):
    wide = values.astype(jnp.float32)
    factor = lax.rsqrt(jnp.mean(wide * wide, axis=-1, keepdims=True) + EPS)
    return (wide * factor * gain.astype(jnp.float32)).astype(jnp.bfloat16)


def rotate(vectors, positions):
    width = vectors.shape[-1]
    half = width // 2
    freqs = THETA ** (-(jnp.arange(half, dtype=jnp.float32) * 2.0 / width))
    angles = positions.astype(jnp.float32)[:, None] * freqs[None, :]
    cosine = jnp.cos(angles)[:, None, :]
    sine = jnp.sin(angles)[:, None, :]
    first = vectors[..., :half]
    second = vectors[..., half:]
    return jnp.concatenate(
        [first * cosine - second * sine, second * cosine + first * sine], axis=-1
    )


def column_term(rows, weight):
    return lax.dot_general(
        weight, rows, (((0,), (1,)), ((), ())), preferred_element_type=jnp.float32
    )


def attn_kernel(limit_ref, span_ref, q_ref, cache_ref, bias_ref, nk_ref, nv_ref, o_ref, top_scr, tot_scr, acc_scr):
    slots = cache_ref.shape[0]
    span_size = nk_ref.shape[0]
    heads = q_ref.shape[0] // span_size
    scale = HD ** (-0.5)
    q_all = q_ref[...]
    row_i = lax.broadcasted_iota(jnp.int32, (span_size, span_size), 0)
    col_j = lax.broadcasted_iota(jnp.int32, (span_size, span_size), 1)
    new_ok = (col_j <= row_i) & (col_j < span_ref[0])
    dims = (((1,), (1,)), ((), ()))

    def cache_raw(s):
        return lax.dot_general(q_all, cache_ref[s, :, :HD], dims, preferred_element_type=jnp.float32)

    def new_raw(h):
        rows = q_ref[h * span_size : (h + 1) * span_size, :]
        return lax.dot_general(rows, nk_ref[...], dims, preferred_element_type=jnp.float32)

    top_scr[...] = jnp.full(top_scr.shape, NEG, jnp.float32)

    def max_step(s, carry):
        @pl.when(limit_ref[s] > 0)
        def _():
            top_scr[...] = jnp.maximum(top_scr[...], cache_raw(s) + bias_ref[pl.ds(s, 1), :])

        return carry

    lax.fori_loop(0, slots, max_step, 0)
    peaks = []
    for h in range(heads):
        part = slice(h * span_size, (h + 1) * span_size)
        raw_top = jnp.maximum(
            jnp.max(top_scr[part, :], axis=1, keepdims=True),
            jnp.max(jnp.where(new_ok, new_raw(h), NEG), axis=1, keepdims=True),
        )
        peaks.append(raw_top * scale)
    peak = jnp.concatenate(peaks, axis=0)

    tot_scr[...] = jnp.zeros(tot_scr.shape, jnp.float32)
    acc_scr[...] = jnp.zeros(acc_scr.shape, jnp.float32)

    def sum_step(s, carry):
        @pl.when(limit_ref[s] > 0)
        def _():
            w = jnp.exp(cache_raw(s) * scale + bias_ref[pl.ds(s, 1), :] - peak)
            tot_scr[...] += w
            acc_scr[...] += jnp.dot(
                w.astype(jnp.bfloat16), cache_ref[s, :, HD:], preferred_element_type=jnp.float32
            )

        return carry

    lax.fori_loop(0, slots, sum_step, 0)
    for h in range(heads):
        part = slice(h * span_size, (h + 1) * span_size)
        w = jnp.where(new_ok, jnp.exp(new_raw(h) * scale - peak[part, :]), 0.0)
        total = jnp.sum(tot_scr[part, :], axis=1, keepdims=True) + jnp.sum(w, axis=1, keepdims=True)
        summed = acc_scr[part, :] + jnp.dot(
            w.astype(jnp.bfloat16), nv_ref[...], preferred_element_type=jnp.float32
        )
        o_ref[part, :] = (summed / total).astype(o_ref.dtype)


def local_attention(limit, span, q_rows, cache_all, new_keys, new_vals):
    rows = q_rows.shape[0]
    bias = jnp.where(
        jnp.arange(BLK, dtype=jnp.int32)[None, :] < limit[:, None], 0.0, NEG
    ).astype(jnp.float32)

    def whole(shape):
        return pl.BlockSpec(shape, lambda i, *_: (0,) * len(shape))

    return pl.pallas_call(
        attn_kernel,
        out_shape=jax.ShapeDtypeStruct((rows, HD), jnp.bfloat16),
        grid_spec=pltpu.PrefetchScalarGridSpec(
            num_scalar_prefetch=2,
            grid=(1,),
            in_specs=[
                whole(q_rows.shape),
                whole(cache_all.shape),
                whole(bias.shape),
                whole(new_keys.shape),
                whole(new_vals.shape),
            ],
            out_specs=whole((rows, HD)),
            scratch_shapes=[
                pltpu.VMEM((rows, BLK), jnp.float32),
                pltpu.VMEM((rows, BLK), jnp.float32),
                pltpu.VMEM((rows, HD), jnp.float32),
            ],
        ),
    )(limit, span, q_rows, cache_all, bias, new_keys, new_vals)


def ffn_kernel(first, chunk, x_ref, gain_ref, wg_ref, wu_ref, wd_ref, o_ref, f_scr, g_acc, u_acc, h_scr):
    step = pl.program_id(0)

    @pl.when(step == 0)
    def _():
        wide = x_ref[...].astype(jnp.float32)
        f_scr[...] = lax.rsqrt(jnp.sum(wide * wide, axis=1, keepdims=True) / x_ref.shape[1] + EPS)
        g_acc[...] = jnp.zeros(g_acc.shape, jnp.float32)
        u_acc[...] = jnp.zeros(u_acc.shape, jnp.float32)

    @pl.when(step < first)
    def _():
        start = pl.multiple_of(jnp.minimum(step, first - 1) * chunk, chunk)
        part = x_ref[:, pl.ds(start, chunk)].astype(jnp.float32)
        x = (part * f_scr[...] * gain_ref[:, pl.ds(start, chunk)]).astype(jnp.bfloat16)
        dims = (((1,), (1,)), ((), ()))
        g_acc[...] += lax.dot_general(x, wg_ref[...], dims, preferred_element_type=jnp.float32)
        u_acc[...] += lax.dot_general(x, wu_ref[...], dims, preferred_element_type=jnp.float32)

    @pl.when(step == first - 1)
    def _():
        g = g_acc[...]
        h_scr[...] = (g / (1.0 + jnp.exp(-g)) * u_acc[...]).astype(h_scr.dtype)

    @pl.when(step >= first)
    def _():
        o_ref[...] = jnp.dot(h_scr[...], wd_ref[...], preferred_element_type=jnp.float32).astype(
            o_ref.dtype
        )


def feed_forward(full_mid, gain, w_gate, w_up, w_down):
    rows, width = full_mid.shape
    units = w_gate.shape[1]
    chunk = 1024 if width % 1024 == 0 else width
    first = width // chunk
    outs = w_down.shape[1] // chunk
    last = first - 1
    return pl.pallas_call(
        functools.partial(ffn_kernel, first, chunk),
        out_shape=jax.ShapeDtypeStruct((rows, w_down.shape[1]), jnp.bfloat16),
        grid=(first + outs,),
        in_specs=[
            pl.BlockSpec((rows, width), lambda i: (0, 0)),
            pl.BlockSpec((1, width), lambda i: (0, 0)),
            pl.BlockSpec((units, chunk), lambda i: (0, jnp.minimum(i, last))),
            pl.BlockSpec((units, chunk), lambda i: (0, jnp.minimum(i, last))),
            pl.BlockSpec((units, chunk), lambda i: (0, jnp.maximum(i - first, 0))),
        ],
        out_specs=pl.BlockSpec((rows, chunk), lambda i: (0, jnp.maximum(i - first, 0))),
        scratch_shapes=[
            pltpu.VMEM((rows, 1), jnp.float32),
            pltpu.VMEM((rows, units), jnp.float32),
            pltpu.VMEM((rows, units), jnp.float32),
            pltpu.VMEM((rows, units), jnp.bfloat16),
        ],
        compiler_params=pltpu.CompilerParams(dimension_semantics=("arbitrary",)),
    )(full_mid, gain.astype(jnp.float32).reshape(1, width), w_gate.T, w_up.T, w_down)


def kv_routes(tp_count, kv_width):
    per_head = HD // kv_width
    heads_dev = HQ // tp_count
    needs = []
    for dev in range(tp_count):
        group = dev * heads_dev // (HQ // KVH)
        keys = [group * per_head + u for u in range(per_head)]
        vals = [KVH * per_head + group * per_head + u for u in range(per_head)]
        own_head = dev * kv_width // HD
        own = [own_head * per_head + u for u in range(per_head)] if own_head < KVH else [dev] * per_head
        needs.append(keys + vals + own)
    rounds = []
    for entry in range(len(needs[0])):
        sets = []
        for dev in range(tp_count):
            src = needs[dev][entry]
            if src == dev:
                continue
            for pairs in sets:
                if all(a != src for a, _ in pairs):
                    pairs.append((src, dev))
                    break
            else:
                sets.append([(src, dev)])
        rounds.append(sets)
    selfs = [[needs[dev][entry] == dev for dev in range(tp_count)] for entry in range(len(needs[0]))]
    return per_head, rounds, selfs


def gather_ctx(value, count):
    parts = [value]
    for shift in range(1, count):
        pairs = [(i, (i + shift) % count) for i in range(count)]
        parts.append(lax.ppermute(value, "ctx", pairs))
    return parts


def per_device(
    resid,
    attn_gain,
    mlp_gain,
    w_query,
    w_kv,
    w_out,
    w_gate,
    w_up,
    w_down,
    kv_cache,
    cache_len,
    span_len,
    slot_req,
    slot_blk,
):
    span_size = resid.shape[0]
    ctx_count = lax.axis_size("ctx")
    q_cols = w_query.shape[1]
    heads_dev = q_cols // HD
    ctx_rank = lax.axis_index("ctx")
    tp_rank = lax.axis_index("tp")
    group = tp_rank * heads_dev // (HQ // KVH)
    my_len = cache_len[ctx_rank]
    my_span = span_len[ctx_rank]
    offsets = jnp.arange(span_size, dtype=jnp.int32)
    positions = my_len + offsets
    live_rows = offsets < my_span

    own_cache = jnp.concatenate(
        [
            lax.dynamic_slice_in_dim(kv_cache, group * HD, HD, 2),
            lax.dynamic_slice_in_dim(kv_cache, KVH * HD + group * HD, HD, 2),
        ],
        axis=2,
    )
    own_meta = jnp.stack([slot_req, slot_blk])
    cache_all = jnp.concatenate(gather_ctx(own_cache, ctx_count), axis=0)
    meta_all = jnp.concatenate(gather_ctx(own_meta, ctx_count), axis=1)

    full_resid = lax.all_gather(resid, "tp", axis=1, tiled=True)
    x_norm = rms_norm(full_resid, attn_gain)
    kv_piece = jnp.dot(x_norm, w_kv, preferred_element_type=jnp.float32).astype(jnp.bfloat16)
    kv_width = kv_piece.shape[1]
    tp_count = lax.axis_size("tp")
    per_head, rounds, selfs = kv_routes(tp_count, kv_width)
    blocks = []
    for entry, sets in enumerate(rounds):
        is_self = jnp.asarray(selfs[entry])[tp_rank]
        got = jnp.where(is_self, kv_piece, jnp.zeros_like(kv_piece))
        for pairs in sets:
            got = got + lax.ppermute(kv_piece, "tp", pairs)
        blocks.append(got)

    def head_of(parts):
        return jnp.concatenate(parts, axis=1) if len(parts) > 1 else parts[0]

    def rotated(raw):
        return (
            rotate(raw.astype(jnp.float32).reshape(span_size, 1, HD), positions)
            .astype(jnp.bfloat16)
            .reshape(span_size, HD)
        )

    new_keys = rotated(head_of(blocks[:per_head]))
    new_vals = head_of(blocks[per_head : 2 * per_head])
    own_rot = lax.dynamic_slice_in_dim(
        rotated(head_of(blocks[2 * per_head :])), (tp_rank * kv_width) % HD, kv_width, 1
    )
    mine = jnp.where(tp_rank * kv_width < KVH * HD, own_rot, kv_piece)
    new_kv = jnp.where(live_rows[:, None], mine, jnp.zeros_like(mine))
    query = rotate(
        jnp.dot(x_norm, w_query, preferred_element_type=jnp.float32).reshape(
            span_size, heads_dev, HD
        ),
        positions,
    ).astype(jnp.bfloat16)

    limit = jnp.where(
        meta_all[0] == ctx_rank, jnp.clip(my_len - meta_all[1] * BLK, 0, BLK), 0
    ).astype(jnp.int32)
    q_rows = query.transpose(1, 0, 2).reshape(heads_dev * span_size, HD)
    attn_heads = local_attention(
        limit, my_span.reshape(1).astype(jnp.int32), q_rows, cache_all, new_keys, new_vals
    )
    attn_rows = (
        attn_heads.reshape(heads_dev, span_size, HD).transpose(1, 0, 2).reshape(span_size, q_cols)
    )
    head_sum = lax.psum_scatter(
        column_term(attn_rows, w_out).astype(jnp.bfloat16), "tp", scatter_dimension=0, tiled=True
    ).astype(jnp.float32)
    mid = (resid.astype(jnp.float32) + head_sum.T).astype(jnp.bfloat16)
    full_mid = lax.all_gather(mid, "tp", axis=1, tiled=True)
    down_sum = lax.psum_scatter(
        feed_forward(full_mid, mlp_gain, w_gate, w_up, w_down), "tp", scatter_dimension=1, tiled=True
    ).astype(jnp.float32)
    layer_out = (mid.astype(jnp.float32) + down_sum).astype(jnp.bfloat16)
    layer_out = jnp.where(live_rows[:, None], layer_out, jnp.zeros_like(layer_out))
    return (layer_out, new_kv)


def solution(mesh):
    return jax.shard_map(
        per_device,
        mesh=mesh,
        in_specs=(
            P("ctx", "tp"),
            P(),
            P(),
            P(None, "tp"),
            P(None, "tp"),
            P("tp", None),
            P(None, "tp"),
            P(None, "tp"),
            P("tp", None),
            P("ctx", None, None),
            P(),
            P(),
            P("ctx"),
            P("ctx"),
        ),
        out_specs=(P("ctx", "tp"), P("ctx", "tp")),
        check_vma=False,
    )
```

```python
import functools

import jax
import jax.numpy as jnp
from jax import lax
from jax.sharding import PartitionSpec as P
from jax.experimental import pallas as pl
from jax.experimental.pallas import tpu as pltpu

HQ = 32
KVH = 4
HD = 128
BLK = 128


THETA = 5000000.0
EPS = 1e-05
NEG = -1e30


def rms_norm(values, gain):
    wide = values.astype(jnp.float32)
    factor = lax.rsqrt(jnp.mean(wide * wide, axis=-1, keepdims=True) + EPS)
    return (wide * factor * gain.astype(jnp.float32)).astype(jnp.bfloat16)


def rotate(vectors, positions):
    width = vectors.shape[-1]
    half = width // 2
    freqs = THETA ** (-(jnp.arange(half, dtype=jnp.float32) * 2.0 / width))
    angles = positions.astype(jnp.float32)[:, None] * freqs[None, :]
    cosine = jnp.cos(angles)[:, None, :]
    sine = jnp.sin(angles)[:, None, :]
    first = vectors[..., :half]
    second = vectors[..., half:]
    return jnp.concatenate(
        [first * cosine - second * sine, second * cosine + first * sine], axis=-1
    )


def column_term(rows, weight):
    return lax.dot_general(
        weight, rows, (((0,), (1,)), ((), ())), preferred_element_type=jnp.float32
    )


def attn_kernel(
    limit_ref, span_ref, q_ref, cache_ref, bias_ref, nk_ref, nv_ref, wo_ref, o_ref, top_scr, tot_scr, acc_scr, out_scr
):
    slots = cache_ref.shape[0]
    span_size = nk_ref.shape[0]
    heads = q_ref.shape[0] // span_size
    scale = HD ** (-0.5)
    q_all = q_ref[...]
    row_i = lax.broadcasted_iota(jnp.int32, (span_size, span_size), 0)
    col_j = lax.broadcasted_iota(jnp.int32, (span_size, span_size), 1)
    new_ok = (col_j <= row_i) & (col_j < span_ref[0])
    dims = (((1,), (1,)), ((), ()))

    def cache_raw(s):
        return lax.dot_general(q_all, cache_ref[s, :, :HD], dims, preferred_element_type=jnp.float32)

    def new_raw(h):
        rows = q_ref[h * span_size : (h + 1) * span_size, :]
        return lax.dot_general(rows, nk_ref[...], dims, preferred_element_type=jnp.float32)

    top_scr[...] = jnp.full(top_scr.shape, NEG, jnp.float32)

    def max_step(s, carry):
        @pl.when(limit_ref[s] > 0)
        def _():
            top_scr[...] = jnp.maximum(top_scr[...], cache_raw(s) + bias_ref[pl.ds(s, 1), :])

        return carry

    lax.fori_loop(0, slots, max_step, 0)
    peaks = []
    for h in range(heads):
        part = slice(h * span_size, (h + 1) * span_size)
        raw_top = jnp.maximum(
            jnp.max(top_scr[part, :], axis=1, keepdims=True),
            jnp.max(jnp.where(new_ok, new_raw(h), NEG), axis=1, keepdims=True),
        )
        peaks.append(raw_top * scale)
    peak = jnp.concatenate(peaks, axis=0)

    tot_scr[...] = jnp.zeros(tot_scr.shape, jnp.float32)
    acc_scr[...] = jnp.zeros(acc_scr.shape, jnp.float32)

    def sum_step(s, carry):
        @pl.when(limit_ref[s] > 0)
        def _():
            w = jnp.exp(cache_raw(s) * scale + bias_ref[pl.ds(s, 1), :] - peak)
            tot_scr[...] += w
            acc_scr[...] += jnp.dot(
                w.astype(jnp.bfloat16), cache_ref[s, :, HD:], preferred_element_type=jnp.float32
            )

        return carry

    lax.fori_loop(0, slots, sum_step, 0)
    for h in range(heads):
        part = slice(h * span_size, (h + 1) * span_size)
        w = jnp.where(new_ok, jnp.exp(new_raw(h) * scale - peak[part, :]), 0.0)
        total = jnp.sum(tot_scr[part, :], axis=1, keepdims=True) + jnp.sum(w, axis=1, keepdims=True)
        summed = acc_scr[part, :] + jnp.dot(
            w.astype(jnp.bfloat16), nv_ref[...], preferred_element_type=jnp.float32
        )
        head_out = (summed / total).astype(jnp.bfloat16)
        term = jnp.dot(head_out, wo_ref[h * HD : (h + 1) * HD, :], preferred_element_type=jnp.float32)
        if h == 0:
            out_scr[...] = term
        else:
            out_scr[...] += term
    o_ref[...] = out_scr[...].astype(o_ref.dtype)


def local_attention(limit, span, q_rows, cache_all, new_keys, new_vals, w_out):
    rows = q_rows.shape[0]
    span_size = new_keys.shape[0]
    width = w_out.shape[1]
    bias = jnp.where(
        jnp.arange(BLK, dtype=jnp.int32)[None, :] < limit[:, None], 0.0, NEG
    ).astype(jnp.float32)

    def whole(shape):
        return pl.BlockSpec(shape, lambda i, *_: (0,) * len(shape))

    return pl.pallas_call(
        attn_kernel,
        out_shape=jax.ShapeDtypeStruct((span_size, width), jnp.bfloat16),
        grid_spec=pltpu.PrefetchScalarGridSpec(
            num_scalar_prefetch=2,
            grid=(1,),
            in_specs=[
                whole(q_rows.shape),
                whole(cache_all.shape),
                whole(bias.shape),
                whole(new_keys.shape),
                whole(new_vals.shape),
                whole(w_out.shape),
            ],
            out_specs=whole((span_size, width)),
            scratch_shapes=[
                pltpu.VMEM((rows, BLK), jnp.float32),
                pltpu.VMEM((rows, BLK), jnp.float32),
                pltpu.VMEM((rows, HD), jnp.float32),
                pltpu.VMEM((span_size, width), jnp.float32),
            ],
        ),
    )(limit, span, q_rows, cache_all, bias, new_keys, new_vals, w_out)


def ffn_kernel(first, chunk, x_ref, gain_ref, wg_ref, wu_ref, wd_ref, o_ref, f_scr, g_acc, u_acc, h_scr):
    step = pl.program_id(0)

    @pl.when(step == 0)
    def _():
        wide = x_ref[...].astype(jnp.float32)
        f_scr[...] = lax.rsqrt(jnp.sum(wide * wide, axis=1, keepdims=True) / x_ref.shape[1] + EPS)
        g_acc[...] = jnp.zeros(g_acc.shape, jnp.float32)
        u_acc[...] = jnp.zeros(u_acc.shape, jnp.float32)

    @pl.when(step < first)
    def _():
        start = pl.multiple_of(jnp.minimum(step, first - 1) * chunk, chunk)
        part = x_ref[:, pl.ds(start, chunk)].astype(jnp.float32)
        x = (part * f_scr[...] * gain_ref[:, pl.ds(start, chunk)]).astype(jnp.bfloat16)
        dims = (((1,), (1,)), ((), ()))
        g_acc[...] += lax.dot_general(x, wg_ref[...], dims, preferred_element_type=jnp.float32)
        u_acc[...] += lax.dot_general(x, wu_ref[...], dims, preferred_element_type=jnp.float32)

    @pl.when(step == first - 1)
    def _():
        g = g_acc[...]
        h_scr[...] = (g / (1.0 + jnp.exp(-g)) * u_acc[...]).astype(h_scr.dtype)

    @pl.when(step >= first)
    def _():
        o_ref[...] = jnp.dot(h_scr[...], wd_ref[...], preferred_element_type=jnp.float32).astype(
            o_ref.dtype
        )


def feed_forward(full_mid, gain, w_gate, w_up, w_down):
    rows, width = full_mid.shape
    units = w_gate.shape[1]
    chunk = 1024 if width % 1024 == 0 else width
    first = width // chunk
    outs = w_down.shape[1] // chunk
    last = first - 1
    return pl.pallas_call(
        functools.partial(ffn_kernel, first, chunk),
        out_shape=jax.ShapeDtypeStruct((rows, w_down.shape[1]), jnp.bfloat16),
        grid=(first + outs,),
        in_specs=[
            pl.BlockSpec((rows, width), lambda i: (0, 0)),
            pl.BlockSpec((1, width), lambda i: (0, 0)),
            pl.BlockSpec((units, chunk), lambda i: (0, jnp.minimum(i, last))),
            pl.BlockSpec((units, chunk), lambda i: (0, jnp.minimum(i, last))),
            pl.BlockSpec((units, chunk), lambda i: (0, jnp.maximum(i - first, 0))),
        ],
        out_specs=pl.BlockSpec((rows, chunk), lambda i: (0, jnp.maximum(i - first, 0))),
        scratch_shapes=[
            pltpu.VMEM((rows, 1), jnp.float32),
            pltpu.VMEM((rows, units), jnp.float32),
            pltpu.VMEM((rows, units), jnp.float32),
            pltpu.VMEM((rows, units), jnp.bfloat16),
        ],
        compiler_params=pltpu.CompilerParams(dimension_semantics=("arbitrary",)),
    )(full_mid, gain.astype(jnp.float32).reshape(1, width), w_gate.T, w_up.T, w_down)


def kv_routes(tp_count, kv_width):
    per_head = HD // kv_width
    heads_dev = HQ // tp_count
    needs = []
    for dev in range(tp_count):
        group = dev * heads_dev // (HQ // KVH)
        keys = [group * per_head + u for u in range(per_head)]
        vals = [KVH * per_head + group * per_head + u for u in range(per_head)]
        own_head = dev * kv_width // HD
        own = [own_head * per_head + u for u in range(per_head)] if own_head < KVH else [dev] * per_head
        needs.append(keys + vals + own)
    rounds = []
    for entry in range(len(needs[0])):
        sets = []
        for dev in range(tp_count):
            src = needs[dev][entry]
            if src == dev:
                continue
            for pairs in sets:
                if all(a != src for a, _ in pairs):
                    pairs.append((src, dev))
                    break
            else:
                sets.append([(src, dev)])
        rounds.append(sets)
    selfs = [[needs[dev][entry] == dev for dev in range(tp_count)] for entry in range(len(needs[0]))]
    return per_head, rounds, selfs


def gather_ctx(value, count):
    parts = [value]
    for shift in range(1, count):
        pairs = [(i, (i + shift) % count) for i in range(count)]
        parts.append(lax.ppermute(value, "ctx", pairs))
    return parts


def per_device(
    resid,
    attn_gain,
    mlp_gain,
    w_query,
    w_kv,
    w_out,
    w_gate,
    w_up,
    w_down,
    kv_cache,
    cache_len,
    span_len,
    slot_req,
    slot_blk,
):
    span_size = resid.shape[0]
    ctx_count = lax.axis_size("ctx")
    q_cols = w_query.shape[1]
    heads_dev = q_cols // HD
    ctx_rank = lax.axis_index("ctx")
    tp_rank = lax.axis_index("tp")
    group = tp_rank * heads_dev // (HQ // KVH)
    my_len = cache_len[ctx_rank]
    my_span = span_len[ctx_rank]
    offsets = jnp.arange(span_size, dtype=jnp.int32)
    positions = my_len + offsets
    live_rows = offsets < my_span

    own_cache = jnp.concatenate(
        [
            lax.dynamic_slice_in_dim(kv_cache, group * HD, HD, 2),
            lax.dynamic_slice_in_dim(kv_cache, KVH * HD + group * HD, HD, 2),
        ],
        axis=2,
    )
    own_meta = jnp.stack([slot_req, slot_blk])
    cache_all = jnp.concatenate(gather_ctx(own_cache, ctx_count), axis=0)
    meta_all = jnp.concatenate(gather_ctx(own_meta, ctx_count), axis=1)

    full_resid = lax.all_gather(resid, "tp", axis=1, tiled=True)
    x_norm = rms_norm(full_resid, attn_gain)
    kv_piece = jnp.dot(x_norm, w_kv, preferred_element_type=jnp.float32).astype(jnp.bfloat16)
    kv_width = kv_piece.shape[1]
    tp_count = lax.axis_size("tp")
    per_head, rounds, selfs = kv_routes(tp_count, kv_width)
    blocks = []
    for entry, sets in enumerate(rounds):
        is_self = jnp.asarray(selfs[entry])[tp_rank]
        got = jnp.where(is_self, kv_piece, jnp.zeros_like(kv_piece))
        for pairs in sets:
            got = got + lax.ppermute(kv_piece, "tp", pairs)
        blocks.append(got)

    def head_of(parts):
        return jnp.concatenate(parts, axis=1) if len(parts) > 1 else parts[0]

    def rotated(raw):
        return (
            rotate(raw.astype(jnp.float32).reshape(span_size, 1, HD), positions)
            .astype(jnp.bfloat16)
            .reshape(span_size, HD)
        )

    new_keys = rotated(head_of(blocks[:per_head]))
    new_vals = head_of(blocks[per_head : 2 * per_head])
    own_rot = lax.dynamic_slice_in_dim(
        rotated(head_of(blocks[2 * per_head :])), (tp_rank * kv_width) % HD, kv_width, 1
    )
    mine = jnp.where(tp_rank * kv_width < KVH * HD, own_rot, kv_piece)
    new_kv = jnp.where(live_rows[:, None], mine, jnp.zeros_like(mine))
    query = rotate(
        jnp.dot(x_norm, w_query, preferred_element_type=jnp.float32).reshape(
            span_size, heads_dev, HD
        ),
        positions,
    ).astype(jnp.bfloat16)

    limit = jnp.where(
        meta_all[0] == ctx_rank, jnp.clip(my_len - meta_all[1] * BLK, 0, BLK), 0
    ).astype(jnp.int32)
    q_rows = query.transpose(1, 0, 2).reshape(heads_dev * span_size, HD)
    head_term = local_attention(
        limit, my_span.reshape(1).astype(jnp.int32), q_rows, cache_all, new_keys, new_vals, w_out
    )
    head_sum = lax.psum_scatter(head_term, "tp", scatter_dimension=1, tiled=True).astype(jnp.float32)
    mid = (resid.astype(jnp.float32) + head_sum).astype(jnp.bfloat16)
    full_mid = lax.all_gather(mid, "tp", axis=1, tiled=True)
    down_sum = lax.psum_scatter(
        feed_forward(full_mid, mlp_gain, w_gate, w_up, w_down), "tp", scatter_dimension=1, tiled=True
    ).astype(jnp.float32)
    layer_out = (mid.astype(jnp.float32) + down_sum).astype(jnp.bfloat16)
    layer_out = jnp.where(live_rows[:, None], layer_out, jnp.zeros_like(layer_out))
    return (layer_out, new_kv)


def solution(mesh):
    return jax.shard_map(
        per_device,
        mesh=mesh,
        in_specs=(
            P("ctx", "tp"),
            P(),
            P(),
            P(None, "tp"),
            P(None, "tp"),
            P("tp", None),
            P(None, "tp"),
            P(None, "tp"),
            P("tp", None),
            P("ctx", None, None),
            P(),
            P(),
            P("ctx"),
            P("ctx"),
        ),
        out_specs=(P("ctx", "tp"), P("ctx", "tp")),
        check_vma=False,
    )
```

```python
import functools

import jax
import jax.numpy as jnp
from jax import lax
from jax.sharding import PartitionSpec as P
from jax.experimental import pallas as pl
from jax.experimental.pallas import tpu as pltpu

HQ = 32
KVH = 4
HD = 128
BLK = 128


THETA = 5000000.0
EPS = 1e-05
NEG = -1e30


def rms_norm(values, gain):
    wide = values.astype(jnp.float32)
    factor = lax.rsqrt(jnp.mean(wide * wide, axis=-1, keepdims=True) + EPS)
    return (wide * factor * gain.astype(jnp.float32)).astype(jnp.bfloat16)


def rotate(vectors, positions):
    width = vectors.shape[-1]
    half = width // 2
    freqs = THETA ** (-(jnp.arange(half, dtype=jnp.float32) * 2.0 / width))
    angles = positions.astype(jnp.float32)[:, None] * freqs[None, :]
    cosine = jnp.cos(angles)[:, None, :]
    sine = jnp.sin(angles)[:, None, :]
    first = vectors[..., :half]
    second = vectors[..., half:]
    return jnp.concatenate(
        [first * cosine - second * sine, second * cosine + first * sine], axis=-1
    )


def column_term(rows, weight):
    return lax.dot_general(
        weight, rows, (((0,), (1,)), ((), ())), preferred_element_type=jnp.float32
    )


def attn_kernel(
    limit_ref, span_ref, q_ref, cache_ref, bias_ref, nk_ref, nv_ref, wo_hbm, o_ref,
    top_scr, tot_scr, acc_scr, out_scr, wo_ref, wo_sem
):
    slots = cache_ref.shape[0]
    span_size = nk_ref.shape[0]
    heads = q_ref.shape[0] // span_size
    scale = HD ** (-0.5)
    wo_copy = pltpu.make_async_copy(wo_hbm, wo_ref, wo_sem)
    wo_copy.start()
    q_all = q_ref[...]
    row_i = lax.broadcasted_iota(jnp.int32, (span_size, span_size), 0)
    col_j = lax.broadcasted_iota(jnp.int32, (span_size, span_size), 1)
    new_ok = (col_j <= row_i) & (col_j < span_ref[0])
    dims = (((1,), (1,)), ((), ()))

    def cache_raw(s):
        return lax.dot_general(q_all, cache_ref[s, :, :HD], dims, preferred_element_type=jnp.float32)

    def new_raw(h):
        rows = q_ref[h * span_size : (h + 1) * span_size, :]
        return lax.dot_general(rows, nk_ref[...], dims, preferred_element_type=jnp.float32)

    top_scr[...] = jnp.full(top_scr.shape, NEG, jnp.float32)

    def max_step(s, carry):
        @pl.when(limit_ref[s] > 0)
        def _():
            top_scr[...] = jnp.maximum(top_scr[...], cache_raw(s) + bias_ref[pl.ds(s, 1), :])

        return carry

    lax.fori_loop(0, slots, max_step, 0)
    peaks = []
    for h in range(heads):
        part = slice(h * span_size, (h + 1) * span_size)
        raw_top = jnp.maximum(
            jnp.max(top_scr[part, :], axis=1, keepdims=True),
            jnp.max(jnp.where(new_ok, new_raw(h), NEG), axis=1, keepdims=True),
        )
        peaks.append(raw_top * scale)
    peak = jnp.concatenate(peaks, axis=0)

    tot_scr[...] = jnp.zeros(tot_scr.shape, jnp.float32)
    acc_scr[...] = jnp.zeros(acc_scr.shape, jnp.float32)

    def sum_step(s, carry):
        @pl.when(limit_ref[s] > 0)
        def _():
            w = jnp.exp(cache_raw(s) * scale + bias_ref[pl.ds(s, 1), :] - peak)
            tot_scr[...] += w
            acc_scr[...] += jnp.dot(
                w.astype(jnp.bfloat16), cache_ref[s, :, HD:], preferred_element_type=jnp.float32
            )

        return carry

    lax.fori_loop(0, slots, sum_step, 0)
    wo_copy.wait()
    for h in range(heads):
        part = slice(h * span_size, (h + 1) * span_size)
        w = jnp.where(new_ok, jnp.exp(new_raw(h) * scale - peak[part, :]), 0.0)
        total = jnp.sum(tot_scr[part, :], axis=1, keepdims=True) + jnp.sum(w, axis=1, keepdims=True)
        summed = acc_scr[part, :] + jnp.dot(
            w.astype(jnp.bfloat16), nv_ref[...], preferred_element_type=jnp.float32
        )
        head_out = (summed / total).astype(jnp.bfloat16)
        term = jnp.dot(head_out, wo_ref[h * HD : (h + 1) * HD, :], preferred_element_type=jnp.float32)
        if h == 0:
            out_scr[...] = term
        else:
            out_scr[...] += term
    o_ref[...] = out_scr[...].astype(o_ref.dtype)


def local_attention(limit, span, q_rows, cache_all, new_keys, new_vals, w_out):
    rows = q_rows.shape[0]
    span_size = new_keys.shape[0]
    width = w_out.shape[1]
    bias = jnp.where(
        jnp.arange(BLK, dtype=jnp.int32)[None, :] < limit[:, None], 0.0, NEG
    ).astype(jnp.float32)

    def whole(shape):
        return pl.BlockSpec(shape, lambda i, *_: (0,) * len(shape))

    return pl.pallas_call(
        attn_kernel,
        out_shape=jax.ShapeDtypeStruct((span_size, width), jnp.bfloat16),
        grid_spec=pltpu.PrefetchScalarGridSpec(
            num_scalar_prefetch=2,
            grid=(1,),
            in_specs=[
                whole(q_rows.shape),
                whole(cache_all.shape),
                whole(bias.shape),
                whole(new_keys.shape),
                whole(new_vals.shape),
                pl.BlockSpec(memory_space=pl.ANY),
            ],
            out_specs=whole((span_size, width)),
            scratch_shapes=[
                pltpu.VMEM((rows, BLK), jnp.float32),
                pltpu.VMEM((rows, BLK), jnp.float32),
                pltpu.VMEM((rows, HD), jnp.float32),
                pltpu.VMEM((span_size, width), jnp.float32),
                pltpu.VMEM(w_out.shape, w_out.dtype),
                pltpu.SemaphoreType.DMA(()),
            ],
        ),
    )(limit, span, q_rows, cache_all, bias, new_keys, new_vals, w_out)


def ffn_kernel(first, chunk, x_ref, gain_ref, wg_ref, wu_ref, wd_ref, o_ref, f_scr, g_acc, u_acc, h_scr):
    step = pl.program_id(0)

    @pl.when(step == 0)
    def _():
        wide = x_ref[...].astype(jnp.float32)
        f_scr[...] = lax.rsqrt(jnp.sum(wide * wide, axis=1, keepdims=True) / x_ref.shape[1] + EPS)
        g_acc[...] = jnp.zeros(g_acc.shape, jnp.float32)
        u_acc[...] = jnp.zeros(u_acc.shape, jnp.float32)

    @pl.when(step < first)
    def _():
        start = pl.multiple_of(jnp.minimum(step, first - 1) * chunk, chunk)
        part = x_ref[:, pl.ds(start, chunk)].astype(jnp.float32)
        x = (part * f_scr[...] * gain_ref[:, pl.ds(start, chunk)]).astype(jnp.bfloat16)
        dims = (((1,), (1,)), ((), ()))
        g_acc[...] += lax.dot_general(x, wg_ref[...], dims, preferred_element_type=jnp.float32)
        u_acc[...] += lax.dot_general(x, wu_ref[...], dims, preferred_element_type=jnp.float32)

    @pl.when(step == first - 1)
    def _():
        g = g_acc[...]
        h_scr[...] = (g / (1.0 + jnp.exp(-g)) * u_acc[...]).astype(h_scr.dtype)

    @pl.when(step >= first)
    def _():
        o_ref[...] = jnp.dot(h_scr[...], wd_ref[...], preferred_element_type=jnp.float32).astype(
            o_ref.dtype
        )


def feed_forward(full_mid, gain, w_gate, w_up, w_down):
    rows, width = full_mid.shape
    units = w_gate.shape[1]
    chunk = 1024 if width % 1024 == 0 else width
    first = width // chunk
    outs = w_down.shape[1] // chunk
    last = first - 1
    return pl.pallas_call(
        functools.partial(ffn_kernel, first, chunk),
        out_shape=jax.ShapeDtypeStruct((rows, w_down.shape[1]), jnp.bfloat16),
        grid=(first + outs,),
        in_specs=[
            pl.BlockSpec((rows, width), lambda i: (0, 0)),
            pl.BlockSpec((1, width), lambda i: (0, 0)),
            pl.BlockSpec((units, chunk), lambda i: (0, jnp.minimum(i, last))),
            pl.BlockSpec((units, chunk), lambda i: (0, jnp.minimum(i, last))),
            pl.BlockSpec((units, chunk), lambda i: (0, jnp.maximum(i - first, 0))),
        ],
        out_specs=pl.BlockSpec((rows, chunk), lambda i: (0, jnp.maximum(i - first, 0))),
        scratch_shapes=[
            pltpu.VMEM((rows, 1), jnp.float32),
            pltpu.VMEM((rows, units), jnp.float32),
            pltpu.VMEM((rows, units), jnp.float32),
            pltpu.VMEM((rows, units), jnp.bfloat16),
        ],
        compiler_params=pltpu.CompilerParams(dimension_semantics=("arbitrary",)),
    )(full_mid, gain.astype(jnp.float32).reshape(1, width), w_gate.T, w_up.T, w_down)


def kv_routes(tp_count, kv_width):
    per_head = HD // kv_width
    heads_dev = HQ // tp_count
    needs = []
    for dev in range(tp_count):
        group = dev * heads_dev // (HQ // KVH)
        keys = [group * per_head + u for u in range(per_head)]
        vals = [KVH * per_head + group * per_head + u for u in range(per_head)]
        own_head = dev * kv_width // HD
        own = [own_head * per_head + u for u in range(per_head)] if own_head < KVH else [dev] * per_head
        needs.append(keys + vals + own)
    rounds = []
    for entry in range(len(needs[0])):
        sets = []
        for dev in range(tp_count):
            src = needs[dev][entry]
            if src == dev:
                continue
            for pairs in sets:
                if all(a != src for a, _ in pairs):
                    pairs.append((src, dev))
                    break
            else:
                sets.append([(src, dev)])
        rounds.append(sets)
    selfs = [[needs[dev][entry] == dev for dev in range(tp_count)] for entry in range(len(needs[0]))]
    return per_head, rounds, selfs


def gather_ctx(value, count):
    parts = [value]
    for shift in range(1, count):
        pairs = [(i, (i + shift) % count) for i in range(count)]
        parts.append(lax.ppermute(value, "ctx", pairs))
    return parts


def per_device(
    resid,
    attn_gain,
    mlp_gain,
    w_query,
    w_kv,
    w_out,
    w_gate,
    w_up,
    w_down,
    kv_cache,
    cache_len,
    span_len,
    slot_req,
    slot_blk,
):
    span_size = resid.shape[0]
    ctx_count = lax.axis_size("ctx")
    q_cols = w_query.shape[1]
    heads_dev = q_cols // HD
    ctx_rank = lax.axis_index("ctx")
    tp_rank = lax.axis_index("tp")
    group = tp_rank * heads_dev // (HQ // KVH)
    my_len = cache_len[ctx_rank]
    my_span = span_len[ctx_rank]
    offsets = jnp.arange(span_size, dtype=jnp.int32)
    positions = my_len + offsets
    live_rows = offsets < my_span

    own_cache = jnp.concatenate(
        [
            lax.dynamic_slice_in_dim(kv_cache, group * HD, HD, 2),
            lax.dynamic_slice_in_dim(kv_cache, KVH * HD + group * HD, HD, 2),
        ],
        axis=2,
    )
    own_meta = jnp.stack([slot_req, slot_blk])
    cache_all = jnp.concatenate(gather_ctx(own_cache, ctx_count), axis=0)
    meta_all = jnp.concatenate(gather_ctx(own_meta, ctx_count), axis=1)

    full_resid = lax.all_gather(resid, "tp", axis=1, tiled=True)
    x_norm = rms_norm(full_resid, attn_gain)
    kv_piece = jnp.dot(x_norm, w_kv, preferred_element_type=jnp.float32).astype(jnp.bfloat16)
    kv_width = kv_piece.shape[1]
    tp_count = lax.axis_size("tp")
    per_head, rounds, selfs = kv_routes(tp_count, kv_width)
    blocks = []
    for entry, sets in enumerate(rounds):
        is_self = jnp.asarray(selfs[entry])[tp_rank]
        got = jnp.where(is_self, kv_piece, jnp.zeros_like(kv_piece))
        for pairs in sets:
            got = got + lax.ppermute(kv_piece, "tp", pairs)
        blocks.append(got)

    def head_of(parts):
        return jnp.concatenate(parts, axis=1) if len(parts) > 1 else parts[0]

    def rotated(raw):
        return (
            rotate(raw.astype(jnp.float32).reshape(span_size, 1, HD), positions)
            .astype(jnp.bfloat16)
            .reshape(span_size, HD)
        )

    new_keys = rotated(head_of(blocks[:per_head]))
    new_vals = head_of(blocks[per_head : 2 * per_head])
    own_rot = lax.dynamic_slice_in_dim(
        rotated(head_of(blocks[2 * per_head :])), (tp_rank * kv_width) % HD, kv_width, 1
    )
    mine = jnp.where(tp_rank * kv_width < KVH * HD, own_rot, kv_piece)
    new_kv = jnp.where(live_rows[:, None], mine, jnp.zeros_like(mine))
    query = rotate(
        jnp.dot(x_norm, w_query, preferred_element_type=jnp.float32).reshape(
            span_size, heads_dev, HD
        ),
        positions,
    ).astype(jnp.bfloat16)

    limit = jnp.where(
        meta_all[0] == ctx_rank, jnp.clip(my_len - meta_all[1] * BLK, 0, BLK), 0
    ).astype(jnp.int32)
    q_rows = query.transpose(1, 0, 2).reshape(heads_dev * span_size, HD)
    head_term = local_attention(
        limit, my_span.reshape(1).astype(jnp.int32), q_rows, cache_all, new_keys, new_vals, w_out
    )
    head_sum = lax.psum_scatter(head_term, "tp", scatter_dimension=1, tiled=True).astype(jnp.float32)
    mid = (resid.astype(jnp.float32) + head_sum).astype(jnp.bfloat16)
    full_mid = lax.all_gather(mid, "tp", axis=1, tiled=True)
    down_sum = lax.psum_scatter(
        feed_forward(full_mid, mlp_gain, w_gate, w_up, w_down), "tp", scatter_dimension=1, tiled=True
    ).astype(jnp.float32)
    layer_out = (mid.astype(jnp.float32) + down_sum).astype(jnp.bfloat16)
    layer_out = jnp.where(live_rows[:, None], layer_out, jnp.zeros_like(layer_out))
    return (layer_out, new_kv)


def solution(mesh):
    return jax.shard_map(
        per_device,
        mesh=mesh,
        in_specs=(
            P("ctx", "tp"),
            P(),
            P(),
            P(None, "tp"),
            P(None, "tp"),
            P("tp", None),
            P(None, "tp"),
            P(None, "tp"),
            P("tp", None),
            P("ctx", None, None),
            P(),
            P(),
            P("ctx"),
            P("ctx"),
        ),
        out_specs=(P("ctx", "tp"), P("ctx", "tp")),
        check_vma=False,
    )
```

```python
import functools

import jax
import jax.numpy as jnp
from jax import lax
from jax.sharding import PartitionSpec as P
from jax.experimental import pallas as pl
from jax.experimental.pallas import tpu as pltpu

HQ = 32
KVH = 4
HD = 128
BLK = 128


THETA = 5000000.0
EPS = 1e-05
NEG = -1e30


def rms_norm(values, gain):
    wide = values.astype(jnp.float32)
    factor = lax.rsqrt(jnp.mean(wide * wide, axis=-1, keepdims=True) + EPS)
    return (wide * factor * gain.astype(jnp.float32)).astype(jnp.bfloat16)


def rotate(vectors, positions):
    width = vectors.shape[-1]
    half = width // 2
    freqs = THETA ** (-(jnp.arange(half, dtype=jnp.float32) * 2.0 / width))
    angles = positions.astype(jnp.float32)[:, None] * freqs[None, :]
    cosine = jnp.cos(angles)[:, None, :]
    sine = jnp.sin(angles)[:, None, :]
    first = vectors[..., :half]
    second = vectors[..., half:]
    return jnp.concatenate(
        [first * cosine - second * sine, second * cosine + first * sine], axis=-1
    )


def column_term(rows, weight):
    return lax.dot_general(
        weight, rows, (((0,), (1,)), ((), ())), preferred_element_type=jnp.float32
    )


def attn_kernel(
    limit_ref, span_ref, q_ref, cache_ref, bias_ref, nk_ref, nv_ref, wo_hbm, o_ref,
    top_scr, tot_scr, acc_scr, out_scr, wo_ref, wo_sem
):
    slots = cache_ref.shape[0]
    span_size = nk_ref.shape[0]
    heads = q_ref.shape[0] // span_size
    scale = HD ** (-0.5)
    wo_copy = pltpu.make_async_copy(wo_hbm, wo_ref, wo_sem)
    wo_copy.start()
    q_all = q_ref[...]
    row_i = lax.broadcasted_iota(jnp.int32, (span_size, span_size), 0)
    col_j = lax.broadcasted_iota(jnp.int32, (span_size, span_size), 1)
    new_ok = (col_j <= row_i) & (col_j < span_ref[0])
    dims = (((1,), (1,)), ((), ()))

    def cache_raw(s):
        return lax.dot_general(q_all, cache_ref[s, :, :HD], dims, preferred_element_type=jnp.float32)

    def new_raw(h):
        rows = q_ref[h * span_size : (h + 1) * span_size, :]
        return lax.dot_general(rows, nk_ref[...], dims, preferred_element_type=jnp.float32)

    top_scr[...] = jnp.full(top_scr.shape, NEG, jnp.float32)

    def max_step(s, carry):
        @pl.when(limit_ref[s] > 0)
        def _():
            top_scr[...] = jnp.maximum(top_scr[...], cache_raw(s) + bias_ref[pl.ds(s, 1), :])

        return carry

    lax.fori_loop(0, slots, max_step, 0)
    peaks = []
    for h in range(heads):
        part = slice(h * span_size, (h + 1) * span_size)
        raw_top = jnp.maximum(
            jnp.max(top_scr[part, :], axis=1, keepdims=True),
            jnp.max(jnp.where(new_ok, new_raw(h), NEG), axis=1, keepdims=True),
        )
        peaks.append(raw_top * scale)
    peak = jnp.concatenate(peaks, axis=0)

    tot_scr[...] = jnp.zeros(tot_scr.shape, jnp.float32)
    acc_scr[...] = jnp.zeros(acc_scr.shape, jnp.float32)

    def sum_step(s, carry):
        @pl.when(limit_ref[s] > 0)
        def _():
            w = jnp.exp(cache_raw(s) * scale + bias_ref[pl.ds(s, 1), :] - peak)
            tot_scr[...] += w
            acc_scr[...] += jnp.dot(
                w.astype(jnp.bfloat16), cache_ref[s, :, HD:], preferred_element_type=jnp.float32
            )

        return carry

    lax.fori_loop(0, slots, sum_step, 0)
    wo_copy.wait()
    for h in range(heads):
        part = slice(h * span_size, (h + 1) * span_size)
        w = jnp.where(new_ok, jnp.exp(new_raw(h) * scale - peak[part, :]), 0.0)
        total = jnp.sum(tot_scr[part, :], axis=1, keepdims=True) + jnp.sum(w, axis=1, keepdims=True)
        summed = acc_scr[part, :] + jnp.dot(
            w.astype(jnp.bfloat16), nv_ref[...], preferred_element_type=jnp.float32
        )
        head_out = (summed / total).astype(jnp.bfloat16)
        term = jnp.dot(head_out, wo_ref[h * HD : (h + 1) * HD, :], preferred_element_type=jnp.float32)
        if h == 0:
            out_scr[...] = term
        else:
            out_scr[...] += term
    o_ref[...] = out_scr[...].astype(o_ref.dtype)


def local_attention(limit, span, q_rows, cache_all, new_keys, new_vals, w_out):
    rows = q_rows.shape[0]
    span_size = new_keys.shape[0]
    width = w_out.shape[1]
    bias = jnp.where(
        jnp.arange(BLK, dtype=jnp.int32)[None, :] < limit[:, None], 0.0, NEG
    ).astype(jnp.float32)

    def whole(shape):
        return pl.BlockSpec(shape, lambda i, *_: (0,) * len(shape))

    return pl.pallas_call(
        attn_kernel,
        out_shape=jax.ShapeDtypeStruct((span_size, width), jnp.bfloat16),
        grid_spec=pltpu.PrefetchScalarGridSpec(
            num_scalar_prefetch=2,
            grid=(1,),
            in_specs=[
                whole(q_rows.shape),
                whole(cache_all.shape),
                whole(bias.shape),
                whole(new_keys.shape),
                whole(new_vals.shape),
                pl.BlockSpec(memory_space=pl.ANY),
            ],
            out_specs=whole((span_size, width)),
            scratch_shapes=[
                pltpu.VMEM((rows, BLK), jnp.float32),
                pltpu.VMEM((rows, BLK), jnp.float32),
                pltpu.VMEM((rows, HD), jnp.float32),
                pltpu.VMEM((span_size, width), jnp.float32),
                pltpu.VMEM(w_out.shape, w_out.dtype),
                pltpu.SemaphoreType.DMA(()),
            ],
        ),
    )(limit, span, q_rows, cache_all, bias, new_keys, new_vals, w_out)


def ffn_kernel(first, chunk, x_ref, gain_ref, wg_ref, wu_ref, wd_ref, o_ref, f_scr, g_acc, u_acc, h_scr):
    step = pl.program_id(0)

    @pl.when(step == 0)
    def _():
        wide = x_ref[...].astype(jnp.float32)
        f_scr[...] = lax.rsqrt(jnp.sum(wide * wide, axis=1, keepdims=True) / x_ref.shape[1] + EPS)
        g_acc[...] = jnp.zeros(g_acc.shape, jnp.float32)
        u_acc[...] = jnp.zeros(u_acc.shape, jnp.float32)

    @pl.when(step < first)
    def _():
        start = pl.multiple_of(jnp.minimum(step, first - 1) * chunk, chunk)
        part = x_ref[:, pl.ds(start, chunk)].astype(jnp.float32)
        x = (part * f_scr[...] * gain_ref[:, pl.ds(start, chunk)]).astype(jnp.bfloat16)
        dims = (((1,), (1,)), ((), ()))
        g_acc[...] += lax.dot_general(x, wg_ref[...], dims, preferred_element_type=jnp.float32)
        u_acc[...] += lax.dot_general(x, wu_ref[...], dims, preferred_element_type=jnp.float32)

    @pl.when(step == first - 1)
    def _():
        g = g_acc[...]
        h_scr[...] = (g / (1.0 + jnp.exp(-g)) * u_acc[...]).astype(h_scr.dtype)

    @pl.when(step >= first)
    def _():
        o_ref[...] = jnp.dot(h_scr[...], wd_ref[...], preferred_element_type=jnp.float32).astype(
            o_ref.dtype
        )


def feed_forward(full_mid, gain, w_gate, w_up, w_down):
    rows, width = full_mid.shape
    units = w_gate.shape[1]
    chunk = 1024 if width % 1024 == 0 else width
    first = width // chunk
    outs = w_down.shape[1] // chunk
    last = first - 1
    return pl.pallas_call(
        functools.partial(ffn_kernel, first, chunk),
        out_shape=jax.ShapeDtypeStruct((rows, w_down.shape[1]), jnp.bfloat16),
        grid=(first + outs,),
        in_specs=[
            pl.BlockSpec((rows, width), lambda i: (0, 0)),
            pl.BlockSpec((1, width), lambda i: (0, 0)),
            pl.BlockSpec((units, chunk), lambda i: (0, jnp.minimum(i, last))),
            pl.BlockSpec((units, chunk), lambda i: (0, jnp.minimum(i, last))),
            pl.BlockSpec((units, chunk), lambda i: (0, jnp.maximum(i - first, 0))),
        ],
        out_specs=pl.BlockSpec((rows, chunk), lambda i: (0, jnp.maximum(i - first, 0))),
        scratch_shapes=[
            pltpu.VMEM((rows, 1), jnp.float32),
            pltpu.VMEM((rows, units), jnp.float32),
            pltpu.VMEM((rows, units), jnp.float32),
            pltpu.VMEM((rows, units), jnp.bfloat16),
        ],
        compiler_params=pltpu.CompilerParams(dimension_semantics=("arbitrary",)),
    )(full_mid, gain.astype(jnp.float32).reshape(1, width), w_gate.T, w_up.T, w_down)


def kv_routes(tp_count, kv_width):
    per_head = HD // kv_width
    heads_dev = HQ // tp_count
    needs = []
    for dev in range(tp_count):
        group = dev * heads_dev // (HQ // KVH)
        keys = [group * per_head + u for u in range(per_head)]
        vals = [KVH * per_head + group * per_head + u for u in range(per_head)]
        own_head = dev * kv_width // HD
        own = [own_head * per_head + u for u in range(per_head)] if own_head < KVH else [dev] * per_head
        needs.append(keys + vals + own)
    entries = len(needs[0])
    colours = []
    slot = [[-1] * tp_count for _ in range(entries)]
    for entry in range(entries):
        for dev in range(tp_count):
            src = needs[dev][entry]
            if src == dev:
                continue
            for index, pairs in enumerate(colours):
                if all(a != src and b != dev for a, b in pairs):
                    pairs.append((src, dev))
                    break
            else:
                index = len(colours)
                colours.append([(src, dev)])
            slot[entry][dev] = index
    selfs = [[needs[dev][entry] == dev for dev in range(tp_count)] for entry in range(entries)]
    return per_head, colours, slot, selfs


def gather_ctx(value, count):
    parts = [value]
    for shift in range(1, count):
        pairs = [(i, (i + shift) % count) for i in range(count)]
        parts.append(lax.ppermute(value, "ctx", pairs))
    return parts


def per_device(
    resid,
    attn_gain,
    mlp_gain,
    w_query,
    w_kv,
    w_out,
    w_gate,
    w_up,
    w_down,
    kv_cache,
    cache_len,
    span_len,
    slot_req,
    slot_blk,
):
    span_size = resid.shape[0]
    ctx_count = lax.axis_size("ctx")
    q_cols = w_query.shape[1]
    heads_dev = q_cols // HD
    ctx_rank = lax.axis_index("ctx")
    tp_rank = lax.axis_index("tp")
    group = tp_rank * heads_dev // (HQ // KVH)
    my_len = cache_len[ctx_rank]
    my_span = span_len[ctx_rank]
    offsets = jnp.arange(span_size, dtype=jnp.int32)
    positions = my_len + offsets
    live_rows = offsets < my_span

    own_cache = jnp.concatenate(
        [
            lax.dynamic_slice_in_dim(kv_cache, group * HD, HD, 2),
            lax.dynamic_slice_in_dim(kv_cache, KVH * HD + group * HD, HD, 2),
        ],
        axis=2,
    )
    own_meta = jnp.stack([slot_req, slot_blk])
    cache_all = jnp.concatenate(gather_ctx(own_cache, ctx_count), axis=0)
    meta_all = jnp.concatenate(gather_ctx(own_meta, ctx_count), axis=1)

    full_resid = lax.all_gather(resid, "tp", axis=1, tiled=True)
    x_norm = rms_norm(full_resid, attn_gain)
    kv_piece = jnp.dot(x_norm, w_kv, preferred_element_type=jnp.float32).astype(jnp.bfloat16)
    kv_width = kv_piece.shape[1]
    tp_count = lax.axis_size("tp")
    per_head, colours, slot, selfs = kv_routes(tp_count, kv_width)
    received = [lax.ppermute(kv_piece, "tp", pairs) for pairs in colours]
    zeros = jnp.zeros_like(kv_piece)
    blocks = []
    for entry in range(len(slot)):
        got = jnp.where(jnp.asarray(selfs[entry])[tp_rank], kv_piece, zeros)
        for index, value in enumerate(received):
            hit = jnp.asarray([slot[entry][dev] == index for dev in range(tp_count)])[tp_rank]
            got = got + jnp.where(hit, value, zeros)
        blocks.append(got)

    def head_of(parts):
        return jnp.concatenate(parts, axis=1) if len(parts) > 1 else parts[0]

    def rotated(raw):
        return (
            rotate(raw.astype(jnp.float32).reshape(span_size, 1, HD), positions)
            .astype(jnp.bfloat16)
            .reshape(span_size, HD)
        )

    new_keys = rotated(head_of(blocks[:per_head]))
    new_vals = head_of(blocks[per_head : 2 * per_head])
    own_rot = lax.dynamic_slice_in_dim(
        rotated(head_of(blocks[2 * per_head :])), (tp_rank * kv_width) % HD, kv_width, 1
    )
    mine = jnp.where(tp_rank * kv_width < KVH * HD, own_rot, kv_piece)
    new_kv = jnp.where(live_rows[:, None], mine, jnp.zeros_like(mine))
    query = rotate(
        jnp.dot(x_norm, w_query, preferred_element_type=jnp.float32).reshape(
            span_size, heads_dev, HD
        ),
        positions,
    ).astype(jnp.bfloat16)

    limit = jnp.where(
        meta_all[0] == ctx_rank, jnp.clip(my_len - meta_all[1] * BLK, 0, BLK), 0
    ).astype(jnp.int32)
    q_rows = query.transpose(1, 0, 2).reshape(heads_dev * span_size, HD)
    head_term = local_attention(
        limit, my_span.reshape(1).astype(jnp.int32), q_rows, cache_all, new_keys, new_vals, w_out
    )
    head_sum = lax.psum_scatter(head_term, "tp", scatter_dimension=1, tiled=True).astype(jnp.float32)
    mid = (resid.astype(jnp.float32) + head_sum).astype(jnp.bfloat16)
    full_mid = lax.all_gather(mid, "tp", axis=1, tiled=True)
    down_sum = lax.psum_scatter(
        feed_forward(full_mid, mlp_gain, w_gate, w_up, w_down), "tp", scatter_dimension=1, tiled=True
    ).astype(jnp.float32)
    layer_out = (mid.astype(jnp.float32) + down_sum).astype(jnp.bfloat16)
    layer_out = jnp.where(live_rows[:, None], layer_out, jnp.zeros_like(layer_out))
    return (layer_out, new_kv)


def solution(mesh):
    return jax.shard_map(
        per_device,
        mesh=mesh,
        in_specs=(
            P("ctx", "tp"),
            P(),
            P(),
            P(None, "tp"),
            P(None, "tp"),
            P("tp", None),
            P(None, "tp"),
            P(None, "tp"),
            P("tp", None),
            P("ctx", None, None),
            P(),
            P(),
            P("ctx"),
            P("ctx"),
        ),
        out_specs=(P("ctx", "tp"), P("ctx", "tp")),
        check_vma=False,
    )
```

```python
import functools

import jax
import jax.numpy as jnp
from jax import lax
from jax.sharding import PartitionSpec as P
from jax.experimental import pallas as pl
from jax.experimental.pallas import tpu as pltpu

HQ = 32
KVH = 4
HD = 128
BLK = 128


THETA = 5000000.0
EPS = 1e-05
NEG = -1e30


def rms_norm(values, gain):
    wide = values.astype(jnp.float32)
    factor = lax.rsqrt(jnp.mean(wide * wide, axis=-1, keepdims=True) + EPS)
    return (wide * factor * gain.astype(jnp.float32)).astype(jnp.bfloat16)


def rotate(vectors, positions):
    width = vectors.shape[-1]
    half = width // 2
    freqs = THETA ** (-(jnp.arange(half, dtype=jnp.float32) * 2.0 / width))
    angles = positions.astype(jnp.float32)[:, None] * freqs[None, :]
    cosine = jnp.cos(angles)[:, None, :]
    sine = jnp.sin(angles)[:, None, :]
    first = vectors[..., :half]
    second = vectors[..., half:]
    return jnp.concatenate(
        [first * cosine - second * sine, second * cosine + first * sine], axis=-1
    )


def column_term(rows, weight):
    return lax.dot_general(
        weight, rows, (((0,), (1,)), ((), ())), preferred_element_type=jnp.float32
    )


def attn_kernel(
    limit_ref, span_ref, q_ref, cache_ref, bias_ref, nk_ref, nv_ref, wo_hbm, o_ref,
    top_scr, tot_scr, acc_scr, out_scr, wo_ref, wo_sem
):
    slots = cache_ref.shape[0]
    span_size = nk_ref.shape[0]
    heads = q_ref.shape[0] // span_size
    scale = HD ** (-0.5)
    wo_copy = pltpu.make_async_copy(wo_hbm, wo_ref, wo_sem)
    wo_copy.start()
    q_all = q_ref[...]
    row_i = lax.broadcasted_iota(jnp.int32, (span_size, span_size), 0)
    col_j = lax.broadcasted_iota(jnp.int32, (span_size, span_size), 1)
    new_ok = (col_j <= row_i) & (col_j < span_ref[0])
    dims = (((1,), (1,)), ((), ()))

    def cache_raw(s):
        return lax.dot_general(q_all, cache_ref[s, :, :HD], dims, preferred_element_type=jnp.float32)

    def new_raw(h):
        rows = q_ref[h * span_size : (h + 1) * span_size, :]
        return lax.dot_general(rows, nk_ref[...], dims, preferred_element_type=jnp.float32)

    top_scr[...] = jnp.full(top_scr.shape, NEG, jnp.float32)

    def max_step(s, carry):
        lim = limit_ref[s]

        @pl.when(lim == BLK)
        def _():
            top_scr[...] = jnp.maximum(top_scr[...], cache_raw(s))

        @pl.when((lim > 0) & (lim < BLK))
        def _():
            top_scr[...] = jnp.maximum(top_scr[...], cache_raw(s) + bias_ref[pl.ds(s, 1), :])

        return carry

    lax.fori_loop(0, slots, max_step, 0)
    peaks = []
    for h in range(heads):
        part = slice(h * span_size, (h + 1) * span_size)
        raw_top = jnp.maximum(
            jnp.max(top_scr[part, :], axis=1, keepdims=True),
            jnp.max(jnp.where(new_ok, new_raw(h), NEG), axis=1, keepdims=True),
        )
        peaks.append(raw_top * scale)
    peak = jnp.concatenate(peaks, axis=0)

    tot_scr[...] = jnp.zeros(tot_scr.shape, jnp.float32)
    acc_scr[...] = jnp.zeros(acc_scr.shape, jnp.float32)

    def add_weights(s, w):
        tot_scr[...] += w
        acc_scr[...] += jnp.dot(
            w.astype(jnp.bfloat16), cache_ref[s, :, HD:], preferred_element_type=jnp.float32
        )

    def sum_step(s, carry):
        lim = limit_ref[s]

        @pl.when(lim == BLK)
        def _():
            add_weights(s, jnp.exp(cache_raw(s) * scale - peak))

        @pl.when((lim > 0) & (lim < BLK))
        def _():
            add_weights(s, jnp.exp(cache_raw(s) * scale + bias_ref[pl.ds(s, 1), :] - peak))

        return carry

    lax.fori_loop(0, slots, sum_step, 0)
    wo_copy.wait()
    for h in range(heads):
        part = slice(h * span_size, (h + 1) * span_size)
        w = jnp.where(new_ok, jnp.exp(new_raw(h) * scale - peak[part, :]), 0.0)
        total = jnp.sum(tot_scr[part, :], axis=1, keepdims=True) + jnp.sum(w, axis=1, keepdims=True)
        summed = acc_scr[part, :] + jnp.dot(
            w.astype(jnp.bfloat16), nv_ref[...], preferred_element_type=jnp.float32
        )
        head_out = (summed / total).astype(jnp.bfloat16)
        term = jnp.dot(head_out, wo_ref[h * HD : (h + 1) * HD, :], preferred_element_type=jnp.float32)
        if h == 0:
            out_scr[...] = term
        else:
            out_scr[...] += term
    o_ref[...] = out_scr[...].astype(o_ref.dtype)


def local_attention(limit, span, q_rows, cache_all, new_keys, new_vals, w_out):
    rows = q_rows.shape[0]
    span_size = new_keys.shape[0]
    width = w_out.shape[1]
    bias = jnp.where(
        jnp.arange(BLK, dtype=jnp.int32)[None, :] < limit[:, None], 0.0, NEG
    ).astype(jnp.float32)

    def whole(shape):
        return pl.BlockSpec(shape, lambda i, *_: (0,) * len(shape))

    return pl.pallas_call(
        attn_kernel,
        out_shape=jax.ShapeDtypeStruct((span_size, width), jnp.bfloat16),
        grid_spec=pltpu.PrefetchScalarGridSpec(
            num_scalar_prefetch=2,
            grid=(1,),
            in_specs=[
                whole(q_rows.shape),
                whole(cache_all.shape),
                whole(bias.shape),
                whole(new_keys.shape),
                whole(new_vals.shape),
                pl.BlockSpec(memory_space=pl.ANY),
            ],
            out_specs=whole((span_size, width)),
            scratch_shapes=[
                pltpu.VMEM((rows, BLK), jnp.float32),
                pltpu.VMEM((rows, BLK), jnp.float32),
                pltpu.VMEM((rows, HD), jnp.float32),
                pltpu.VMEM((span_size, width), jnp.float32),
                pltpu.VMEM(w_out.shape, w_out.dtype),
                pltpu.SemaphoreType.DMA(()),
            ],
        ),
    )(limit, span, q_rows, cache_all, bias, new_keys, new_vals, w_out)


def ffn_kernel(first, chunk, x_ref, gain_ref, wg_ref, wu_ref, wd_ref, o_ref, f_scr, g_acc, u_acc, h_scr):
    step = pl.program_id(0)

    @pl.when(step == 0)
    def _():
        wide = x_ref[...].astype(jnp.float32)
        f_scr[...] = lax.rsqrt(jnp.sum(wide * wide, axis=1, keepdims=True) / x_ref.shape[1] + EPS)
        g_acc[...] = jnp.zeros(g_acc.shape, jnp.float32)
        u_acc[...] = jnp.zeros(u_acc.shape, jnp.float32)

    @pl.when(step < first)
    def _():
        start = pl.multiple_of(jnp.minimum(step, first - 1) * chunk, chunk)
        part = x_ref[:, pl.ds(start, chunk)].astype(jnp.float32)
        x = (part * f_scr[...] * gain_ref[:, pl.ds(start, chunk)]).astype(jnp.bfloat16)
        dims = (((1,), (1,)), ((), ()))
        g_acc[...] += lax.dot_general(x, wg_ref[...], dims, preferred_element_type=jnp.float32)
        u_acc[...] += lax.dot_general(x, wu_ref[...], dims, preferred_element_type=jnp.float32)

    @pl.when(step == first - 1)
    def _():
        g = g_acc[...]
        h_scr[...] = (g / (1.0 + jnp.exp(-g)) * u_acc[...]).astype(h_scr.dtype)

    @pl.when(step >= first)
    def _():
        o_ref[...] = jnp.dot(h_scr[...], wd_ref[...], preferred_element_type=jnp.float32).astype(
            o_ref.dtype
        )


def feed_forward(full_mid, gain, w_gate, w_up, w_down):
    rows, width = full_mid.shape
    units = w_gate.shape[1]
    chunk = 1024 if width % 1024 == 0 else width
    first = width // chunk
    outs = w_down.shape[1] // chunk
    last = first - 1
    return pl.pallas_call(
        functools.partial(ffn_kernel, first, chunk),
        out_shape=jax.ShapeDtypeStruct((rows, w_down.shape[1]), jnp.bfloat16),
        grid=(first + outs,),
        in_specs=[
            pl.BlockSpec((rows, width), lambda i: (0, 0)),
            pl.BlockSpec((1, width), lambda i: (0, 0)),
            pl.BlockSpec((units, chunk), lambda i: (0, jnp.minimum(i, last))),
            pl.BlockSpec((units, chunk), lambda i: (0, jnp.minimum(i, last))),
            pl.BlockSpec((units, chunk), lambda i: (0, jnp.maximum(i - first, 0))),
        ],
        out_specs=pl.BlockSpec((rows, chunk), lambda i: (0, jnp.maximum(i - first, 0))),
        scratch_shapes=[
            pltpu.VMEM((rows, 1), jnp.float32),
            pltpu.VMEM((rows, units), jnp.float32),
            pltpu.VMEM((rows, units), jnp.float32),
            pltpu.VMEM((rows, units), jnp.bfloat16),
        ],
        compiler_params=pltpu.CompilerParams(dimension_semantics=("arbitrary",)),
    )(full_mid, gain.astype(jnp.float32).reshape(1, width), w_gate.T, w_up.T, w_down)


def kv_routes(tp_count, kv_width):
    per_head = HD // kv_width
    heads_dev = HQ // tp_count
    needs = []
    for dev in range(tp_count):
        group = dev * heads_dev // (HQ // KVH)
        keys = [group * per_head + u for u in range(per_head)]
        vals = [KVH * per_head + group * per_head + u for u in range(per_head)]
        own_head = dev * kv_width // HD
        own = [own_head * per_head + u for u in range(per_head)] if own_head < KVH else [dev] * per_head
        needs.append(keys + vals + own)
    entries = len(needs[0])
    colours = []
    slot = [[-1] * tp_count for _ in range(entries)]
    for entry in range(entries):
        for dev in range(tp_count):
            src = needs[dev][entry]
            if src == dev:
                continue
            for index, pairs in enumerate(colours):
                if all(a != src and b != dev for a, b in pairs):
                    pairs.append((src, dev))
                    break
            else:
                index = len(colours)
                colours.append([(src, dev)])
            slot[entry][dev] = index
    selfs = [[needs[dev][entry] == dev for dev in range(tp_count)] for entry in range(entries)]
    return per_head, colours, slot, selfs


def gather_ctx(value, count):
    parts = [value]
    for shift in range(1, count):
        pairs = [(i, (i + shift) % count) for i in range(count)]
        parts.append(lax.ppermute(value, "ctx", pairs))
    return parts


def per_device(
    resid,
    attn_gain,
    mlp_gain,
    w_query,
    w_kv,
    w_out,
    w_gate,
    w_up,
    w_down,
    kv_cache,
    cache_len,
    span_len,
    slot_req,
    slot_blk,
):
    span_size = resid.shape[0]
    ctx_count = lax.axis_size("ctx")
    q_cols = w_query.shape[1]
    heads_dev = q_cols // HD
    ctx_rank = lax.axis_index("ctx")
    tp_rank = lax.axis_index("tp")
    group = tp_rank * heads_dev // (HQ // KVH)
    my_len = cache_len[ctx_rank]
    my_span = span_len[ctx_rank]
    offsets = jnp.arange(span_size, dtype=jnp.int32)
    positions = my_len + offsets
    live_rows = offsets < my_span

    own_cache = jnp.concatenate(
        [
            lax.dynamic_slice_in_dim(kv_cache, group * HD, HD, 2),
            lax.dynamic_slice_in_dim(kv_cache, KVH * HD + group * HD, HD, 2),
        ],
        axis=2,
    )
    own_meta = jnp.stack([slot_req, slot_blk])
    cache_all = jnp.concatenate(gather_ctx(own_cache, ctx_count), axis=0)
    meta_all = jnp.concatenate(gather_ctx(own_meta, ctx_count), axis=1)

    full_resid = lax.all_gather(resid, "tp", axis=1, tiled=True)
    x_norm = rms_norm(full_resid, attn_gain)
    kv_piece = jnp.dot(x_norm, w_kv, preferred_element_type=jnp.float32).astype(jnp.bfloat16)
    kv_width = kv_piece.shape[1]
    tp_count = lax.axis_size("tp")
    per_head, colours, slot, selfs = kv_routes(tp_count, kv_width)
    received = [lax.ppermute(kv_piece, "tp", pairs) for pairs in colours]
    zeros = jnp.zeros_like(kv_piece)
    blocks = []
    for entry in range(len(slot)):
        got = jnp.where(jnp.asarray(selfs[entry])[tp_rank], kv_piece, zeros)
        for index, value in enumerate(received):
            hit = jnp.asarray([slot[entry][dev] == index for dev in range(tp_count)])[tp_rank]
            got = got + jnp.where(hit, value, zeros)
        blocks.append(got)

    def head_of(parts):
        return jnp.concatenate(parts, axis=1) if len(parts) > 1 else parts[0]

    def rotated(raw):
        return (
            rotate(raw.astype(jnp.float32).reshape(span_size, 1, HD), positions)
            .astype(jnp.bfloat16)
            .reshape(span_size, HD)
        )

    new_keys = rotated(head_of(blocks[:per_head]))
    new_vals = head_of(blocks[per_head : 2 * per_head])
    own_rot = lax.dynamic_slice_in_dim(
        rotated(head_of(blocks[2 * per_head :])), (tp_rank * kv_width) % HD, kv_width, 1
    )
    mine = jnp.where(tp_rank * kv_width < KVH * HD, own_rot, kv_piece)
    new_kv = jnp.where(live_rows[:, None], mine, jnp.zeros_like(mine))
    query = rotate(
        jnp.dot(x_norm, w_query, preferred_element_type=jnp.float32).reshape(
            span_size, heads_dev, HD
        ),
        positions,
    ).astype(jnp.bfloat16)

    limit = jnp.where(
        meta_all[0] == ctx_rank, jnp.clip(my_len - meta_all[1] * BLK, 0, BLK), 0
    ).astype(jnp.int32)
    q_rows = query.transpose(1, 0, 2).reshape(heads_dev * span_size, HD)
    head_term = local_attention(
        limit, my_span.reshape(1).astype(jnp.int32), q_rows, cache_all, new_keys, new_vals, w_out
    )
    head_sum = lax.psum_scatter(head_term, "tp", scatter_dimension=1, tiled=True).astype(jnp.float32)
    mid = (resid.astype(jnp.float32) + head_sum).astype(jnp.bfloat16)
    full_mid = lax.all_gather(mid, "tp", axis=1, tiled=True)
    down_sum = lax.psum_scatter(
        feed_forward(full_mid, mlp_gain, w_gate, w_up, w_down), "tp", scatter_dimension=1, tiled=True
    ).astype(jnp.float32)
    layer_out = (mid.astype(jnp.float32) + down_sum).astype(jnp.bfloat16)
    layer_out = jnp.where(live_rows[:, None], layer_out, jnp.zeros_like(layer_out))
    return (layer_out, new_kv)


def solution(mesh):
    return jax.shard_map(
        per_device,
        mesh=mesh,
        in_specs=(
            P("ctx", "tp"),
            P(),
            P(),
            P(None, "tp"),
            P(None, "tp"),
            P("tp", None),
            P(None, "tp"),
            P(None, "tp"),
            P("tp", None),
            P("ctx", None, None),
            P(),
            P(),
            P("ctx"),
            P("ctx"),
        ),
        out_specs=(P("ctx", "tp"), P("ctx", "tp")),
        check_vma=False,
    )
```

```python
import functools

import jax
import jax.numpy as jnp
from jax import lax
from jax.sharding import PartitionSpec as P
from jax.experimental import pallas as pl
from jax.experimental.pallas import tpu as pltpu

HQ = 32
KVH = 4
HD = 128
BLK = 128


THETA = 5000000.0
EPS = 1e-05
NEG = -1e30


def rms_norm(values, gain):
    wide = values.astype(jnp.float32)
    factor = lax.rsqrt(jnp.mean(wide * wide, axis=-1, keepdims=True) + EPS)
    return (wide * factor * gain.astype(jnp.float32)).astype(jnp.bfloat16)


def rotate(vectors, positions):
    width = vectors.shape[-1]
    half = width // 2
    freqs = THETA ** (-(jnp.arange(half, dtype=jnp.float32) * 2.0 / width))
    angles = positions.astype(jnp.float32)[:, None] * freqs[None, :]
    cosine = jnp.cos(angles)[:, None, :]
    sine = jnp.sin(angles)[:, None, :]
    first = vectors[..., :half]
    second = vectors[..., half:]
    return jnp.concatenate(
        [first * cosine - second * sine, second * cosine + first * sine], axis=-1
    )


def column_term(rows, weight):
    return lax.dot_general(
        weight, rows, (((0,), (1,)), ((), ())), preferred_element_type=jnp.float32
    )


def attn_kernel(
    limit_ref, span_ref, q_ref, cache_ref, bias_ref, nk_ref, nv_ref, wo_hbm, o_ref,
    top_scr, tot_scr, acc_scr, out_scr, wo_ref, wo_sem
):
    slots = cache_ref.shape[0]
    span_size = nk_ref.shape[0]
    heads = q_ref.shape[0] // span_size
    scale = HD ** (-0.5)
    wo_copy = pltpu.make_async_copy(wo_hbm, wo_ref, wo_sem)
    wo_copy.start()
    q_all = q_ref[...]
    row_i = lax.broadcasted_iota(jnp.int32, (span_size, span_size), 0)
    col_j = lax.broadcasted_iota(jnp.int32, (span_size, span_size), 1)
    new_ok = (col_j <= row_i) & (col_j < span_ref[0])
    dims = (((1,), (1,)), ((), ()))

    def cache_raw(s):
        return lax.dot_general(q_all, cache_ref[s, :, :HD], dims, preferred_element_type=jnp.float32)

    def new_raw(h):
        rows = q_ref[h * span_size : (h + 1) * span_size, :]
        return lax.dot_general(rows, nk_ref[...], dims, preferred_element_type=jnp.float32)

    top_scr[...] = jnp.full(top_scr.shape, NEG, jnp.float32)

    def max_step(s, carry):
        lim = limit_ref[s]

        @pl.when(lim == BLK)
        def _():
            top_scr[...] = jnp.maximum(top_scr[...], cache_raw(s))

        @pl.when((lim > 0) & (lim < BLK))
        def _():
            top_scr[...] = jnp.maximum(top_scr[...], cache_raw(s) + bias_ref[pl.ds(s, 1), :])

        return carry

    lax.fori_loop(0, slots, max_step, 0)
    peaks = []
    for h in range(heads):
        part = slice(h * span_size, (h + 1) * span_size)
        raw_top = jnp.maximum(
            jnp.max(top_scr[part, :], axis=1, keepdims=True),
            jnp.max(jnp.where(new_ok, new_raw(h), NEG), axis=1, keepdims=True),
        )
        peaks.append(raw_top * scale)
    peak = jnp.concatenate(peaks, axis=0)

    tot_scr[...] = jnp.zeros(tot_scr.shape, jnp.float32)
    acc_scr[...] = jnp.zeros(acc_scr.shape, jnp.float32)

    def add_weights(s, w):
        tot_scr[...] += w
        acc_scr[...] += jnp.dot(
            w.astype(jnp.bfloat16), cache_ref[s, :, HD:], preferred_element_type=jnp.float32
        )

    def sum_step(s, carry):
        lim = limit_ref[s]

        @pl.when(lim == BLK)
        def _():
            add_weights(s, jnp.exp(cache_raw(s) * scale - peak))

        @pl.when((lim > 0) & (lim < BLK))
        def _():
            add_weights(s, jnp.exp(cache_raw(s) * scale + bias_ref[pl.ds(s, 1), :] - peak))

        return carry

    lax.fori_loop(0, slots, sum_step, 0)
    wo_copy.wait()
    for h in range(heads):
        part = slice(h * span_size, (h + 1) * span_size)
        w = jnp.where(new_ok, jnp.exp(new_raw(h) * scale - peak[part, :]), 0.0)
        total = jnp.sum(tot_scr[part, :], axis=1, keepdims=True) + jnp.sum(w, axis=1, keepdims=True)
        summed = acc_scr[part, :] + jnp.dot(
            w.astype(jnp.bfloat16), nv_ref[...], preferred_element_type=jnp.float32
        )
        head_out = (summed / total).astype(jnp.bfloat16)
        term = jnp.dot(head_out, wo_ref[h * HD : (h + 1) * HD, :], preferred_element_type=jnp.float32)
        if h == 0:
            out_scr[...] = term
        else:
            out_scr[...] += term
    o_ref[...] = out_scr[...].astype(o_ref.dtype)


def local_attention(limit, span, q_rows, cache_all, new_keys, new_vals, w_out):
    rows = q_rows.shape[0]
    span_size = new_keys.shape[0]
    width = w_out.shape[1]
    bias = jnp.where(
        jnp.arange(BLK, dtype=jnp.int32)[None, :] < limit[:, None], 0.0, NEG
    ).astype(jnp.float32)

    def whole(shape):
        return pl.BlockSpec(shape, lambda i, *_: (0,) * len(shape))

    return pl.pallas_call(
        attn_kernel,
        out_shape=jax.ShapeDtypeStruct((span_size, width), jnp.bfloat16),
        grid_spec=pltpu.PrefetchScalarGridSpec(
            num_scalar_prefetch=2,
            grid=(1,),
            in_specs=[
                whole(q_rows.shape),
                whole(cache_all.shape),
                whole(bias.shape),
                whole(new_keys.shape),
                whole(new_vals.shape),
                pl.BlockSpec(memory_space=pl.ANY),
            ],
            out_specs=whole((span_size, width)),
            scratch_shapes=[
                pltpu.VMEM((rows, BLK), jnp.float32),
                pltpu.VMEM((rows, BLK), jnp.float32),
                pltpu.VMEM((rows, HD), jnp.float32),
                pltpu.VMEM((span_size, width), jnp.float32),
                pltpu.VMEM(w_out.shape, w_out.dtype),
                pltpu.SemaphoreType.DMA(()),
            ],
        ),
    )(limit, span, q_rows, cache_all, bias, new_keys, new_vals, w_out)


def ffn_kernel(first, chunk, x_ref, gain_ref, wg_ref, wu_ref, wd_ref, o_ref, f_scr, g_acc, u_acc, h_scr):
    step = pl.program_id(0)

    @pl.when(step == 0)
    def _():
        wide = x_ref[...].astype(jnp.float32)
        f_scr[...] = lax.rsqrt(jnp.sum(wide * wide, axis=1, keepdims=True) / x_ref.shape[1] + EPS)
        g_acc[...] = jnp.zeros(g_acc.shape, jnp.float32)
        u_acc[...] = jnp.zeros(u_acc.shape, jnp.float32)

    @pl.when(step < first)
    def _():
        start = pl.multiple_of(jnp.minimum(step, first - 1) * chunk, chunk)
        part = x_ref[:, pl.ds(start, chunk)].astype(jnp.float32)
        x = (part * f_scr[...] * gain_ref[:, pl.ds(start, chunk)]).astype(jnp.bfloat16)
        dims = (((1,), (1,)), ((), ()))
        g_acc[...] += lax.dot_general(x, wg_ref[...], dims, preferred_element_type=jnp.float32)
        u_acc[...] += lax.dot_general(x, wu_ref[...], dims, preferred_element_type=jnp.float32)

    @pl.when(step == first - 1)
    def _():
        g = g_acc[...]
        h_scr[...] = (g / (1.0 + jnp.exp(-g)) * u_acc[...]).astype(h_scr.dtype)

    @pl.when(step >= first)
    def _():
        o_ref[...] = jnp.dot(h_scr[...], wd_ref[...], preferred_element_type=jnp.float32).astype(
            o_ref.dtype
        )


def feed_forward(full_mid, gain, w_gate, w_up, w_down):
    rows, width = full_mid.shape
    units = w_gate.shape[1]
    chunk = 512 if width % 512 == 0 else width
    out_chunk = 1024 if w_down.shape[1] % 1024 == 0 else w_down.shape[1]
    first = width // chunk
    outs = w_down.shape[1] // out_chunk
    last = first - 1
    return pl.pallas_call(
        functools.partial(ffn_kernel, first, chunk),
        out_shape=jax.ShapeDtypeStruct((rows, w_down.shape[1]), jnp.bfloat16),
        grid=(first + outs,),
        in_specs=[
            pl.BlockSpec((rows, width), lambda i: (0, 0)),
            pl.BlockSpec((1, width), lambda i: (0, 0)),
            pl.BlockSpec((units, chunk), lambda i: (0, jnp.minimum(i, last))),
            pl.BlockSpec((units, chunk), lambda i: (0, jnp.minimum(i, last))),
            pl.BlockSpec((units, out_chunk), lambda i: (0, jnp.maximum(i - first, 0))),
        ],
        out_specs=pl.BlockSpec((rows, out_chunk), lambda i: (0, jnp.maximum(i - first, 0))),
        scratch_shapes=[
            pltpu.VMEM((rows, 1), jnp.float32),
            pltpu.VMEM((rows, units), jnp.float32),
            pltpu.VMEM((rows, units), jnp.float32),
            pltpu.VMEM((rows, units), jnp.bfloat16),
        ],
        compiler_params=pltpu.CompilerParams(dimension_semantics=("arbitrary",)),
    )(full_mid, gain.astype(jnp.float32).reshape(1, width), w_gate.T, w_up.T, w_down)


def kv_routes(tp_count, kv_width):
    per_head = HD // kv_width
    heads_dev = HQ // tp_count
    needs = []
    for dev in range(tp_count):
        group = dev * heads_dev // (HQ // KVH)
        keys = [group * per_head + u for u in range(per_head)]
        vals = [KVH * per_head + group * per_head + u for u in range(per_head)]
        own_head = dev * kv_width // HD
        own = [own_head * per_head + u for u in range(per_head)] if own_head < KVH else [dev] * per_head
        needs.append(keys + vals + own)
    entries = len(needs[0])
    colours = []
    slot = [[-1] * tp_count for _ in range(entries)]
    for entry in range(entries):
        for dev in range(tp_count):
            src = needs[dev][entry]
            if src == dev:
                continue
            for index, pairs in enumerate(colours):
                if all(a != src and b != dev for a, b in pairs):
                    pairs.append((src, dev))
                    break
            else:
                index = len(colours)
                colours.append([(src, dev)])
            slot[entry][dev] = index
    selfs = [[needs[dev][entry] == dev for dev in range(tp_count)] for entry in range(entries)]
    return per_head, colours, slot, selfs


def gather_ctx(value, count):
    parts = [value]
    for shift in range(1, count):
        pairs = [(i, (i + shift) % count) for i in range(count)]
        parts.append(lax.ppermute(value, "ctx", pairs))
    return parts


def per_device(
    resid,
    attn_gain,
    mlp_gain,
    w_query,
    w_kv,
    w_out,
    w_gate,
    w_up,
    w_down,
    kv_cache,
    cache_len,
    span_len,
    slot_req,
    slot_blk,
):
    span_size = resid.shape[0]
    ctx_count = lax.axis_size("ctx")
    q_cols = w_query.shape[1]
    heads_dev = q_cols // HD
    ctx_rank = lax.axis_index("ctx")
    tp_rank = lax.axis_index("tp")
    group = tp_rank * heads_dev // (HQ // KVH)
    my_len = cache_len[ctx_rank]
    my_span = span_len[ctx_rank]
    offsets = jnp.arange(span_size, dtype=jnp.int32)
    positions = my_len + offsets
    live_rows = offsets < my_span

    own_cache = jnp.concatenate(
        [
            lax.dynamic_slice_in_dim(kv_cache, group * HD, HD, 2),
            lax.dynamic_slice_in_dim(kv_cache, KVH * HD + group * HD, HD, 2),
        ],
        axis=2,
    )
    own_meta = jnp.stack([slot_req, slot_blk])
    cache_all = jnp.concatenate(gather_ctx(own_cache, ctx_count), axis=0)
    meta_all = jnp.concatenate(gather_ctx(own_meta, ctx_count), axis=1)

    full_resid = lax.all_gather(resid, "tp", axis=1, tiled=True)
    x_norm = rms_norm(full_resid, attn_gain)
    kv_piece = jnp.dot(x_norm, w_kv, preferred_element_type=jnp.float32).astype(jnp.bfloat16)
    kv_width = kv_piece.shape[1]
    tp_count = lax.axis_size("tp")
    per_head, colours, slot, selfs = kv_routes(tp_count, kv_width)
    received = [lax.ppermute(kv_piece, "tp", pairs) for pairs in colours]
    zeros = jnp.zeros_like(kv_piece)
    blocks = []
    for entry in range(len(slot)):
        got = jnp.where(jnp.asarray(selfs[entry])[tp_rank], kv_piece, zeros)
        for index, value in enumerate(received):
            hit = jnp.asarray([slot[entry][dev] == index for dev in range(tp_count)])[tp_rank]
            got = got + jnp.where(hit, value, zeros)
        blocks.append(got)

    def head_of(parts):
        return jnp.concatenate(parts, axis=1) if len(parts) > 1 else parts[0]

    def rotated(raw):
        return (
            rotate(raw.astype(jnp.float32).reshape(span_size, 1, HD), positions)
            .astype(jnp.bfloat16)
            .reshape(span_size, HD)
        )

    new_keys = rotated(head_of(blocks[:per_head]))
    new_vals = head_of(blocks[per_head : 2 * per_head])
    own_rot = lax.dynamic_slice_in_dim(
        rotated(head_of(blocks[2 * per_head :])), (tp_rank * kv_width) % HD, kv_width, 1
    )
    mine = jnp.where(tp_rank * kv_width < KVH * HD, own_rot, kv_piece)
    new_kv = jnp.where(live_rows[:, None], mine, jnp.zeros_like(mine))
    query = rotate(
        jnp.dot(x_norm, w_query, preferred_element_type=jnp.float32).reshape(
            span_size, heads_dev, HD
        ),
        positions,
    ).astype(jnp.bfloat16)

    limit = jnp.where(
        meta_all[0] == ctx_rank, jnp.clip(my_len - meta_all[1] * BLK, 0, BLK), 0
    ).astype(jnp.int32)
    q_rows = query.transpose(1, 0, 2).reshape(heads_dev * span_size, HD)
    head_term = local_attention(
        limit, my_span.reshape(1).astype(jnp.int32), q_rows, cache_all, new_keys, new_vals, w_out
    )
    head_sum = lax.psum_scatter(head_term, "tp", scatter_dimension=1, tiled=True).astype(jnp.float32)
    mid = (resid.astype(jnp.float32) + head_sum).astype(jnp.bfloat16)
    full_mid = lax.all_gather(mid, "tp", axis=1, tiled=True)
    down_sum = lax.psum_scatter(
        feed_forward(full_mid, mlp_gain, w_gate, w_up, w_down), "tp", scatter_dimension=1, tiled=True
    ).astype(jnp.float32)
    layer_out = (mid.astype(jnp.float32) + down_sum).astype(jnp.bfloat16)
    layer_out = jnp.where(live_rows[:, None], layer_out, jnp.zeros_like(layer_out))
    return (layer_out, new_kv)


def solution(mesh):
    return jax.shard_map(
        per_device,
        mesh=mesh,
        in_specs=(
            P("ctx", "tp"),
            P(),
            P(),
            P(None, "tp"),
            P(None, "tp"),
            P("tp", None),
            P(None, "tp"),
            P(None, "tp"),
            P("tp", None),
            P("ctx", None, None),
            P(),
            P(),
            P("ctx"),
            P("ctx"),
        ),
        out_specs=(P("ctx", "tp"), P("ctx", "tp")),
        check_vma=False,
    )
```

```python
import functools

import jax
import jax.numpy as jnp
from jax import lax
from jax.sharding import PartitionSpec as P
from jax.experimental import pallas as pl
from jax.experimental.pallas import tpu as pltpu

HQ = 32
KVH = 4
HD = 128
BLK = 128


THETA = 5000000.0
EPS = 1e-05
NEG = -1e30


def rms_norm(values, gain):
    wide = values.astype(jnp.float32)
    factor = lax.rsqrt(jnp.mean(wide * wide, axis=-1, keepdims=True) + EPS)
    return (wide * factor * gain.astype(jnp.float32)).astype(jnp.bfloat16)


def rotate(vectors, positions):
    width = vectors.shape[-1]
    half = width // 2
    freqs = THETA ** (-(jnp.arange(half, dtype=jnp.float32) * 2.0 / width))
    angles = positions.astype(jnp.float32)[:, None] * freqs[None, :]
    cosine = jnp.cos(angles)[:, None, :]
    sine = jnp.sin(angles)[:, None, :]
    first = vectors[..., :half]
    second = vectors[..., half:]
    return jnp.concatenate(
        [first * cosine - second * sine, second * cosine + first * sine], axis=-1
    )


def column_term(rows, weight):
    return lax.dot_general(
        weight, rows, (((0,), (1,)), ((), ())), preferred_element_type=jnp.float32
    )


def attn_kernel(
    limit_ref, span_ref, q_ref, cache_ref, bias_ref, nk_ref, nv_ref, wo_hbm, o_ref,
    top_scr, tot_scr, acc_scr, out_scr, wo_ref, wo_sem
):
    slots = cache_ref.shape[0]
    span_size = nk_ref.shape[0]
    heads = q_ref.shape[0] // span_size
    scale = HD ** (-0.5)
    wo_copy = pltpu.make_async_copy(wo_hbm, wo_ref, wo_sem)
    wo_copy.start()
    q_all = q_ref[...]
    row_i = lax.broadcasted_iota(jnp.int32, (span_size, span_size), 0)
    col_j = lax.broadcasted_iota(jnp.int32, (span_size, span_size), 1)
    new_ok = (col_j <= row_i) & (col_j < span_ref[0])
    dims = (((1,), (1,)), ((), ()))

    def cache_raw(s):
        return lax.dot_general(q_all, cache_ref[s, :, :HD], dims, preferred_element_type=jnp.float32)

    def new_raw(h):
        rows = q_ref[h * span_size : (h + 1) * span_size, :]
        return lax.dot_general(rows, nk_ref[...], dims, preferred_element_type=jnp.float32)

    top_scr[...] = jnp.full(top_scr.shape, NEG, jnp.float32)

    def max_step(s, carry):
        @pl.when(limit_ref[s] > 0)
        def _():
            top_scr[...] = jnp.maximum(top_scr[...], cache_raw(s) + bias_ref[pl.ds(s, 1), :])

        return carry

    lax.fori_loop(0, slots, max_step, 0)
    peaks = []
    for h in range(heads):
        part = slice(h * span_size, (h + 1) * span_size)
        raw_top = jnp.maximum(
            jnp.max(top_scr[part, :], axis=1, keepdims=True),
            jnp.max(jnp.where(new_ok, new_raw(h), NEG), axis=1, keepdims=True),
        )
        peaks.append(raw_top * scale)
    peak = jnp.concatenate(peaks, axis=0)

    tot_scr[...] = jnp.zeros(tot_scr.shape, jnp.float32)
    acc_scr[...] = jnp.zeros(acc_scr.shape, jnp.float32)

    def sum_step(s, carry):
        @pl.when(limit_ref[s] > 0)
        def _():
            w = jnp.exp(cache_raw(s) * scale + bias_ref[pl.ds(s, 1), :] - peak)
            tot_scr[...] += w
            acc_scr[...] += jnp.dot(
                w.astype(jnp.bfloat16), cache_ref[s, :, HD:], preferred_element_type=jnp.float32
            )

        return carry

    lax.fori_loop(0, slots, sum_step, 0)
    wo_copy.wait()
    for h in range(heads):
        part = slice(h * span_size, (h + 1) * span_size)
        w = jnp.where(new_ok, jnp.exp(new_raw(h) * scale - peak[part, :]), 0.0)
        total = jnp.sum(tot_scr[part, :], axis=1, keepdims=True) + jnp.sum(w, axis=1, keepdims=True)
        summed = acc_scr[part, :] + jnp.dot(
            w.astype(jnp.bfloat16), nv_ref[...], preferred_element_type=jnp.float32
        )
        head_out = (summed / total).astype(jnp.bfloat16)
        term = jnp.dot(head_out, wo_ref[h * HD : (h + 1) * HD, :], preferred_element_type=jnp.float32)
        if h == 0:
            out_scr[...] = term
        else:
            out_scr[...] += term
    o_ref[...] = out_scr[...].astype(o_ref.dtype)


def local_attention(limit, span, q_rows, cache_all, new_keys, new_vals, w_out):
    rows = q_rows.shape[0]
    span_size = new_keys.shape[0]
    width = w_out.shape[1]
    bias = jnp.where(
        jnp.arange(BLK, dtype=jnp.int32)[None, :] < limit[:, None], 0.0, NEG
    ).astype(jnp.float32)

    def whole(shape):
        return pl.BlockSpec(shape, lambda i, *_: (0,) * len(shape))

    return pl.pallas_call(
        attn_kernel,
        out_shape=jax.ShapeDtypeStruct((span_size, width), jnp.bfloat16),
        grid_spec=pltpu.PrefetchScalarGridSpec(
            num_scalar_prefetch=2,
            grid=(1,),
            in_specs=[
                whole(q_rows.shape),
                whole(cache_all.shape),
                whole(bias.shape),
                whole(new_keys.shape),
                whole(new_vals.shape),
                pl.BlockSpec(memory_space=pl.ANY),
            ],
            out_specs=whole((span_size, width)),
            scratch_shapes=[
                pltpu.VMEM((rows, BLK), jnp.float32),
                pltpu.VMEM((rows, BLK), jnp.float32),
                pltpu.VMEM((rows, HD), jnp.float32),
                pltpu.VMEM((span_size, width), jnp.float32),
                pltpu.VMEM(w_out.shape, w_out.dtype),
                pltpu.SemaphoreType.DMA(()),
            ],
        ),
    )(limit, span, q_rows, cache_all, bias, new_keys, new_vals, w_out)


def ffn_kernel(first, chunk, x_ref, gain_ref, wg_ref, wu_ref, wd_ref, o_ref, f_scr, g_acc, u_acc, h_scr):
    step = pl.program_id(0)

    @pl.when(step == 0)
    def _():
        wide = x_ref[...].astype(jnp.float32)
        f_scr[...] = lax.rsqrt(jnp.sum(wide * wide, axis=1, keepdims=True) / x_ref.shape[1] + EPS)
        g_acc[...] = jnp.zeros(g_acc.shape, jnp.float32)
        u_acc[...] = jnp.zeros(u_acc.shape, jnp.float32)

    @pl.when(step < first)
    def _():
        start = pl.multiple_of(jnp.minimum(step, first - 1) * chunk, chunk)
        part = x_ref[:, pl.ds(start, chunk)].astype(jnp.float32)
        x = (part * f_scr[...] * gain_ref[:, pl.ds(start, chunk)]).astype(jnp.bfloat16)
        dims = (((1,), (1,)), ((), ()))
        g_acc[...] += lax.dot_general(x, wg_ref[...], dims, preferred_element_type=jnp.float32)
        u_acc[...] += lax.dot_general(x, wu_ref[...], dims, preferred_element_type=jnp.float32)

    @pl.when(step == first - 1)
    def _():
        g = g_acc[...]
        h_scr[...] = (g / (1.0 + jnp.exp(-g)) * u_acc[...]).astype(h_scr.dtype)

    @pl.when(step >= first)
    def _():
        o_ref[...] = jnp.dot(h_scr[...], wd_ref[...], preferred_element_type=jnp.float32).astype(
            o_ref.dtype
        )


def feed_forward(full_mid, gain, w_gate, w_up, w_down):
    rows, width = full_mid.shape
    units = w_gate.shape[1]
    chunk = 1024 if width % 1024 == 0 else width
    first = width // chunk
    outs = w_down.shape[1] // chunk
    last = first - 1
    return pl.pallas_call(
        functools.partial(ffn_kernel, first, chunk),
        out_shape=jax.ShapeDtypeStruct((rows, w_down.shape[1]), jnp.bfloat16),
        grid=(first + outs,),
        in_specs=[
            pl.BlockSpec((rows, width), lambda i: (0, 0)),
            pl.BlockSpec((1, width), lambda i: (0, 0)),
            pl.BlockSpec((units, chunk), lambda i: (0, jnp.minimum(i, last))),
            pl.BlockSpec((units, chunk), lambda i: (0, jnp.minimum(i, last))),
            pl.BlockSpec((units, chunk), lambda i: (0, jnp.maximum(i - first, 0))),
        ],
        out_specs=pl.BlockSpec((rows, chunk), lambda i: (0, jnp.maximum(i - first, 0))),
        scratch_shapes=[
            pltpu.VMEM((rows, 1), jnp.float32),
            pltpu.VMEM((rows, units), jnp.float32),
            pltpu.VMEM((rows, units), jnp.float32),
            pltpu.VMEM((rows, units), jnp.bfloat16),
        ],
        compiler_params=pltpu.CompilerParams(dimension_semantics=("arbitrary",)),
    )(full_mid, gain.astype(jnp.float32).reshape(1, width), w_gate.T, w_up.T, w_down)


def kv_routes(tp_count, kv_width):
    per_head = HD // kv_width
    heads_dev = HQ // tp_count
    needs = []
    for dev in range(tp_count):
        group = dev * heads_dev // (HQ // KVH)
        keys = [group * per_head + u for u in range(per_head)]
        vals = [KVH * per_head + group * per_head + u for u in range(per_head)]
        own_head = dev * kv_width // HD
        own = [own_head * per_head + u for u in range(per_head)] if own_head < KVH else [dev] * per_head
        needs.append(keys + vals + own)
    entries = len(needs[0])
    colours = []
    slot = [[-1] * tp_count for _ in range(entries)]
    for entry in range(entries):
        for dev in range(tp_count):
            src = needs[dev][entry]
            if src == dev:
                continue
            for index, pairs in enumerate(colours):
                if all(a != src and b != dev for a, b in pairs):
                    pairs.append((src, dev))
                    break
            else:
                index = len(colours)
                colours.append([(src, dev)])
            slot[entry][dev] = index
    selfs = [[needs[dev][entry] == dev for dev in range(tp_count)] for entry in range(entries)]
    return per_head, colours, slot, selfs


def gather_ctx(value, count):
    parts = [value]
    for shift in range(1, count):
        pairs = [(i, (i + shift) % count) for i in range(count)]
        parts.append(lax.ppermute(value, "ctx", pairs))
    return parts


def per_device(
    resid,
    attn_gain,
    mlp_gain,
    w_query,
    w_kv,
    w_out,
    w_gate,
    w_up,
    w_down,
    kv_cache,
    cache_len,
    span_len,
    slot_req,
    slot_blk,
):
    span_size = resid.shape[0]
    ctx_count = lax.axis_size("ctx")
    q_cols = w_query.shape[1]
    heads_dev = q_cols // HD
    ctx_rank = lax.axis_index("ctx")
    tp_rank = lax.axis_index("tp")
    group = tp_rank * heads_dev // (HQ // KVH)
    my_len = cache_len[ctx_rank]
    my_span = span_len[ctx_rank]
    offsets = jnp.arange(span_size, dtype=jnp.int32)
    positions = my_len + offsets
    live_rows = offsets < my_span

    own_cache = jnp.concatenate(
        [
            lax.dynamic_slice_in_dim(kv_cache, group * HD, HD, 2),
            lax.dynamic_slice_in_dim(kv_cache, KVH * HD + group * HD, HD, 2),
        ],
        axis=2,
    )
    own_meta = jnp.stack([slot_req, slot_blk])
    cache_all = jnp.concatenate(gather_ctx(own_cache, ctx_count), axis=0)
    meta_all = jnp.concatenate(gather_ctx(own_meta, ctx_count), axis=1)

    full_resid = lax.all_gather(resid, "tp", axis=1, tiled=True)
    x_norm = rms_norm(full_resid, attn_gain)
    kv_piece = jnp.dot(x_norm, w_kv, preferred_element_type=jnp.float32).astype(jnp.bfloat16)
    kv_width = kv_piece.shape[1]
    tp_count = lax.axis_size("tp")
    per_head, colours, slot, selfs = kv_routes(tp_count, kv_width)
    stacked = jnp.stack([kv_piece] + [lax.ppermute(kv_piece, "tp", pairs) for pairs in colours])
    blocks = []
    for entry in range(len(slot)):
        pick = jnp.asarray([0 if selfs[entry][dev] else 1 + slot[entry][dev] for dev in range(tp_count)])
        blocks.append(lax.dynamic_index_in_dim(stacked, pick[tp_rank], 0, keepdims=False))

    def head_of(parts):
        return jnp.concatenate(parts, axis=1) if len(parts) > 1 else parts[0]

    def rotated(raw):
        return (
            rotate(raw.astype(jnp.float32).reshape(span_size, 1, HD), positions)
            .astype(jnp.bfloat16)
            .reshape(span_size, HD)
        )

    new_keys = rotated(head_of(blocks[:per_head]))
    new_vals = head_of(blocks[per_head : 2 * per_head])
    own_rot = lax.dynamic_slice_in_dim(
        rotated(head_of(blocks[2 * per_head :])), (tp_rank * kv_width) % HD, kv_width, 1
    )
    mine = jnp.where(tp_rank * kv_width < KVH * HD, own_rot, kv_piece)
    new_kv = jnp.where(live_rows[:, None], mine, jnp.zeros_like(mine))
    query = rotate(
        jnp.dot(x_norm, w_query, preferred_element_type=jnp.float32).reshape(
            span_size, heads_dev, HD
        ),
        positions,
    ).astype(jnp.bfloat16)

    limit = jnp.where(
        meta_all[0] == ctx_rank, jnp.clip(my_len - meta_all[1] * BLK, 0, BLK), 0
    ).astype(jnp.int32)
    q_rows = query.transpose(1, 0, 2).reshape(heads_dev * span_size, HD)
    head_term = local_attention(
        limit, my_span.reshape(1).astype(jnp.int32), q_rows, cache_all, new_keys, new_vals, w_out
    )
    head_sum = lax.psum_scatter(head_term, "tp", scatter_dimension=1, tiled=True).astype(jnp.float32)
    mid = (resid.astype(jnp.float32) + head_sum).astype(jnp.bfloat16)
    full_mid = lax.all_gather(mid, "tp", axis=1, tiled=True)
    down_sum = lax.psum_scatter(
        feed_forward(full_mid, mlp_gain, w_gate, w_up, w_down), "tp", scatter_dimension=1, tiled=True
    ).astype(jnp.float32)
    layer_out = (mid.astype(jnp.float32) + down_sum).astype(jnp.bfloat16)
    layer_out = jnp.where(live_rows[:, None], layer_out, jnp.zeros_like(layer_out))
    return (layer_out, new_kv)


def solution(mesh):
    return jax.shard_map(
        per_device,
        mesh=mesh,
        in_specs=(
            P("ctx", "tp"),
            P(),
            P(),
            P(None, "tp"),
            P(None, "tp"),
            P("tp", None),
            P(None, "tp"),
            P(None, "tp"),
            P("tp", None),
            P("ctx", None, None),
            P(),
            P(),
            P("ctx"),
            P("ctx"),
        ),
        out_specs=(P("ctx", "tp"), P("ctx", "tp")),
        check_vma=False,
    )
```

```python
import functools

import jax
import jax.numpy as jnp
from jax import lax
from jax.sharding import PartitionSpec as P
from jax.experimental import pallas as pl
from jax.experimental.pallas import tpu as pltpu

HQ = 32
KVH = 4
HD = 128
BLK = 128


THETA = 5000000.0
EPS = 1e-05
NEG = -1e30


def rms_norm(values, gain):
    wide = values.astype(jnp.float32)
    factor = lax.rsqrt(jnp.mean(wide * wide, axis=-1, keepdims=True) + EPS)
    return (wide * factor * gain.astype(jnp.float32)).astype(jnp.bfloat16)


def rotate(vectors, positions):
    width = vectors.shape[-1]
    half = width // 2
    freqs = THETA ** (-(jnp.arange(half, dtype=jnp.float32) * 2.0 / width))
    angles = positions.astype(jnp.float32)[:, None] * freqs[None, :]
    cosine = jnp.cos(angles)[:, None, :]
    sine = jnp.sin(angles)[:, None, :]
    first = vectors[..., :half]
    second = vectors[..., half:]
    return jnp.concatenate(
        [first * cosine - second * sine, second * cosine + first * sine], axis=-1
    )


def column_term(rows, weight):
    return lax.dot_general(
        weight, rows, (((0,), (1,)), ((), ())), preferred_element_type=jnp.float32
    )


def attn_kernel(
    limit_ref, span_ref, q_ref, cache_ref, bias_ref, nk_ref, nv_ref, wo_hbm, o_ref,
    top_scr, tot_scr, acc_scr, out_scr, wo_ref, wo_sem
):
    slots = cache_ref.shape[0]
    span_size = nk_ref.shape[0]
    heads = q_ref.shape[0] // span_size
    scale = HD ** (-0.5)
    wo_copy = pltpu.make_async_copy(wo_hbm, wo_ref, wo_sem)
    wo_copy.start()
    q_all = q_ref[...]
    row_i = lax.broadcasted_iota(jnp.int32, (span_size, span_size), 0)
    col_j = lax.broadcasted_iota(jnp.int32, (span_size, span_size), 1)
    new_ok = (col_j <= row_i) & (col_j < span_ref[0])
    dims = (((1,), (1,)), ((), ()))

    def cache_raw(s):
        return lax.dot_general(q_all, cache_ref[s, :, :HD], dims, preferred_element_type=jnp.float32)

    def new_raw(h):
        rows = q_ref[h * span_size : (h + 1) * span_size, :]
        return lax.dot_general(rows, nk_ref[...], dims, preferred_element_type=jnp.float32)

    top_scr[...] = jnp.full(top_scr.shape, NEG, jnp.float32)

    def max_step(s, carry):
        @pl.when(limit_ref[s] > 0)
        def _():
            top_scr[...] = jnp.maximum(top_scr[...], cache_raw(s) + bias_ref[pl.ds(s, 1), :])

        return carry

    lax.fori_loop(0, slots, max_step, 0)
    peaks = []
    for h in range(heads):
        part = slice(h * span_size, (h + 1) * span_size)
        raw_top = jnp.maximum(
            jnp.max(top_scr[part, :], axis=1, keepdims=True),
            jnp.max(jnp.where(new_ok, new_raw(h), NEG), axis=1, keepdims=True),
        )
        peaks.append(raw_top * scale)
    peak = jnp.concatenate(peaks, axis=0)

    tot_scr[...] = jnp.zeros(tot_scr.shape, jnp.float32)
    acc_scr[...] = jnp.zeros(acc_scr.shape, jnp.float32)

    def sum_step(s, carry):
        @pl.when(limit_ref[s] > 0)
        def _():
            w = jnp.exp(cache_raw(s) * scale + bias_ref[pl.ds(s, 1), :] - peak)
            tot_scr[...] += w
            acc_scr[...] += jnp.dot(
                w.astype(jnp.bfloat16), cache_ref[s, :, HD:], preferred_element_type=jnp.float32
            )

        return carry

    lax.fori_loop(0, slots, sum_step, 0)
    wo_copy.wait()
    for h in range(heads):
        part = slice(h * span_size, (h + 1) * span_size)
        w = jnp.where(new_ok, jnp.exp(new_raw(h) * scale - peak[part, :]), 0.0)
        total = jnp.sum(tot_scr[part, :], axis=1, keepdims=True) + jnp.sum(w, axis=1, keepdims=True)
        summed = acc_scr[part, :] + jnp.dot(
            w.astype(jnp.bfloat16), nv_ref[...], preferred_element_type=jnp.float32
        )
        out_scr[:, h * HD : (h + 1) * HD] = (summed / total).astype(out_scr.dtype)
    o_ref[...] = jnp.dot(out_scr[...], wo_ref[...], preferred_element_type=jnp.float32).astype(o_ref.dtype)


def local_attention(limit, span, q_rows, cache_all, new_keys, new_vals, w_out):
    rows = q_rows.shape[0]
    span_size = new_keys.shape[0]
    width = w_out.shape[1]
    bias = jnp.where(
        jnp.arange(BLK, dtype=jnp.int32)[None, :] < limit[:, None], 0.0, NEG
    ).astype(jnp.float32)

    def whole(shape):
        return pl.BlockSpec(shape, lambda i, *_: (0,) * len(shape))

    return pl.pallas_call(
        attn_kernel,
        out_shape=jax.ShapeDtypeStruct((span_size, width), jnp.bfloat16),
        grid_spec=pltpu.PrefetchScalarGridSpec(
            num_scalar_prefetch=2,
            grid=(1,),
            in_specs=[
                whole(q_rows.shape),
                whole(cache_all.shape),
                whole(bias.shape),
                whole(new_keys.shape),
                whole(new_vals.shape),
                pl.BlockSpec(memory_space=pl.ANY),
            ],
            out_specs=whole((span_size, width)),
            scratch_shapes=[
                pltpu.VMEM((rows, BLK), jnp.float32),
                pltpu.VMEM((rows, BLK), jnp.float32),
                pltpu.VMEM((rows, HD), jnp.float32),
                pltpu.VMEM((span_size, w_out.shape[0]), jnp.bfloat16),
                pltpu.VMEM(w_out.shape, w_out.dtype),
                pltpu.SemaphoreType.DMA(()),
            ],
        ),
    )(limit, span, q_rows, cache_all, bias, new_keys, new_vals, w_out)


def ffn_kernel(first, chunk, x_ref, gain_ref, wg_ref, wu_ref, wd_ref, o_ref, f_scr, g_acc, u_acc, h_scr):
    step = pl.program_id(0)

    @pl.when(step == 0)
    def _():
        wide = x_ref[...].astype(jnp.float32)
        f_scr[...] = lax.rsqrt(jnp.sum(wide * wide, axis=1, keepdims=True) / x_ref.shape[1] + EPS)
        g_acc[...] = jnp.zeros(g_acc.shape, jnp.float32)
        u_acc[...] = jnp.zeros(u_acc.shape, jnp.float32)

    @pl.when(step < first)
    def _():
        start = pl.multiple_of(jnp.minimum(step, first - 1) * chunk, chunk)
        part = x_ref[:, pl.ds(start, chunk)].astype(jnp.float32)
        x = (part * f_scr[...] * gain_ref[:, pl.ds(start, chunk)]).astype(jnp.bfloat16)
        dims = (((1,), (1,)), ((), ()))
        g_acc[...] += lax.dot_general(x, wg_ref[...], dims, preferred_element_type=jnp.float32)
        u_acc[...] += lax.dot_general(x, wu_ref[...], dims, preferred_element_type=jnp.float32)

    @pl.when(step == first - 1)
    def _():
        g = g_acc[...]
        h_scr[...] = (g / (1.0 + jnp.exp(-g)) * u_acc[...]).astype(h_scr.dtype)

    @pl.when(step >= first)
    def _():
        o_ref[...] = jnp.dot(h_scr[...], wd_ref[...], preferred_element_type=jnp.float32).astype(
            o_ref.dtype
        )


def feed_forward(full_mid, gain, w_gate, w_up, w_down):
    rows, width = full_mid.shape
    units = w_gate.shape[1]
    chunk = 1024 if width % 1024 == 0 else width
    first = width // chunk
    outs = w_down.shape[1] // chunk
    last = first - 1
    return pl.pallas_call(
        functools.partial(ffn_kernel, first, chunk),
        out_shape=jax.ShapeDtypeStruct((rows, w_down.shape[1]), jnp.bfloat16),
        grid=(first + outs,),
        in_specs=[
            pl.BlockSpec((rows, width), lambda i: (0, 0)),
            pl.BlockSpec((1, width), lambda i: (0, 0)),
            pl.BlockSpec((units, chunk), lambda i: (0, jnp.minimum(i, last))),
            pl.BlockSpec((units, chunk), lambda i: (0, jnp.minimum(i, last))),
            pl.BlockSpec((units, chunk), lambda i: (0, jnp.maximum(i - first, 0))),
        ],
        out_specs=pl.BlockSpec((rows, chunk), lambda i: (0, jnp.maximum(i - first, 0))),
        scratch_shapes=[
            pltpu.VMEM((rows, 1), jnp.float32),
            pltpu.VMEM((rows, units), jnp.float32),
            pltpu.VMEM((rows, units), jnp.float32),
            pltpu.VMEM((rows, units), jnp.bfloat16),
        ],
        compiler_params=pltpu.CompilerParams(dimension_semantics=("arbitrary",)),
    )(full_mid, gain.astype(jnp.float32).reshape(1, width), w_gate.T, w_up.T, w_down)


def kv_routes(tp_count, kv_width):
    per_head = HD // kv_width
    heads_dev = HQ // tp_count
    needs = []
    for dev in range(tp_count):
        group = dev * heads_dev // (HQ // KVH)
        keys = [group * per_head + u for u in range(per_head)]
        vals = [KVH * per_head + group * per_head + u for u in range(per_head)]
        own_head = dev * kv_width // HD
        own = [own_head * per_head + u for u in range(per_head)] if own_head < KVH else [dev] * per_head
        needs.append(keys + vals + own)
    entries = len(needs[0])
    colours = []
    slot = [[-1] * tp_count for _ in range(entries)]
    for entry in range(entries):
        for dev in range(tp_count):
            src = needs[dev][entry]
            if src == dev:
                continue
            for index, pairs in enumerate(colours):
                if all(a != src and b != dev for a, b in pairs):
                    pairs.append((src, dev))
                    break
            else:
                index = len(colours)
                colours.append([(src, dev)])
            slot[entry][dev] = index
    selfs = [[needs[dev][entry] == dev for dev in range(tp_count)] for entry in range(entries)]
    return per_head, colours, slot, selfs


def gather_ctx(value, count):
    parts = [value]
    for shift in range(1, count):
        pairs = [(i, (i + shift) % count) for i in range(count)]
        parts.append(lax.ppermute(value, "ctx", pairs))
    return parts


def per_device(
    resid,
    attn_gain,
    mlp_gain,
    w_query,
    w_kv,
    w_out,
    w_gate,
    w_up,
    w_down,
    kv_cache,
    cache_len,
    span_len,
    slot_req,
    slot_blk,
):
    span_size = resid.shape[0]
    ctx_count = lax.axis_size("ctx")
    q_cols = w_query.shape[1]
    heads_dev = q_cols // HD
    ctx_rank = lax.axis_index("ctx")
    tp_rank = lax.axis_index("tp")
    group = tp_rank * heads_dev // (HQ // KVH)
    my_len = cache_len[ctx_rank]
    my_span = span_len[ctx_rank]
    offsets = jnp.arange(span_size, dtype=jnp.int32)
    positions = my_len + offsets
    live_rows = offsets < my_span

    own_cache = jnp.concatenate(
        [
            lax.dynamic_slice_in_dim(kv_cache, group * HD, HD, 2),
            lax.dynamic_slice_in_dim(kv_cache, KVH * HD + group * HD, HD, 2),
        ],
        axis=2,
    )
    own_meta = jnp.stack([slot_req, slot_blk])
    cache_all = jnp.concatenate(gather_ctx(own_cache, ctx_count), axis=0)
    meta_all = jnp.concatenate(gather_ctx(own_meta, ctx_count), axis=1)

    full_resid = lax.all_gather(resid, "tp", axis=1, tiled=True)
    x_norm = rms_norm(full_resid, attn_gain)
    kv_piece = jnp.dot(x_norm, w_kv, preferred_element_type=jnp.float32).astype(jnp.bfloat16)
    kv_width = kv_piece.shape[1]
    tp_count = lax.axis_size("tp")
    per_head, colours, slot, selfs = kv_routes(tp_count, kv_width)
    stacked = jnp.stack([kv_piece] + [lax.ppermute(kv_piece, "tp", pairs) for pairs in colours])
    blocks = []
    for entry in range(len(slot)):
        pick = jnp.asarray([0 if selfs[entry][dev] else 1 + slot[entry][dev] for dev in range(tp_count)])
        blocks.append(lax.dynamic_index_in_dim(stacked, pick[tp_rank], 0, keepdims=False))

    def head_of(parts):
        return jnp.concatenate(parts, axis=1) if len(parts) > 1 else parts[0]

    def rotated(raw):
        return (
            rotate(raw.astype(jnp.float32).reshape(span_size, 1, HD), positions)
            .astype(jnp.bfloat16)
            .reshape(span_size, HD)
        )

    new_keys = rotated(head_of(blocks[:per_head]))
    new_vals = head_of(blocks[per_head : 2 * per_head])
    own_rot = lax.dynamic_slice_in_dim(
        rotated(head_of(blocks[2 * per_head :])), (tp_rank * kv_width) % HD, kv_width, 1
    )
    mine = jnp.where(tp_rank * kv_width < KVH * HD, own_rot, kv_piece)
    new_kv = jnp.where(live_rows[:, None], mine, jnp.zeros_like(mine))
    query = rotate(
        jnp.dot(x_norm, w_query, preferred_element_type=jnp.float32).reshape(
            span_size, heads_dev, HD
        ),
        positions,
    ).astype(jnp.bfloat16)

    limit = jnp.where(
        meta_all[0] == ctx_rank, jnp.clip(my_len - meta_all[1] * BLK, 0, BLK), 0
    ).astype(jnp.int32)
    q_rows = query.transpose(1, 0, 2).reshape(heads_dev * span_size, HD)
    head_term = local_attention(
        limit, my_span.reshape(1).astype(jnp.int32), q_rows, cache_all, new_keys, new_vals, w_out
    )
    head_sum = lax.psum_scatter(head_term, "tp", scatter_dimension=1, tiled=True).astype(jnp.float32)
    mid = (resid.astype(jnp.float32) + head_sum).astype(jnp.bfloat16)
    full_mid = lax.all_gather(mid, "tp", axis=1, tiled=True)
    down_sum = lax.psum_scatter(
        feed_forward(full_mid, mlp_gain, w_gate, w_up, w_down), "tp", scatter_dimension=1, tiled=True
    ).astype(jnp.float32)
    layer_out = (mid.astype(jnp.float32) + down_sum).astype(jnp.bfloat16)
    layer_out = jnp.where(live_rows[:, None], layer_out, jnp.zeros_like(layer_out))
    return (layer_out, new_kv)


def solution(mesh):
    return jax.shard_map(
        per_device,
        mesh=mesh,
        in_specs=(
            P("ctx", "tp"),
            P(),
            P(),
            P(None, "tp"),
            P(None, "tp"),
            P("tp", None),
            P(None, "tp"),
            P(None, "tp"),
            P("tp", None),
            P("ctx", None, None),
            P(),
            P(),
            P("ctx"),
            P("ctx"),
        ),
        out_specs=(P("ctx", "tp"), P("ctx", "tp")),
        check_vma=False,
    )
```

```python
import functools

import jax
import jax.numpy as jnp
from jax import lax
from jax.sharding import PartitionSpec as P
from jax.experimental import pallas as pl
from jax.experimental.pallas import tpu as pltpu

HQ = 32
KVH = 4
HD = 128
BLK = 128


THETA = 5000000.0
EPS = 1e-05
NEG = -1e30


def rms_norm(values, gain):
    wide = values.astype(jnp.float32)
    factor = lax.rsqrt(jnp.mean(wide * wide, axis=-1, keepdims=True) + EPS)
    return (wide * factor * gain.astype(jnp.float32)).astype(jnp.bfloat16)


def rotate(vectors, positions):
    width = vectors.shape[-1]
    half = width // 2
    freqs = THETA ** (-(jnp.arange(half, dtype=jnp.float32) * 2.0 / width))
    angles = positions.astype(jnp.float32)[:, None] * freqs[None, :]
    cosine = jnp.cos(angles)[:, None, :]
    sine = jnp.sin(angles)[:, None, :]
    first = vectors[..., :half]
    second = vectors[..., half:]
    return jnp.concatenate(
        [first * cosine - second * sine, second * cosine + first * sine], axis=-1
    )


def column_term(rows, weight):
    return lax.dot_general(
        weight, rows, (((0,), (1,)), ((), ())), preferred_element_type=jnp.float32
    )


def attn_kernel(
    limit_ref, span_ref, q_ref, cache_ref, bias_ref, nk_ref, nv_ref, wo_hbm, o_ref,
    top_scr, tot_scr, acc_scr, out_scr, wo_ref, wo_sem
):
    slots = cache_ref.shape[0]
    span_size = nk_ref.shape[0]
    heads = q_ref.shape[0] // span_size
    scale = HD ** (-0.5)
    wo_copy = pltpu.make_async_copy(wo_hbm, wo_ref, wo_sem)
    wo_copy.start()
    q_all = q_ref[...]
    row_i = lax.broadcasted_iota(jnp.int32, (span_size, span_size), 0)
    col_j = lax.broadcasted_iota(jnp.int32, (span_size, span_size), 1)
    new_ok = (col_j <= row_i) & (col_j < span_ref[0])
    dims = (((1,), (1,)), ((), ()))

    def cache_raw(s):
        return lax.dot_general(q_all, cache_ref[s, :, :HD], dims, preferred_element_type=jnp.float32)

    def new_raw(h):
        rows = q_ref[h * span_size : (h + 1) * span_size, :]
        return lax.dot_general(rows, nk_ref[...], dims, preferred_element_type=jnp.float32)

    top_scr[...] = jnp.full(top_scr.shape, NEG, jnp.float32)

    def max_step(s, carry):
        @pl.when(limit_ref[s] > 0)
        def _():
            top_scr[...] = jnp.maximum(top_scr[...], cache_raw(s) + bias_ref[pl.ds(s, 1), :])

        return carry

    lax.fori_loop(0, slots, max_step, 0)
    peaks = []
    for h in range(heads):
        part = slice(h * span_size, (h + 1) * span_size)
        raw_top = jnp.maximum(
            jnp.max(top_scr[part, :], axis=1, keepdims=True),
            jnp.max(jnp.where(new_ok, new_raw(h), NEG), axis=1, keepdims=True),
        )
        peaks.append(raw_top * scale)
    peak = jnp.concatenate(peaks, axis=0)

    tot_scr[...] = jnp.zeros(tot_scr.shape, jnp.float32)
    acc_scr[...] = jnp.zeros(acc_scr.shape, jnp.float32)

    def sum_step(s, carry):
        @pl.when(limit_ref[s] > 0)
        def _():
            w = jnp.exp(cache_raw(s) * scale + bias_ref[pl.ds(s, 1), :] - peak)
            tot_scr[...] += w
            acc_scr[...] += jnp.dot(
                w.astype(jnp.bfloat16), cache_ref[s, :, HD:], preferred_element_type=jnp.float32
            )

        return carry

    lax.fori_loop(0, slots, sum_step, 0)
    wo_copy.wait()
    for h in range(heads):
        part = slice(h * span_size, (h + 1) * span_size)
        w = jnp.where(new_ok, jnp.exp(new_raw(h) * scale - peak[part, :]), 0.0)
        total = jnp.sum(tot_scr[part, :], axis=1, keepdims=True) + jnp.sum(w, axis=1, keepdims=True)
        summed = acc_scr[part, :] + jnp.dot(
            w.astype(jnp.bfloat16), nv_ref[...], preferred_element_type=jnp.float32
        )
        out_scr[:, h * HD : (h + 1) * HD] = (summed / total).astype(out_scr.dtype)
    o_ref[...] = jnp.dot(out_scr[...], wo_ref[...], preferred_element_type=jnp.float32).astype(o_ref.dtype)


def local_attention(limit, span, q_rows, cache_all, new_keys, new_vals, w_out):
    rows = q_rows.shape[0]
    span_size = new_keys.shape[0]
    width = w_out.shape[1]
    bias = jnp.where(
        jnp.arange(BLK, dtype=jnp.int32)[None, :] < limit[:, None], 0.0, NEG
    ).astype(jnp.float32)

    def whole(shape):
        return pl.BlockSpec(shape, lambda i, *_: (0,) * len(shape))

    return pl.pallas_call(
        attn_kernel,
        out_shape=jax.ShapeDtypeStruct((span_size, width), jnp.bfloat16),
        grid_spec=pltpu.PrefetchScalarGridSpec(
            num_scalar_prefetch=2,
            grid=(1,),
            in_specs=[
                whole(q_rows.shape),
                whole(cache_all.shape),
                whole(bias.shape),
                whole(new_keys.shape),
                whole(new_vals.shape),
                pl.BlockSpec(memory_space=pl.ANY),
            ],
            out_specs=whole((span_size, width)),
            scratch_shapes=[
                pltpu.VMEM((rows, BLK), jnp.float32),
                pltpu.VMEM((rows, BLK), jnp.float32),
                pltpu.VMEM((rows, HD), jnp.float32),
                pltpu.VMEM((span_size, w_out.shape[0]), jnp.bfloat16),
                pltpu.VMEM(w_out.shape, w_out.dtype),
                pltpu.SemaphoreType.DMA(()),
            ],
        ),
    )(limit, span, q_rows, cache_all, bias, new_keys, new_vals, w_out)


def ffn_kernel(first, chunk, x_ref, gain_ref, wg_ref, wu_ref, wd_ref, o_ref, f_scr, g_acc, u_acc, h_scr):
    step = pl.program_id(0)

    @pl.when(step == 0)
    def _():
        wide = x_ref[...].astype(jnp.float32)
        f_scr[...] = lax.rsqrt(jnp.sum(wide * wide, axis=1, keepdims=True) / x_ref.shape[1] + EPS)
        g_acc[...] = jnp.zeros(g_acc.shape, jnp.float32)
        u_acc[...] = jnp.zeros(u_acc.shape, jnp.float32)

    @pl.when(step < first)
    def _():
        start = pl.multiple_of(jnp.minimum(step, first - 1) * chunk, chunk)
        part = x_ref[:, pl.ds(start, chunk)].astype(jnp.float32)
        x = (part * f_scr[...] * gain_ref[:, pl.ds(start, chunk)]).astype(jnp.bfloat16)
        dims = (((1,), (1,)), ((), ()))
        g_acc[...] += lax.dot_general(x, wg_ref[...], dims, preferred_element_type=jnp.float32)
        u_acc[...] += lax.dot_general(x, wu_ref[...], dims, preferred_element_type=jnp.float32)

    @pl.when(step == first - 1)
    def _():
        g = g_acc[...]
        h_scr[...] = (g / (1.0 + jnp.exp(-g)) * u_acc[...]).astype(h_scr.dtype)

    @pl.when(step >= first)
    def _():
        o_ref[...] = jnp.dot(h_scr[...], wd_ref[...], preferred_element_type=jnp.float32).astype(
            o_ref.dtype
        )


def feed_forward(full_mid, gain, w_gate, w_up, w_down):
    rows, width = full_mid.shape
    units = w_gate.shape[1]
    chunk = 1024 if width % 1024 == 0 else width
    out_chunk = 2048 if w_down.shape[1] % 2048 == 0 else w_down.shape[1]
    first = width // chunk
    outs = w_down.shape[1] // out_chunk
    last = first - 1
    return pl.pallas_call(
        functools.partial(ffn_kernel, first, chunk),
        out_shape=jax.ShapeDtypeStruct((rows, w_down.shape[1]), jnp.bfloat16),
        grid=(first + outs,),
        in_specs=[
            pl.BlockSpec((rows, width), lambda i: (0, 0)),
            pl.BlockSpec((1, width), lambda i: (0, 0)),
            pl.BlockSpec((units, chunk), lambda i: (0, jnp.minimum(i, last))),
            pl.BlockSpec((units, chunk), lambda i: (0, jnp.minimum(i, last))),
            pl.BlockSpec((units, out_chunk), lambda i: (0, jnp.maximum(i - first, 0))),
        ],
        out_specs=pl.BlockSpec((rows, out_chunk), lambda i: (0, jnp.maximum(i - first, 0))),
        scratch_shapes=[
            pltpu.VMEM((rows, 1), jnp.float32),
            pltpu.VMEM((rows, units), jnp.float32),
            pltpu.VMEM((rows, units), jnp.float32),
            pltpu.VMEM((rows, units), jnp.bfloat16),
        ],
        compiler_params=pltpu.CompilerParams(dimension_semantics=("arbitrary",)),
    )(full_mid, gain.astype(jnp.float32).reshape(1, width), w_gate.T, w_up.T, w_down)


def kv_routes(tp_count, kv_width):
    per_head = HD // kv_width
    heads_dev = HQ // tp_count
    needs = []
    for dev in range(tp_count):
        group = dev * heads_dev // (HQ // KVH)
        keys = [group * per_head + u for u in range(per_head)]
        vals = [KVH * per_head + group * per_head + u for u in range(per_head)]
        own_head = dev * kv_width // HD
        own = [own_head * per_head + u for u in range(per_head)] if own_head < KVH else [dev] * per_head
        needs.append(keys + vals + own)
    entries = len(needs[0])
    colours = []
    slot = [[-1] * tp_count for _ in range(entries)]
    for entry in range(entries):
        for dev in range(tp_count):
            src = needs[dev][entry]
            if src == dev:
                continue
            for index, pairs in enumerate(colours):
                if all(a != src and b != dev for a, b in pairs):
                    pairs.append((src, dev))
                    break
            else:
                index = len(colours)
                colours.append([(src, dev)])
            slot[entry][dev] = index
    selfs = [[needs[dev][entry] == dev for dev in range(tp_count)] for entry in range(entries)]
    return per_head, colours, slot, selfs


def gather_ctx(value, count):
    parts = [value]
    for shift in range(1, count):
        pairs = [(i, (i + shift) % count) for i in range(count)]
        parts.append(lax.ppermute(value, "ctx", pairs))
    return parts


def per_device(
    resid,
    attn_gain,
    mlp_gain,
    w_query,
    w_kv,
    w_out,
    w_gate,
    w_up,
    w_down,
    kv_cache,
    cache_len,
    span_len,
    slot_req,
    slot_blk,
):
    span_size = resid.shape[0]
    ctx_count = lax.axis_size("ctx")
    q_cols = w_query.shape[1]
    heads_dev = q_cols // HD
    ctx_rank = lax.axis_index("ctx")
    tp_rank = lax.axis_index("tp")
    group = tp_rank * heads_dev // (HQ // KVH)
    my_len = cache_len[ctx_rank]
    my_span = span_len[ctx_rank]
    offsets = jnp.arange(span_size, dtype=jnp.int32)
    positions = my_len + offsets
    live_rows = offsets < my_span

    own_cache = jnp.concatenate(
        [
            lax.dynamic_slice_in_dim(kv_cache, group * HD, HD, 2),
            lax.dynamic_slice_in_dim(kv_cache, KVH * HD + group * HD, HD, 2),
        ],
        axis=2,
    )
    own_meta = jnp.stack([slot_req, slot_blk])
    cache_all = jnp.concatenate(gather_ctx(own_cache, ctx_count), axis=0)
    meta_all = jnp.concatenate(gather_ctx(own_meta, ctx_count), axis=1)

    full_resid = lax.all_gather(resid, "tp", axis=1, tiled=True)
    x_norm = rms_norm(full_resid, attn_gain)
    kv_piece = jnp.dot(x_norm, w_kv, preferred_element_type=jnp.float32).astype(jnp.bfloat16)
    kv_width = kv_piece.shape[1]
    tp_count = lax.axis_size("tp")
    per_head, colours, slot, selfs = kv_routes(tp_count, kv_width)
    stacked = jnp.stack([kv_piece] + [lax.ppermute(kv_piece, "tp", pairs) for pairs in colours])
    blocks = []
    for entry in range(len(slot)):
        pick = jnp.asarray([0 if selfs[entry][dev] else 1 + slot[entry][dev] for dev in range(tp_count)])
        blocks.append(lax.dynamic_index_in_dim(stacked, pick[tp_rank], 0, keepdims=False))

    def head_of(parts):
        return jnp.concatenate(parts, axis=1) if len(parts) > 1 else parts[0]

    def rotated(raw):
        return (
            rotate(raw.astype(jnp.float32).reshape(span_size, 1, HD), positions)
            .astype(jnp.bfloat16)
            .reshape(span_size, HD)
        )

    new_keys = rotated(head_of(blocks[:per_head]))
    new_vals = head_of(blocks[per_head : 2 * per_head])
    own_rot = lax.dynamic_slice_in_dim(
        rotated(head_of(blocks[2 * per_head :])), (tp_rank * kv_width) % HD, kv_width, 1
    )
    mine = jnp.where(tp_rank * kv_width < KVH * HD, own_rot, kv_piece)
    new_kv = jnp.where(live_rows[:, None], mine, jnp.zeros_like(mine))
    query = rotate(
        jnp.dot(x_norm, w_query, preferred_element_type=jnp.float32).reshape(
            span_size, heads_dev, HD
        ),
        positions,
    ).astype(jnp.bfloat16)

    limit = jnp.where(
        meta_all[0] == ctx_rank, jnp.clip(my_len - meta_all[1] * BLK, 0, BLK), 0
    ).astype(jnp.int32)
    q_rows = query.transpose(1, 0, 2).reshape(heads_dev * span_size, HD)
    head_term = local_attention(
        limit, my_span.reshape(1).astype(jnp.int32), q_rows, cache_all, new_keys, new_vals, w_out
    )
    head_sum = lax.psum_scatter(head_term, "tp", scatter_dimension=1, tiled=True).astype(jnp.float32)
    mid = (resid.astype(jnp.float32) + head_sum).astype(jnp.bfloat16)
    full_mid = lax.all_gather(mid, "tp", axis=1, tiled=True)
    down_sum = lax.psum_scatter(
        feed_forward(full_mid, mlp_gain, w_gate, w_up, w_down), "tp", scatter_dimension=1, tiled=True
    ).astype(jnp.float32)
    layer_out = (mid.astype(jnp.float32) + down_sum).astype(jnp.bfloat16)
    layer_out = jnp.where(live_rows[:, None], layer_out, jnp.zeros_like(layer_out))
    return (layer_out, new_kv)


def solution(mesh):
    return jax.shard_map(
        per_device,
        mesh=mesh,
        in_specs=(
            P("ctx", "tp"),
            P(),
            P(),
            P(None, "tp"),
            P(None, "tp"),
            P("tp", None),
            P(None, "tp"),
            P(None, "tp"),
            P("tp", None),
            P("ctx", None, None),
            P(),
            P(),
            P("ctx"),
            P("ctx"),
        ),
        out_specs=(P("ctx", "tp"), P("ctx", "tp")),
        check_vma=False,
    )
```

```python
import functools

import jax
import jax.numpy as jnp
from jax import lax
from jax.sharding import PartitionSpec as P
from jax.experimental import pallas as pl
from jax.experimental.pallas import tpu as pltpu

HQ = 32
KVH = 4
HD = 128
BLK = 128


THETA = 5000000.0
EPS = 1e-05
NEG = -1e30


def rms_norm(values, gain):
    wide = values.astype(jnp.float32)
    factor = lax.rsqrt(jnp.mean(wide * wide, axis=-1, keepdims=True) + EPS)
    return (wide * factor * gain.astype(jnp.float32)).astype(jnp.bfloat16)


def rotate(vectors, positions):
    width = vectors.shape[-1]
    half = width // 2
    freqs = THETA ** (-(jnp.arange(half, dtype=jnp.float32) * 2.0 / width))
    angles = positions.astype(jnp.float32)[:, None] * freqs[None, :]
    cosine = jnp.cos(angles)[:, None, :]
    sine = jnp.sin(angles)[:, None, :]
    first = vectors[..., :half]
    second = vectors[..., half:]
    return jnp.concatenate(
        [first * cosine - second * sine, second * cosine + first * sine], axis=-1
    )


def column_term(rows, weight):
    return lax.dot_general(
        weight, rows, (((0,), (1,)), ((), ())), preferred_element_type=jnp.float32
    )


def attn_kernel(
    limit_ref, span_ref, q_ref, cache_hbm, bias_ref, nk_ref, nv_ref, wo_hbm, o_ref,
    top_scr, tot_scr, acc_scr, out_scr, wo_ref, wo_sem, cache_ref, cache_sem
):
    slots = cache_ref.shape[0]
    span_size = nk_ref.shape[0]
    heads = q_ref.shape[0] // span_size
    scale = HD ** (-0.5)
    cache_copy = pltpu.make_async_copy(cache_hbm, cache_ref, cache_sem)
    cache_copy.start()
    wo_copy = pltpu.make_async_copy(wo_hbm, wo_ref, wo_sem)
    wo_copy.start()
    q_all = q_ref[...]
    row_i = lax.broadcasted_iota(jnp.int32, (span_size, span_size), 0)
    col_j = lax.broadcasted_iota(jnp.int32, (span_size, span_size), 1)
    new_ok = (col_j <= row_i) & (col_j < span_ref[0])
    dims = (((1,), (1,)), ((), ()))

    def cache_raw(s):
        return lax.dot_general(q_all, cache_ref[s, :, :HD], dims, preferred_element_type=jnp.float32)

    def new_raw(h):
        rows = q_ref[h * span_size : (h + 1) * span_size, :]
        return lax.dot_general(rows, nk_ref[...], dims, preferred_element_type=jnp.float32)

    new_tops = [
        jnp.max(jnp.where(new_ok, new_raw(h), NEG), axis=1, keepdims=True) for h in range(heads)
    ]
    top_scr[...] = jnp.full(top_scr.shape, NEG, jnp.float32)
    cache_copy.wait()

    def max_step(s, carry):
        @pl.when(limit_ref[s] > 0)
        def _():
            top_scr[...] = jnp.maximum(top_scr[...], cache_raw(s) + bias_ref[pl.ds(s, 1), :])

        return carry

    lax.fori_loop(0, slots, max_step, 0)
    peaks = []
    for h in range(heads):
        part = slice(h * span_size, (h + 1) * span_size)
        raw_top = jnp.maximum(jnp.max(top_scr[part, :], axis=1, keepdims=True), new_tops[h])
        peaks.append(raw_top * scale)
    peak = jnp.concatenate(peaks, axis=0)

    tot_scr[...] = jnp.zeros(tot_scr.shape, jnp.float32)
    acc_scr[...] = jnp.zeros(acc_scr.shape, jnp.float32)

    def sum_step(s, carry):
        @pl.when(limit_ref[s] > 0)
        def _():
            w = jnp.exp(cache_raw(s) * scale + bias_ref[pl.ds(s, 1), :] - peak)
            tot_scr[...] += w
            acc_scr[...] += jnp.dot(
                w.astype(jnp.bfloat16), cache_ref[s, :, HD:], preferred_element_type=jnp.float32
            )

        return carry

    lax.fori_loop(0, slots, sum_step, 0)
    wo_copy.wait()
    for h in range(heads):
        part = slice(h * span_size, (h + 1) * span_size)
        w = jnp.where(new_ok, jnp.exp(new_raw(h) * scale - peak[part, :]), 0.0)
        total = jnp.sum(tot_scr[part, :], axis=1, keepdims=True) + jnp.sum(w, axis=1, keepdims=True)
        summed = acc_scr[part, :] + jnp.dot(
            w.astype(jnp.bfloat16), nv_ref[...], preferred_element_type=jnp.float32
        )
        out_scr[:, h * HD : (h + 1) * HD] = (summed / total).astype(out_scr.dtype)
    o_ref[...] = jnp.dot(out_scr[...], wo_ref[...], preferred_element_type=jnp.float32).astype(o_ref.dtype)


def local_attention(limit, span, q_rows, cache_all, new_keys, new_vals, w_out):
    rows = q_rows.shape[0]
    span_size = new_keys.shape[0]
    width = w_out.shape[1]
    bias = jnp.where(
        jnp.arange(BLK, dtype=jnp.int32)[None, :] < limit[:, None], 0.0, NEG
    ).astype(jnp.float32)

    def whole(shape):
        return pl.BlockSpec(shape, lambda i, *_: (0,) * len(shape))

    return pl.pallas_call(
        attn_kernel,
        out_shape=jax.ShapeDtypeStruct((span_size, width), jnp.bfloat16),
        grid_spec=pltpu.PrefetchScalarGridSpec(
            num_scalar_prefetch=2,
            grid=(1,),
            in_specs=[
                whole(q_rows.shape),
                pl.BlockSpec(memory_space=pl.ANY),
                whole(bias.shape),
                whole(new_keys.shape),
                whole(new_vals.shape),
                pl.BlockSpec(memory_space=pl.ANY),
            ],
            out_specs=whole((span_size, width)),
            scratch_shapes=[
                pltpu.VMEM((rows, BLK), jnp.float32),
                pltpu.VMEM((rows, BLK), jnp.float32),
                pltpu.VMEM((rows, HD), jnp.float32),
                pltpu.VMEM((span_size, w_out.shape[0]), jnp.bfloat16),
                pltpu.VMEM(w_out.shape, w_out.dtype),
                pltpu.SemaphoreType.DMA(()),
                pltpu.VMEM(cache_all.shape, cache_all.dtype),
                pltpu.SemaphoreType.DMA(()),
            ],
        ),
    )(limit, span, q_rows, cache_all, bias, new_keys, new_vals, w_out)


def ffn_kernel(first, chunk, x_ref, gain_ref, wg_ref, wu_ref, wd_ref, o_ref, f_scr, g_acc, u_acc, h_scr):
    step = pl.program_id(0)

    @pl.when(step == 0)
    def _():
        wide = x_ref[...].astype(jnp.float32)
        f_scr[...] = lax.rsqrt(jnp.sum(wide * wide, axis=1, keepdims=True) / x_ref.shape[1] + EPS)
        g_acc[...] = jnp.zeros(g_acc.shape, jnp.float32)
        u_acc[...] = jnp.zeros(u_acc.shape, jnp.float32)

    @pl.when(step < first)
    def _():
        start = pl.multiple_of(jnp.minimum(step, first - 1) * chunk, chunk)
        part = x_ref[:, pl.ds(start, chunk)].astype(jnp.float32)
        x = (part * f_scr[...] * gain_ref[:, pl.ds(start, chunk)]).astype(jnp.bfloat16)
        dims = (((1,), (1,)), ((), ()))
        g_acc[...] += lax.dot_general(x, wg_ref[...], dims, preferred_element_type=jnp.float32)
        u_acc[...] += lax.dot_general(x, wu_ref[...], dims, preferred_element_type=jnp.float32)

    @pl.when(step == first - 1)
    def _():
        g = g_acc[...]
        h_scr[...] = (g / (1.0 + jnp.exp(-g)) * u_acc[...]).astype(h_scr.dtype)

    @pl.when(step >= first)
    def _():
        o_ref[...] = jnp.dot(h_scr[...], wd_ref[...], preferred_element_type=jnp.float32).astype(
            o_ref.dtype
        )


def feed_forward(full_mid, gain, w_gate, w_up, w_down):
    rows, width = full_mid.shape
    units = w_gate.shape[1]
    chunk = 1024 if width % 1024 == 0 else width
    out_chunk = 2048 if w_down.shape[1] % 2048 == 0 else w_down.shape[1]
    first = width // chunk
    outs = w_down.shape[1] // out_chunk
    last = first - 1
    return pl.pallas_call(
        functools.partial(ffn_kernel, first, chunk),
        out_shape=jax.ShapeDtypeStruct((rows, w_down.shape[1]), jnp.bfloat16),
        grid=(first + outs,),
        in_specs=[
            pl.BlockSpec((rows, width), lambda i: (0, 0)),
            pl.BlockSpec((1, width), lambda i: (0, 0)),
            pl.BlockSpec((units, chunk), lambda i: (0, jnp.minimum(i, last))),
            pl.BlockSpec((units, chunk), lambda i: (0, jnp.minimum(i, last))),
            pl.BlockSpec((units, out_chunk), lambda i: (0, jnp.maximum(i - first, 0))),
        ],
        out_specs=pl.BlockSpec((rows, out_chunk), lambda i: (0, jnp.maximum(i - first, 0))),
        scratch_shapes=[
            pltpu.VMEM((rows, 1), jnp.float32),
            pltpu.VMEM((rows, units), jnp.float32),
            pltpu.VMEM((rows, units), jnp.float32),
            pltpu.VMEM((rows, units), jnp.bfloat16),
        ],
        compiler_params=pltpu.CompilerParams(dimension_semantics=("arbitrary",)),
    )(full_mid, gain.astype(jnp.float32).reshape(1, width), w_gate.T, w_up.T, w_down)


def kv_routes(tp_count, kv_width):
    per_head = HD // kv_width
    heads_dev = HQ // tp_count
    needs = []
    for dev in range(tp_count):
        group = dev * heads_dev // (HQ // KVH)
        keys = [group * per_head + u for u in range(per_head)]
        vals = [KVH * per_head + group * per_head + u for u in range(per_head)]
        own_head = dev * kv_width // HD
        own = [own_head * per_head + u for u in range(per_head)] if own_head < KVH else [dev] * per_head
        needs.append(keys + vals + own)
    entries = len(needs[0])
    colours = []
    slot = [[-1] * tp_count for _ in range(entries)]
    for entry in range(entries):
        for dev in range(tp_count):
            src = needs[dev][entry]
            if src == dev:
                continue
            for index, pairs in enumerate(colours):
                if all(a != src and b != dev for a, b in pairs):
                    pairs.append((src, dev))
                    break
            else:
                index = len(colours)
                colours.append([(src, dev)])
            slot[entry][dev] = index
    selfs = [[needs[dev][entry] == dev for dev in range(tp_count)] for entry in range(entries)]
    return per_head, colours, slot, selfs


def gather_ctx(value, count):
    parts = [value]
    for shift in range(1, count):
        pairs = [(i, (i + shift) % count) for i in range(count)]
        parts.append(lax.ppermute(value, "ctx", pairs))
    return parts


def per_device(
    resid,
    attn_gain,
    mlp_gain,
    w_query,
    w_kv,
    w_out,
    w_gate,
    w_up,
    w_down,
    kv_cache,
    cache_len,
    span_len,
    slot_req,
    slot_blk,
):
    span_size = resid.shape[0]
    ctx_count = lax.axis_size("ctx")
    q_cols = w_query.shape[1]
    heads_dev = q_cols // HD
    ctx_rank = lax.axis_index("ctx")
    tp_rank = lax.axis_index("tp")
    group = tp_rank * heads_dev // (HQ // KVH)
    my_len = cache_len[ctx_rank]
    my_span = span_len[ctx_rank]
    offsets = jnp.arange(span_size, dtype=jnp.int32)
    positions = my_len + offsets
    live_rows = offsets < my_span

    own_cache = jnp.concatenate(
        [
            lax.dynamic_slice_in_dim(kv_cache, group * HD, HD, 2),
            lax.dynamic_slice_in_dim(kv_cache, KVH * HD + group * HD, HD, 2),
        ],
        axis=2,
    )
    own_meta = jnp.stack([slot_req, slot_blk])
    cache_all = jnp.concatenate(gather_ctx(own_cache, ctx_count), axis=0)
    meta_all = jnp.concatenate(gather_ctx(own_meta, ctx_count), axis=1)

    full_resid = lax.all_gather(resid, "tp", axis=1, tiled=True)
    x_norm = rms_norm(full_resid, attn_gain)
    kv_piece = jnp.dot(x_norm, w_kv, preferred_element_type=jnp.float32).astype(jnp.bfloat16)
    kv_width = kv_piece.shape[1]
    tp_count = lax.axis_size("tp")
    per_head, colours, slot, selfs = kv_routes(tp_count, kv_width)
    stacked = jnp.stack([kv_piece] + [lax.ppermute(kv_piece, "tp", pairs) for pairs in colours])
    blocks = []
    for entry in range(len(slot)):
        pick = jnp.asarray([0 if selfs[entry][dev] else 1 + slot[entry][dev] for dev in range(tp_count)])
        blocks.append(lax.dynamic_index_in_dim(stacked, pick[tp_rank], 0, keepdims=False))

    def head_of(parts):
        return jnp.concatenate(parts, axis=1) if len(parts) > 1 else parts[0]

    def rotated(raw):
        return (
            rotate(raw.astype(jnp.float32).reshape(span_size, 1, HD), positions)
            .astype(jnp.bfloat16)
            .reshape(span_size, HD)
        )

    new_keys = rotated(head_of(blocks[:per_head]))
    new_vals = head_of(blocks[per_head : 2 * per_head])
    own_rot = lax.dynamic_slice_in_dim(
        rotated(head_of(blocks[2 * per_head :])), (tp_rank * kv_width) % HD, kv_width, 1
    )
    mine = jnp.where(tp_rank * kv_width < KVH * HD, own_rot, kv_piece)
    new_kv = jnp.where(live_rows[:, None], mine, jnp.zeros_like(mine))
    query = rotate(
        jnp.dot(x_norm, w_query, preferred_element_type=jnp.float32).reshape(
            span_size, heads_dev, HD
        ),
        positions,
    ).astype(jnp.bfloat16)

    limit = jnp.where(
        meta_all[0] == ctx_rank, jnp.clip(my_len - meta_all[1] * BLK, 0, BLK), 0
    ).astype(jnp.int32)
    q_rows = query.transpose(1, 0, 2).reshape(heads_dev * span_size, HD)
    head_term = local_attention(
        limit, my_span.reshape(1).astype(jnp.int32), q_rows, cache_all, new_keys, new_vals, w_out
    )
    head_sum = lax.psum_scatter(head_term, "tp", scatter_dimension=1, tiled=True).astype(jnp.float32)
    mid = (resid.astype(jnp.float32) + head_sum).astype(jnp.bfloat16)
    full_mid = lax.all_gather(mid, "tp", axis=1, tiled=True)
    down_sum = lax.psum_scatter(
        feed_forward(full_mid, mlp_gain, w_gate, w_up, w_down), "tp", scatter_dimension=1, tiled=True
    ).astype(jnp.float32)
    layer_out = (mid.astype(jnp.float32) + down_sum).astype(jnp.bfloat16)
    layer_out = jnp.where(live_rows[:, None], layer_out, jnp.zeros_like(layer_out))
    return (layer_out, new_kv)


def solution(mesh):
    return jax.shard_map(
        per_device,
        mesh=mesh,
        in_specs=(
            P("ctx", "tp"),
            P(),
            P(),
            P(None, "tp"),
            P(None, "tp"),
            P("tp", None),
            P(None, "tp"),
            P(None, "tp"),
            P("tp", None),
            P("ctx", None, None),
            P(),
            P(),
            P("ctx"),
            P("ctx"),
        ),
        out_specs=(P("ctx", "tp"), P("ctx", "tp")),
        check_vma=False,
    )
```

```python
import functools

import jax
import jax.numpy as jnp
from jax import lax
from jax.sharding import PartitionSpec as P
from jax.experimental import pallas as pl
from jax.experimental.pallas import tpu as pltpu

HQ = 32
KVH = 4
HD = 128
BLK = 128


THETA = 5000000.0
EPS = 1e-05
NEG = -1e30


def rms_norm(values, gain):
    wide = values.astype(jnp.float32)
    factor = lax.rsqrt(jnp.mean(wide * wide, axis=-1, keepdims=True) + EPS)
    return (wide * factor * gain.astype(jnp.float32)).astype(jnp.bfloat16)


def rotate(vectors, positions):
    width = vectors.shape[-1]
    half = width // 2
    freqs = THETA ** (-(jnp.arange(half, dtype=jnp.float32) * 2.0 / width))
    angles = positions.astype(jnp.float32)[:, None] * freqs[None, :]
    cosine = jnp.cos(angles)[:, None, :]
    sine = jnp.sin(angles)[:, None, :]
    first = vectors[..., :half]
    second = vectors[..., half:]
    return jnp.concatenate(
        [first * cosine - second * sine, second * cosine + first * sine], axis=-1
    )


def column_term(rows, weight):
    return lax.dot_general(
        weight, rows, (((0,), (1,)), ((), ())), preferred_element_type=jnp.float32
    )


def attn_kernel(
    limit_ref, span_ref, q_ref, cache_ref, bias_ref, nk_ref, nv_ref, wo_hbm, o_ref,
    top_scr, tot_scr, acc_scr, out_scr, wo_ref, wo_sem
):
    slots = cache_ref.shape[0]
    span_size = nk_ref.shape[0]
    heads = q_ref.shape[0] // span_size
    scale = HD ** (-0.5)
    wo_copy = pltpu.make_async_copy(wo_hbm, wo_ref, wo_sem)
    wo_copy.start()
    q_all = q_ref[...]
    row_i = lax.broadcasted_iota(jnp.int32, (span_size, span_size), 0)
    col_j = lax.broadcasted_iota(jnp.int32, (span_size, span_size), 1)
    new_ok = (col_j <= row_i) & (col_j < span_ref[0])
    dims = (((1,), (1,)), ((), ()))

    def cache_raw(s):
        return lax.dot_general(q_all, cache_ref[s, :, :HD], dims, preferred_element_type=jnp.float32)

    def new_raw(h):
        rows = q_ref[h * span_size : (h + 1) * span_size, :]
        return lax.dot_general(rows, nk_ref[...], dims, preferred_element_type=jnp.float32)

    top_scr[...] = jnp.full(top_scr.shape, NEG, jnp.float32)

    def max_step(s, carry):
        lim = limit_ref[s]

        @pl.when(lim == BLK)
        def _():
            top_scr[...] = jnp.maximum(top_scr[...], cache_raw(s))

        @pl.when((lim > 0) & (lim < BLK))
        def _():
            top_scr[...] = jnp.maximum(top_scr[...], cache_raw(s) + bias_ref[pl.ds(s, 1), :])

        return carry

    lax.fori_loop(0, slots, max_step, 0)
    peaks = []
    for h in range(heads):
        part = slice(h * span_size, (h + 1) * span_size)
        raw_top = jnp.maximum(
            jnp.max(top_scr[part, :], axis=1, keepdims=True),
            jnp.max(jnp.where(new_ok, new_raw(h), NEG), axis=1, keepdims=True),
        )
        peaks.append(raw_top * scale)
    peak = jnp.concatenate(peaks, axis=0)

    tot_scr[...] = jnp.zeros(tot_scr.shape, jnp.float32)
    acc_scr[...] = jnp.zeros(acc_scr.shape, jnp.float32)

    def add_weights(s, w):
        tot_scr[...] += w
        acc_scr[...] += jnp.dot(
            w.astype(jnp.bfloat16), cache_ref[s, :, HD:], preferred_element_type=jnp.float32
        )

    def sum_step(s, carry):
        lim = limit_ref[s]

        @pl.when(lim == BLK)
        def _():
            add_weights(s, jnp.exp(cache_raw(s) * scale - peak))

        @pl.when((lim > 0) & (lim < BLK))
        def _():
            add_weights(s, jnp.exp(cache_raw(s) * scale + bias_ref[pl.ds(s, 1), :] - peak))

        return carry

    lax.fori_loop(0, slots, sum_step, 0)
    wo_copy.wait()
    for h in range(heads):
        part = slice(h * span_size, (h + 1) * span_size)
        w = jnp.where(new_ok, jnp.exp(new_raw(h) * scale - peak[part, :]), 0.0)
        total = jnp.sum(tot_scr[part, :], axis=1, keepdims=True) + jnp.sum(w, axis=1, keepdims=True)
        summed = acc_scr[part, :] + jnp.dot(
            w.astype(jnp.bfloat16), nv_ref[...], preferred_element_type=jnp.float32
        )
        out_scr[:, h * HD : (h + 1) * HD] = (summed / total).astype(out_scr.dtype)
    o_ref[...] = jnp.dot(out_scr[...], wo_ref[...], preferred_element_type=jnp.float32).astype(o_ref.dtype)


def local_attention(limit, span, q_rows, cache_all, new_keys, new_vals, w_out):
    rows = q_rows.shape[0]
    span_size = new_keys.shape[0]
    width = w_out.shape[1]
    bias = jnp.where(
        jnp.arange(BLK, dtype=jnp.int32)[None, :] < limit[:, None], 0.0, NEG
    ).astype(jnp.float32)

    def whole(shape):
        return pl.BlockSpec(shape, lambda i, *_: (0,) * len(shape))

    return pl.pallas_call(
        attn_kernel,
        out_shape=jax.ShapeDtypeStruct((span_size, width), jnp.bfloat16),
        grid_spec=pltpu.PrefetchScalarGridSpec(
            num_scalar_prefetch=2,
            grid=(1,),
            in_specs=[
                whole(q_rows.shape),
                whole(cache_all.shape),
                whole(bias.shape),
                whole(new_keys.shape),
                whole(new_vals.shape),
                pl.BlockSpec(memory_space=pl.ANY),
            ],
            out_specs=whole((span_size, width)),
            scratch_shapes=[
                pltpu.VMEM((rows, BLK), jnp.float32),
                pltpu.VMEM((rows, BLK), jnp.float32),
                pltpu.VMEM((rows, HD), jnp.float32),
                pltpu.VMEM((span_size, w_out.shape[0]), jnp.bfloat16),
                pltpu.VMEM(w_out.shape, w_out.dtype),
                pltpu.SemaphoreType.DMA(()),
            ],
        ),
    )(limit, span, q_rows, cache_all, bias, new_keys, new_vals, w_out)


def ffn_kernel(first, chunk, x_ref, gain_ref, wg_ref, wu_ref, wd_ref, o_ref, f_scr, g_acc, u_acc, h_scr):
    step = pl.program_id(0)

    @pl.when(step == 0)
    def _():
        wide = x_ref[...].astype(jnp.float32)
        f_scr[...] = lax.rsqrt(jnp.sum(wide * wide, axis=1, keepdims=True) / x_ref.shape[1] + EPS)
        g_acc[...] = jnp.zeros(g_acc.shape, jnp.float32)
        u_acc[...] = jnp.zeros(u_acc.shape, jnp.float32)

    @pl.when(step < first)
    def _():
        start = pl.multiple_of(jnp.minimum(step, first - 1) * chunk, chunk)
        part = x_ref[:, pl.ds(start, chunk)].astype(jnp.float32)
        x = (part * f_scr[...] * gain_ref[:, pl.ds(start, chunk)]).astype(jnp.bfloat16)
        dims = (((1,), (1,)), ((), ()))
        g_acc[...] += lax.dot_general(x, wg_ref[...], dims, preferred_element_type=jnp.float32)
        u_acc[...] += lax.dot_general(x, wu_ref[...], dims, preferred_element_type=jnp.float32)

    @pl.when(step == first - 1)
    def _():
        g = g_acc[...]
        h_scr[...] = (g / (1.0 + jnp.exp(-g)) * u_acc[...]).astype(h_scr.dtype)

    @pl.when(step >= first)
    def _():
        o_ref[...] = jnp.dot(h_scr[...], wd_ref[...], preferred_element_type=jnp.float32).astype(
            o_ref.dtype
        )


def feed_forward(full_mid, gain, w_gate, w_up, w_down):
    rows, width = full_mid.shape
    units = w_gate.shape[1]
    chunk = 1024 if width % 1024 == 0 else width
    out_chunk = 2048 if w_down.shape[1] % 2048 == 0 else w_down.shape[1]
    first = width // chunk
    outs = w_down.shape[1] // out_chunk
    last = first - 1
    return pl.pallas_call(
        functools.partial(ffn_kernel, first, chunk),
        out_shape=jax.ShapeDtypeStruct((rows, w_down.shape[1]), jnp.bfloat16),
        grid=(first + outs,),
        in_specs=[
            pl.BlockSpec((rows, width), lambda i: (0, 0)),
            pl.BlockSpec((1, width), lambda i: (0, 0)),
            pl.BlockSpec((units, chunk), lambda i: (0, jnp.minimum(i, last))),
            pl.BlockSpec((units, chunk), lambda i: (0, jnp.minimum(i, last))),
            pl.BlockSpec((units, out_chunk), lambda i: (0, jnp.maximum(i - first, 0))),
        ],
        out_specs=pl.BlockSpec((rows, out_chunk), lambda i: (0, jnp.maximum(i - first, 0))),
        scratch_shapes=[
            pltpu.VMEM((rows, 1), jnp.float32),
            pltpu.VMEM((rows, units), jnp.float32),
            pltpu.VMEM((rows, units), jnp.float32),
            pltpu.VMEM((rows, units), jnp.bfloat16),
        ],
        compiler_params=pltpu.CompilerParams(dimension_semantics=("arbitrary",)),
    )(full_mid, gain.astype(jnp.float32).reshape(1, width), w_gate.T, w_up.T, w_down)


def kv_routes(tp_count, kv_width):
    per_head = HD // kv_width
    heads_dev = HQ // tp_count
    needs = []
    for dev in range(tp_count):
        group = dev * heads_dev // (HQ // KVH)
        keys = [group * per_head + u for u in range(per_head)]
        vals = [KVH * per_head + group * per_head + u for u in range(per_head)]
        own_head = dev * kv_width // HD
        own = [own_head * per_head + u for u in range(per_head)] if own_head < KVH else [dev] * per_head
        needs.append(keys + vals + own)
    entries = len(needs[0])
    colours = []
    slot = [[-1] * tp_count for _ in range(entries)]
    for entry in range(entries):
        for dev in range(tp_count):
            src = needs[dev][entry]
            if src == dev:
                continue
            for index, pairs in enumerate(colours):
                if all(a != src and b != dev for a, b in pairs):
                    pairs.append((src, dev))
                    break
            else:
                index = len(colours)
                colours.append([(src, dev)])
            slot[entry][dev] = index
    selfs = [[needs[dev][entry] == dev for dev in range(tp_count)] for entry in range(entries)]
    return per_head, colours, slot, selfs


def gather_ctx(value, count):
    parts = [value]
    for shift in range(1, count):
        pairs = [(i, (i + shift) % count) for i in range(count)]
        parts.append(lax.ppermute(value, "ctx", pairs))
    return parts


def per_device(
    resid,
    attn_gain,
    mlp_gain,
    w_query,
    w_kv,
    w_out,
    w_gate,
    w_up,
    w_down,
    kv_cache,
    cache_len,
    span_len,
    slot_req,
    slot_blk,
):
    span_size = resid.shape[0]
    ctx_count = lax.axis_size("ctx")
    q_cols = w_query.shape[1]
    heads_dev = q_cols // HD
    ctx_rank = lax.axis_index("ctx")
    tp_rank = lax.axis_index("tp")
    group = tp_rank * heads_dev // (HQ // KVH)
    my_len = cache_len[ctx_rank]
    my_span = span_len[ctx_rank]
    offsets = jnp.arange(span_size, dtype=jnp.int32)
    positions = my_len + offsets
    live_rows = offsets < my_span

    own_cache = jnp.concatenate(
        [
            lax.dynamic_slice_in_dim(kv_cache, group * HD, HD, 2),
            lax.dynamic_slice_in_dim(kv_cache, KVH * HD + group * HD, HD, 2),
        ],
        axis=2,
    )
    own_meta = jnp.stack([slot_req, slot_blk])
    cache_all = jnp.concatenate(gather_ctx(own_cache, ctx_count), axis=0)
    meta_all = jnp.concatenate(gather_ctx(own_meta, ctx_count), axis=1)

    full_resid = lax.all_gather(resid, "tp", axis=1, tiled=True)
    x_norm = rms_norm(full_resid, attn_gain)
    kv_piece = jnp.dot(x_norm, w_kv, preferred_element_type=jnp.float32).astype(jnp.bfloat16)
    kv_width = kv_piece.shape[1]
    tp_count = lax.axis_size("tp")
    per_head, colours, slot, selfs = kv_routes(tp_count, kv_width)
    stacked = jnp.stack([kv_piece] + [lax.ppermute(kv_piece, "tp", pairs) for pairs in colours])
    blocks = []
    for entry in range(len(slot)):
        pick = jnp.asarray([0 if selfs[entry][dev] else 1 + slot[entry][dev] for dev in range(tp_count)])
        blocks.append(lax.dynamic_index_in_dim(stacked, pick[tp_rank], 0, keepdims=False))

    def head_of(parts):
        return jnp.concatenate(parts, axis=1) if len(parts) > 1 else parts[0]

    def rotated(raw):
        return (
            rotate(raw.astype(jnp.float32).reshape(span_size, 1, HD), positions)
            .astype(jnp.bfloat16)
            .reshape(span_size, HD)
        )

    new_keys = rotated(head_of(blocks[:per_head]))
    new_vals = head_of(blocks[per_head : 2 * per_head])
    own_rot = lax.dynamic_slice_in_dim(
        rotated(head_of(blocks[2 * per_head :])), (tp_rank * kv_width) % HD, kv_width, 1
    )
    mine = jnp.where(tp_rank * kv_width < KVH * HD, own_rot, kv_piece)
    new_kv = jnp.where(live_rows[:, None], mine, jnp.zeros_like(mine))
    query = rotate(
        jnp.dot(x_norm, w_query, preferred_element_type=jnp.float32).reshape(
            span_size, heads_dev, HD
        ),
        positions,
    ).astype(jnp.bfloat16)

    limit = jnp.where(
        meta_all[0] == ctx_rank, jnp.clip(my_len - meta_all[1] * BLK, 0, BLK), 0
    ).astype(jnp.int32)
    q_rows = query.transpose(1, 0, 2).reshape(heads_dev * span_size, HD)
    head_term = local_attention(
        limit, my_span.reshape(1).astype(jnp.int32), q_rows, cache_all, new_keys, new_vals, w_out
    )
    head_sum = lax.psum_scatter(head_term, "tp", scatter_dimension=1, tiled=True).astype(jnp.float32)
    mid = (resid.astype(jnp.float32) + head_sum).astype(jnp.bfloat16)
    full_mid = lax.all_gather(mid, "tp", axis=1, tiled=True)
    down_sum = lax.psum_scatter(
        feed_forward(full_mid, mlp_gain, w_gate, w_up, w_down), "tp", scatter_dimension=1, tiled=True
    ).astype(jnp.float32)
    layer_out = (mid.astype(jnp.float32) + down_sum).astype(jnp.bfloat16)
    layer_out = jnp.where(live_rows[:, None], layer_out, jnp.zeros_like(layer_out))
    return (layer_out, new_kv)


def solution(mesh):
    return jax.shard_map(
        per_device,
        mesh=mesh,
        in_specs=(
            P("ctx", "tp"),
            P(),
            P(),
            P(None, "tp"),
            P(None, "tp"),
            P("tp", None),
            P(None, "tp"),
            P(None, "tp"),
            P("tp", None),
            P("ctx", None, None),
            P(),
            P(),
            P("ctx"),
            P("ctx"),
        ),
        out_specs=(P("ctx", "tp"), P("ctx", "tp")),
        check_vma=False,
    )
```

```python
import functools

import jax
import jax.numpy as jnp
from jax import lax
from jax.sharding import PartitionSpec as P
from jax.experimental import pallas as pl
from jax.experimental.pallas import tpu as pltpu

HQ = 32
KVH = 4
HD = 128
BLK = 128


THETA = 5000000.0
EPS = 1e-05
NEG = -1e30


def rms_norm(values, gain):
    wide = values.astype(jnp.float32)
    factor = lax.rsqrt(jnp.mean(wide * wide, axis=-1, keepdims=True) + EPS)
    return (wide * factor * gain.astype(jnp.float32)).astype(jnp.bfloat16)


def rotate(vectors, positions):
    width = vectors.shape[-1]
    half = width // 2
    freqs = THETA ** (-(jnp.arange(half, dtype=jnp.float32) * 2.0 / width))
    angles = positions.astype(jnp.float32)[:, None] * freqs[None, :]
    cosine = jnp.cos(angles)[:, None, :]
    sine = jnp.sin(angles)[:, None, :]
    first = vectors[..., :half]
    second = vectors[..., half:]
    return jnp.concatenate(
        [first * cosine - second * sine, second * cosine + first * sine], axis=-1
    )


def column_term(rows, weight):
    return lax.dot_general(
        weight, rows, (((0,), (1,)), ((), ())), preferred_element_type=jnp.float32
    )


def attn_kernel(
    limit_ref, span_ref, q_ref, cache_ref, bias_ref, nk_ref, nv_ref, wo_hbm, o_ref,
    top_scr, tot_scr, acc_scr, out_scr, wo_ref, wo_sem
):
    slots = cache_ref.shape[0]
    span_size = nk_ref.shape[0]
    heads = q_ref.shape[0] // span_size
    scale = HD ** (-0.5)
    wo_copy = pltpu.make_async_copy(wo_hbm, wo_ref, wo_sem)
    wo_copy.start()
    q_all = q_ref[...]
    row_i = lax.broadcasted_iota(jnp.int32, (span_size, span_size), 0)
    col_j = lax.broadcasted_iota(jnp.int32, (span_size, span_size), 1)
    new_ok = (col_j <= row_i) & (col_j < span_ref[0])
    dims = (((1,), (1,)), ((), ()))

    def cache_raw(s):
        return lax.dot_general(q_all, cache_ref[s, :, :HD], dims, preferred_element_type=jnp.float32)

    def new_raw(h):
        rows = q_ref[h * span_size : (h + 1) * span_size, :]
        return lax.dot_general(rows, nk_ref[...], dims, preferred_element_type=jnp.float32)

    top_scr[...] = jnp.full(top_scr.shape, NEG, jnp.float32)

    def max_step(s, carry):
        lim = limit_ref[s]

        @pl.when(lim == BLK)
        def _():
            top_scr[...] = jnp.maximum(top_scr[...], cache_raw(s))

        @pl.when((lim > 0) & (lim < BLK))
        def _():
            top_scr[...] = jnp.maximum(top_scr[...], cache_raw(s) + bias_ref[pl.ds(s, 1), :])

        return carry

    lax.fori_loop(0, slots, max_step, 0)
    peaks = []
    new_sc = [new_raw(h) for h in range(heads)]
    for h in range(heads):
        part = slice(h * span_size, (h + 1) * span_size)
        raw_top = jnp.maximum(
            jnp.max(top_scr[part, :], axis=1, keepdims=True),
            jnp.max(jnp.where(new_ok, new_sc[h], NEG), axis=1, keepdims=True),
        )
        peaks.append(raw_top * scale)
    peak = jnp.concatenate(peaks, axis=0)

    tot_scr[...] = jnp.zeros(tot_scr.shape, jnp.float32)
    acc_scr[...] = jnp.zeros(acc_scr.shape, jnp.float32)

    def add_weights(s, w):
        tot_scr[...] += w
        acc_scr[...] += jnp.dot(
            w.astype(jnp.bfloat16), cache_ref[s, :, HD:], preferred_element_type=jnp.float32
        )

    def sum_step(s, carry):
        lim = limit_ref[s]

        @pl.when(lim == BLK)
        def _():
            add_weights(s, jnp.exp(cache_raw(s) * scale - peak))

        @pl.when((lim > 0) & (lim < BLK))
        def _():
            add_weights(s, jnp.exp(cache_raw(s) * scale + bias_ref[pl.ds(s, 1), :] - peak))

        return carry

    lax.fori_loop(0, slots, sum_step, 0)
    wo_copy.wait()
    for h in range(heads):
        part = slice(h * span_size, (h + 1) * span_size)
        w = jnp.where(new_ok, jnp.exp(new_sc[h] * scale - peak[part, :]), 0.0)
        total = jnp.sum(tot_scr[part, :], axis=1, keepdims=True) + jnp.sum(w, axis=1, keepdims=True)
        summed = acc_scr[part, :] + jnp.dot(
            w.astype(jnp.bfloat16), nv_ref[...], preferred_element_type=jnp.float32
        )
        out_scr[:, h * HD : (h + 1) * HD] = (summed / total).astype(out_scr.dtype)
    o_ref[...] = jnp.dot(out_scr[...], wo_ref[...], preferred_element_type=jnp.float32).astype(o_ref.dtype)


def local_attention(limit, span, q_rows, cache_all, new_keys, new_vals, w_out):
    rows = q_rows.shape[0]
    span_size = new_keys.shape[0]
    width = w_out.shape[1]
    bias = jnp.where(
        jnp.arange(BLK, dtype=jnp.int32)[None, :] < limit[:, None], 0.0, NEG
    ).astype(jnp.float32)

    def whole(shape):
        return pl.BlockSpec(shape, lambda i, *_: (0,) * len(shape))

    return pl.pallas_call(
        attn_kernel,
        out_shape=jax.ShapeDtypeStruct((span_size, width), jnp.bfloat16),
        grid_spec=pltpu.PrefetchScalarGridSpec(
            num_scalar_prefetch=2,
            grid=(1,),
            in_specs=[
                whole(q_rows.shape),
                whole(cache_all.shape),
                whole(bias.shape),
                whole(new_keys.shape),
                whole(new_vals.shape),
                pl.BlockSpec(memory_space=pl.ANY),
            ],
            out_specs=whole((span_size, width)),
            scratch_shapes=[
                pltpu.VMEM((rows, BLK), jnp.float32),
                pltpu.VMEM((rows, BLK), jnp.float32),
                pltpu.VMEM((rows, HD), jnp.float32),
                pltpu.VMEM((span_size, w_out.shape[0]), jnp.bfloat16),
                pltpu.VMEM(w_out.shape, w_out.dtype),
                pltpu.SemaphoreType.DMA(()),
            ],
        ),
    )(limit, span, q_rows, cache_all, bias, new_keys, new_vals, w_out)


def ffn_kernel(first, chunk, x_ref, gain_ref, wg_ref, wu_ref, wd_ref, o_ref, f_scr, g_acc, u_acc, h_scr):
    step = pl.program_id(0)

    @pl.when(step == 0)
    def _():
        wide = x_ref[...].astype(jnp.float32)
        f_scr[...] = lax.rsqrt(jnp.sum(wide * wide, axis=1, keepdims=True) / x_ref.shape[1] + EPS)
        g_acc[...] = jnp.zeros(g_acc.shape, jnp.float32)
        u_acc[...] = jnp.zeros(u_acc.shape, jnp.float32)

    @pl.when(step < first)
    def _():
        start = pl.multiple_of(jnp.minimum(step, first - 1) * chunk, chunk)
        part = x_ref[:, pl.ds(start, chunk)].astype(jnp.float32)
        x = (part * f_scr[...] * gain_ref[:, pl.ds(start, chunk)]).astype(jnp.bfloat16)
        dims = (((1,), (1,)), ((), ()))
        g_acc[...] += lax.dot_general(x, wg_ref[...], dims, preferred_element_type=jnp.float32)
        u_acc[...] += lax.dot_general(x, wu_ref[...], dims, preferred_element_type=jnp.float32)

    @pl.when(step == first - 1)
    def _():
        g = g_acc[...]
        h_scr[...] = (g / (1.0 + jnp.exp(-g)) * u_acc[...]).astype(h_scr.dtype)

    @pl.when(step >= first)
    def _():
        o_ref[...] = jnp.dot(h_scr[...], wd_ref[...], preferred_element_type=jnp.float32).astype(
            o_ref.dtype
        )


def feed_forward(full_mid, gain, w_gate, w_up, w_down):
    rows, width = full_mid.shape
    units = w_gate.shape[1]
    chunk = 1024 if width % 1024 == 0 else width
    out_chunk = 2048 if w_down.shape[1] % 2048 == 0 else w_down.shape[1]
    first = width // chunk
    outs = w_down.shape[1] // out_chunk
    last = first - 1
    return pl.pallas_call(
        functools.partial(ffn_kernel, first, chunk),
        out_shape=jax.ShapeDtypeStruct((rows, w_down.shape[1]), jnp.bfloat16),
        grid=(first + outs,),
        in_specs=[
            pl.BlockSpec((rows, width), lambda i: (0, 0)),
            pl.BlockSpec((1, width), lambda i: (0, 0)),
            pl.BlockSpec((units, chunk), lambda i: (0, jnp.minimum(i, last))),
            pl.BlockSpec((units, chunk), lambda i: (0, jnp.minimum(i, last))),
            pl.BlockSpec((units, out_chunk), lambda i: (0, jnp.maximum(i - first, 0))),
        ],
        out_specs=pl.BlockSpec((rows, out_chunk), lambda i: (0, jnp.maximum(i - first, 0))),
        scratch_shapes=[
            pltpu.VMEM((rows, 1), jnp.float32),
            pltpu.VMEM((rows, units), jnp.float32),
            pltpu.VMEM((rows, units), jnp.float32),
            pltpu.VMEM((rows, units), jnp.bfloat16),
        ],
        compiler_params=pltpu.CompilerParams(dimension_semantics=("arbitrary",)),
    )(full_mid, gain.astype(jnp.float32).reshape(1, width), w_gate.T, w_up.T, w_down)


def kv_routes(tp_count, kv_width):
    per_head = HD // kv_width
    heads_dev = HQ // tp_count
    needs = []
    for dev in range(tp_count):
        group = dev * heads_dev // (HQ // KVH)
        keys = [group * per_head + u for u in range(per_head)]
        vals = [KVH * per_head + group * per_head + u for u in range(per_head)]
        own_head = dev * kv_width // HD
        own = [own_head * per_head + u for u in range(per_head)] if own_head < KVH else [dev] * per_head
        needs.append(keys + vals + own)
    entries = len(needs[0])
    colours = []
    slot = [[-1] * tp_count for _ in range(entries)]
    for entry in range(entries):
        for dev in range(tp_count):
            src = needs[dev][entry]
            if src == dev:
                continue
            for index, pairs in enumerate(colours):
                if all(a != src and b != dev for a, b in pairs):
                    pairs.append((src, dev))
                    break
            else:
                index = len(colours)
                colours.append([(src, dev)])
            slot[entry][dev] = index
    selfs = [[needs[dev][entry] == dev for dev in range(tp_count)] for entry in range(entries)]
    return per_head, colours, slot, selfs


def gather_ctx(value, count):
    parts = [value]
    for shift in range(1, count):
        pairs = [(i, (i + shift) % count) for i in range(count)]
        parts.append(lax.ppermute(value, "ctx", pairs))
    return parts


def per_device(
    resid,
    attn_gain,
    mlp_gain,
    w_query,
    w_kv,
    w_out,
    w_gate,
    w_up,
    w_down,
    kv_cache,
    cache_len,
    span_len,
    slot_req,
    slot_blk,
):
    span_size = resid.shape[0]
    ctx_count = lax.axis_size("ctx")
    q_cols = w_query.shape[1]
    heads_dev = q_cols // HD
    ctx_rank = lax.axis_index("ctx")
    tp_rank = lax.axis_index("tp")
    group = tp_rank * heads_dev // (HQ // KVH)
    my_len = cache_len[ctx_rank]
    my_span = span_len[ctx_rank]
    offsets = jnp.arange(span_size, dtype=jnp.int32)
    positions = my_len + offsets
    live_rows = offsets < my_span

    own_cache = jnp.concatenate(
        [
            lax.dynamic_slice_in_dim(kv_cache, group * HD, HD, 2),
            lax.dynamic_slice_in_dim(kv_cache, KVH * HD + group * HD, HD, 2),
        ],
        axis=2,
    )
    own_meta = jnp.stack([slot_req, slot_blk])
    cache_all = jnp.concatenate(gather_ctx(own_cache, ctx_count), axis=0)
    meta_all = jnp.concatenate(gather_ctx(own_meta, ctx_count), axis=1)

    full_resid = lax.all_gather(resid, "tp", axis=1, tiled=True)
    x_norm = rms_norm(full_resid, attn_gain)
    kv_piece = jnp.dot(x_norm, w_kv, preferred_element_type=jnp.float32).astype(jnp.bfloat16)
    kv_width = kv_piece.shape[1]
    tp_count = lax.axis_size("tp")
    per_head, colours, slot, selfs = kv_routes(tp_count, kv_width)
    stacked = jnp.stack([kv_piece] + [lax.ppermute(kv_piece, "tp", pairs) for pairs in colours])
    blocks = []
    for entry in range(len(slot)):
        pick = jnp.asarray([0 if selfs[entry][dev] else 1 + slot[entry][dev] for dev in range(tp_count)])
        blocks.append(lax.dynamic_index_in_dim(stacked, pick[tp_rank], 0, keepdims=False))

    def head_of(parts):
        return jnp.concatenate(parts, axis=1) if len(parts) > 1 else parts[0]

    def rotated(raw):
        return (
            rotate(raw.astype(jnp.float32).reshape(span_size, 1, HD), positions)
            .astype(jnp.bfloat16)
            .reshape(span_size, HD)
        )

    new_keys = rotated(head_of(blocks[:per_head]))
    new_vals = head_of(blocks[per_head : 2 * per_head])
    own_rot = lax.dynamic_slice_in_dim(
        rotated(head_of(blocks[2 * per_head :])), (tp_rank * kv_width) % HD, kv_width, 1
    )
    mine = jnp.where(tp_rank * kv_width < KVH * HD, own_rot, kv_piece)
    new_kv = jnp.where(live_rows[:, None], mine, jnp.zeros_like(mine))
    query = rotate(
        jnp.dot(x_norm, w_query, preferred_element_type=jnp.float32).reshape(
            span_size, heads_dev, HD
        ),
        positions,
    ).astype(jnp.bfloat16)

    limit = jnp.where(
        meta_all[0] == ctx_rank, jnp.clip(my_len - meta_all[1] * BLK, 0, BLK), 0
    ).astype(jnp.int32)
    q_rows = query.transpose(1, 0, 2).reshape(heads_dev * span_size, HD)
    head_term = local_attention(
        limit, my_span.reshape(1).astype(jnp.int32), q_rows, cache_all, new_keys, new_vals, w_out
    )
    head_sum = lax.psum_scatter(head_term, "tp", scatter_dimension=1, tiled=True).astype(jnp.float32)
    mid = (resid.astype(jnp.float32) + head_sum).astype(jnp.bfloat16)
    full_mid = lax.all_gather(mid, "tp", axis=1, tiled=True)
    down_sum = lax.psum_scatter(
        feed_forward(full_mid, mlp_gain, w_gate, w_up, w_down), "tp", scatter_dimension=1, tiled=True
    ).astype(jnp.float32)
    layer_out = (mid.astype(jnp.float32) + down_sum).astype(jnp.bfloat16)
    layer_out = jnp.where(live_rows[:, None], layer_out, jnp.zeros_like(layer_out))
    return (layer_out, new_kv)


def solution(mesh):
    return jax.shard_map(
        per_device,
        mesh=mesh,
        in_specs=(
            P("ctx", "tp"),
            P(),
            P(),
            P(None, "tp"),
            P(None, "tp"),
            P("tp", None),
            P(None, "tp"),
            P(None, "tp"),
            P("tp", None),
            P("ctx", None, None),
            P(),
            P(),
            P("ctx"),
            P("ctx"),
        ),
        out_specs=(P("ctx", "tp"), P("ctx", "tp")),
        check_vma=False,
    )
```

```python
import functools

import jax
import jax.numpy as jnp
from jax import lax
from jax.sharding import PartitionSpec as P
from jax.experimental import pallas as pl
from jax.experimental.pallas import tpu as pltpu

HQ = 32
KVH = 4
HD = 128
BLK = 128


THETA = 5000000.0
EPS = 1e-05
NEG = -1e30


def rms_norm(values, gain):
    wide = values.astype(jnp.float32)
    factor = lax.rsqrt(jnp.mean(wide * wide, axis=-1, keepdims=True) + EPS)
    return (wide * factor * gain.astype(jnp.float32)).astype(jnp.bfloat16)


def rotate(vectors, positions):
    width = vectors.shape[-1]
    half = width // 2
    freqs = THETA ** (-(jnp.arange(half, dtype=jnp.float32) * 2.0 / width))
    angles = positions.astype(jnp.float32)[:, None] * freqs[None, :]
    cosine = jnp.cos(angles)[:, None, :]
    sine = jnp.sin(angles)[:, None, :]
    first = vectors[..., :half]
    second = vectors[..., half:]
    return jnp.concatenate(
        [first * cosine - second * sine, second * cosine + first * sine], axis=-1
    )


def column_term(rows, weight):
    return lax.dot_general(
        weight, rows, (((0,), (1,)), ((), ())), preferred_element_type=jnp.float32
    )


def attn_kernel(
    limit_ref, span_ref, q_ref, cache_ref, bias_ref, nk_ref, nv_ref, wo_hbm, o_ref,
    top_scr, tot_scr, acc_scr, out_scr, wo_ref, wo_sem
):
    slots = cache_ref.shape[0]
    span_size = nk_ref.shape[0]
    heads = q_ref.shape[0] // span_size
    scale = HD ** (-0.5)
    wo_copy = pltpu.make_async_copy(wo_hbm, wo_ref, wo_sem)
    wo_copy.start()
    q_all = q_ref[...]
    row_i = lax.broadcasted_iota(jnp.int32, (span_size, span_size), 0)
    col_j = lax.broadcasted_iota(jnp.int32, (span_size, span_size), 1)
    new_ok = (col_j <= row_i) & (col_j < span_ref[0])
    dims = (((1,), (1,)), ((), ()))

    def cache_raw(s):
        return lax.dot_general(q_all, cache_ref[s, :, :HD], dims, preferred_element_type=jnp.float32)

    def new_raw(h):
        rows = q_ref[h * span_size : (h + 1) * span_size, :]
        return lax.dot_general(rows, nk_ref[...], dims, preferred_element_type=jnp.float32)

    top_scr[...] = jnp.full(top_scr.shape, NEG, jnp.float32)

    def max_step(s, carry):
        lim = limit_ref[s]

        @pl.when(lim == BLK)
        def _():
            top_scr[...] = jnp.maximum(top_scr[...], cache_raw(s))

        @pl.when((lim > 0) & (lim < BLK))
        def _():
            top_scr[...] = jnp.maximum(top_scr[...], cache_raw(s) + bias_ref[pl.ds(s, 1), :])

        return carry

    lax.fori_loop(0, slots, max_step, 0)
    peaks = []
    new_sc = [new_raw(h) for h in range(heads)]
    for h in range(heads):
        part = slice(h * span_size, (h + 1) * span_size)
        raw_top = jnp.maximum(
            jnp.max(top_scr[part, :], axis=1, keepdims=True),
            jnp.max(jnp.where(new_ok, new_sc[h], NEG), axis=1, keepdims=True),
        )
        peaks.append(raw_top * scale)
    peak = jnp.concatenate(peaks, axis=0)

    tot_scr[...] = jnp.zeros(tot_scr.shape, jnp.float32)
    acc_scr[...] = jnp.zeros(acc_scr.shape, jnp.float32)

    def add_weights(s, w):
        tot_scr[...] += w
        acc_scr[...] += jnp.dot(
            w.astype(jnp.bfloat16), cache_ref[s, :, HD:], preferred_element_type=jnp.float32
        )

    def sum_step(s, carry):
        lim = limit_ref[s]

        @pl.when(lim == BLK)
        def _():
            add_weights(s, jnp.exp(cache_raw(s) * scale - peak))

        @pl.when((lim > 0) & (lim < BLK))
        def _():
            add_weights(s, jnp.exp(cache_raw(s) * scale + bias_ref[pl.ds(s, 1), :] - peak))

        return carry

    lax.fori_loop(0, slots, sum_step, 0)
    wo_copy.wait()
    for h in range(heads):
        part = slice(h * span_size, (h + 1) * span_size)
        w = jnp.where(new_ok, jnp.exp(new_sc[h] * scale - peak[part, :]), 0.0)
        total = jnp.sum(tot_scr[part, :], axis=1, keepdims=True) + jnp.sum(w, axis=1, keepdims=True)
        summed = acc_scr[part, :] + jnp.dot(
            w.astype(jnp.bfloat16), nv_ref[...], preferred_element_type=jnp.float32
        )
        out_scr[:, h * HD : (h + 1) * HD] = (summed / total).astype(out_scr.dtype)
    o_ref[...] = jnp.dot(out_scr[...], wo_ref[...], preferred_element_type=jnp.float32).astype(o_ref.dtype)


def local_attention(limit, span, q_rows, cache_all, new_keys, new_vals, w_out):
    rows = q_rows.shape[0]
    span_size = new_keys.shape[0]
    width = w_out.shape[1]
    bias = jnp.where(
        jnp.arange(BLK, dtype=jnp.int32)[None, :] < limit[:, None], 0.0, NEG
    ).astype(jnp.float32)

    def whole(shape):
        return pl.BlockSpec(shape, lambda i, *_: (0,) * len(shape))

    return pl.pallas_call(
        attn_kernel,
        out_shape=jax.ShapeDtypeStruct((span_size, width), jnp.bfloat16),
        grid_spec=pltpu.PrefetchScalarGridSpec(
            num_scalar_prefetch=2,
            grid=(1,),
            in_specs=[
                whole(q_rows.shape),
                whole(cache_all.shape),
                whole(bias.shape),
                whole(new_keys.shape),
                whole(new_vals.shape),
                pl.BlockSpec(memory_space=pl.ANY),
            ],
            out_specs=whole((span_size, width)),
            scratch_shapes=[
                pltpu.VMEM((rows, BLK), jnp.float32),
                pltpu.VMEM((rows, BLK), jnp.float32),
                pltpu.VMEM((rows, HD), jnp.float32),
                pltpu.VMEM((span_size, w_out.shape[0]), jnp.bfloat16),
                pltpu.VMEM(w_out.shape, w_out.dtype),
                pltpu.SemaphoreType.DMA(()),
            ],
        ),
    )(limit, span, q_rows, cache_all, bias, new_keys, new_vals, w_out)


def ffn_kernel(first, chunk, x_ref, gain_ref, wg_ref, wu_ref, wd_ref, o_ref, f_scr, g_acc, u_acc, h_scr):
    step = pl.program_id(0)

    @pl.when(step == 0)
    def _():
        wide = x_ref[...].astype(jnp.float32)
        f_scr[...] = lax.rsqrt(jnp.sum(wide * wide, axis=1, keepdims=True) / x_ref.shape[1] + EPS)
        g_acc[...] = jnp.zeros(g_acc.shape, jnp.float32)
        u_acc[...] = jnp.zeros(u_acc.shape, jnp.float32)

    @pl.when(step < first)
    def _():
        start = pl.multiple_of(jnp.minimum(step, first - 1) * chunk, chunk)
        part = x_ref[:, pl.ds(start, chunk)].astype(jnp.float32)
        x = (part * f_scr[...] * gain_ref[:, pl.ds(start, chunk)]).astype(jnp.bfloat16)
        dims = (((1,), (1,)), ((), ()))
        g_acc[...] += lax.dot_general(x, wg_ref[...], dims, preferred_element_type=jnp.float32)
        u_acc[...] += lax.dot_general(x, wu_ref[...], dims, preferred_element_type=jnp.float32)

    @pl.when(step == first - 1)
    def _():
        g = g_acc[...]
        h_scr[...] = (g / (1.0 + jnp.exp(-g)) * u_acc[...]).astype(h_scr.dtype)

    @pl.when(step >= first)
    def _():
        o_ref[...] = jnp.dot(h_scr[...], wd_ref[...], preferred_element_type=jnp.float32).astype(
            o_ref.dtype
        )


def feed_forward(full_mid, gain, w_gate, w_up, w_down):
    rows, width = full_mid.shape
    units = w_gate.shape[1]
    chunk = 2048 if width % 2048 == 0 else width
    out_chunk = 2048 if w_down.shape[1] % 2048 == 0 else w_down.shape[1]
    first = width // chunk
    outs = w_down.shape[1] // out_chunk
    last = first - 1
    return pl.pallas_call(
        functools.partial(ffn_kernel, first, chunk),
        out_shape=jax.ShapeDtypeStruct((rows, w_down.shape[1]), jnp.bfloat16),
        grid=(first + outs,),
        in_specs=[
            pl.BlockSpec((rows, width), lambda i: (0, 0)),
            pl.BlockSpec((1, width), lambda i: (0, 0)),
            pl.BlockSpec((units, chunk), lambda i: (0, jnp.minimum(i, last))),
            pl.BlockSpec((units, chunk), lambda i: (0, jnp.minimum(i, last))),
            pl.BlockSpec((units, out_chunk), lambda i: (0, jnp.maximum(i - first, 0))),
        ],
        out_specs=pl.BlockSpec((rows, out_chunk), lambda i: (0, jnp.maximum(i - first, 0))),
        scratch_shapes=[
            pltpu.VMEM((rows, 1), jnp.float32),
            pltpu.VMEM((rows, units), jnp.float32),
            pltpu.VMEM((rows, units), jnp.float32),
            pltpu.VMEM((rows, units), jnp.bfloat16),
        ],
        compiler_params=pltpu.CompilerParams(dimension_semantics=("arbitrary",)),
    )(full_mid, gain.astype(jnp.float32).reshape(1, width), w_gate.T, w_up.T, w_down)


def kv_routes(tp_count, kv_width):
    per_head = HD // kv_width
    heads_dev = HQ // tp_count
    needs = []
    for dev in range(tp_count):
        group = dev * heads_dev // (HQ // KVH)
        keys = [group * per_head + u for u in range(per_head)]
        vals = [KVH * per_head + group * per_head + u for u in range(per_head)]
        own_head = dev * kv_width // HD
        own = [own_head * per_head + u for u in range(per_head)] if own_head < KVH else [dev] * per_head
        needs.append(keys + vals + own)
    entries = len(needs[0])
    colours = []
    slot = [[-1] * tp_count for _ in range(entries)]
    for entry in range(entries):
        for dev in range(tp_count):
            src = needs[dev][entry]
            if src == dev:
                continue
            for index, pairs in enumerate(colours):
                if all(a != src and b != dev for a, b in pairs):
                    pairs.append((src, dev))
                    break
            else:
                index = len(colours)
                colours.append([(src, dev)])
            slot[entry][dev] = index
    selfs = [[needs[dev][entry] == dev for dev in range(tp_count)] for entry in range(entries)]
    return per_head, colours, slot, selfs


def gather_ctx(value, count):
    parts = [value]
    for shift in range(1, count):
        pairs = [(i, (i + shift) % count) for i in range(count)]
        parts.append(lax.ppermute(value, "ctx", pairs))
    return parts


def per_device(
    resid,
    attn_gain,
    mlp_gain,
    w_query,
    w_kv,
    w_out,
    w_gate,
    w_up,
    w_down,
    kv_cache,
    cache_len,
    span_len,
    slot_req,
    slot_blk,
):
    span_size = resid.shape[0]
    ctx_count = lax.axis_size("ctx")
    q_cols = w_query.shape[1]
    heads_dev = q_cols // HD
    ctx_rank = lax.axis_index("ctx")
    tp_rank = lax.axis_index("tp")
    group = tp_rank * heads_dev // (HQ // KVH)
    my_len = cache_len[ctx_rank]
    my_span = span_len[ctx_rank]
    offsets = jnp.arange(span_size, dtype=jnp.int32)
    positions = my_len + offsets
    live_rows = offsets < my_span

    own_cache = jnp.concatenate(
        [
            lax.dynamic_slice_in_dim(kv_cache, group * HD, HD, 2),
            lax.dynamic_slice_in_dim(kv_cache, KVH * HD + group * HD, HD, 2),
        ],
        axis=2,
    )
    own_meta = jnp.stack([slot_req, slot_blk])
    cache_all = jnp.concatenate(gather_ctx(own_cache, ctx_count), axis=0)
    meta_all = jnp.concatenate(gather_ctx(own_meta, ctx_count), axis=1)

    full_resid = lax.all_gather(resid, "tp", axis=1, tiled=True)
    x_norm = rms_norm(full_resid, attn_gain)
    kv_piece = jnp.dot(x_norm, w_kv, preferred_element_type=jnp.float32).astype(jnp.bfloat16)
    kv_width = kv_piece.shape[1]
    tp_count = lax.axis_size("tp")
    per_head, colours, slot, selfs = kv_routes(tp_count, kv_width)
    stacked = jnp.stack([kv_piece] + [lax.ppermute(kv_piece, "tp", pairs) for pairs in colours])
    blocks = []
    for entry in range(len(slot)):
        pick = jnp.asarray([0 if selfs[entry][dev] else 1 + slot[entry][dev] for dev in range(tp_count)])
        blocks.append(lax.dynamic_index_in_dim(stacked, pick[tp_rank], 0, keepdims=False))

    def head_of(parts):
        return jnp.concatenate(parts, axis=1) if len(parts) > 1 else parts[0]

    def rotated(raw):
        return (
            rotate(raw.astype(jnp.float32).reshape(span_size, 1, HD), positions)
            .astype(jnp.bfloat16)
            .reshape(span_size, HD)
        )

    new_keys = rotated(head_of(blocks[:per_head]))
    new_vals = head_of(blocks[per_head : 2 * per_head])
    own_rot = lax.dynamic_slice_in_dim(
        rotated(head_of(blocks[2 * per_head :])), (tp_rank * kv_width) % HD, kv_width, 1
    )
    mine = jnp.where(tp_rank * kv_width < KVH * HD, own_rot, kv_piece)
    new_kv = jnp.where(live_rows[:, None], mine, jnp.zeros_like(mine))
    query = rotate(
        jnp.dot(x_norm, w_query, preferred_element_type=jnp.float32).reshape(
            span_size, heads_dev, HD
        ),
        positions,
    ).astype(jnp.bfloat16)

    limit = jnp.where(
        meta_all[0] == ctx_rank, jnp.clip(my_len - meta_all[1] * BLK, 0, BLK), 0
    ).astype(jnp.int32)
    q_rows = query.transpose(1, 0, 2).reshape(heads_dev * span_size, HD)
    head_term = local_attention(
        limit, my_span.reshape(1).astype(jnp.int32), q_rows, cache_all, new_keys, new_vals, w_out
    )
    head_sum = lax.psum_scatter(head_term, "tp", scatter_dimension=1, tiled=True).astype(jnp.float32)
    mid = (resid.astype(jnp.float32) + head_sum).astype(jnp.bfloat16)
    full_mid = lax.all_gather(mid, "tp", axis=1, tiled=True)
    down_sum = lax.psum_scatter(
        feed_forward(full_mid, mlp_gain, w_gate, w_up, w_down), "tp", scatter_dimension=1, tiled=True
    ).astype(jnp.float32)
    layer_out = (mid.astype(jnp.float32) + down_sum).astype(jnp.bfloat16)
    layer_out = jnp.where(live_rows[:, None], layer_out, jnp.zeros_like(layer_out))
    return (layer_out, new_kv)


def solution(mesh):
    return jax.shard_map(
        per_device,
        mesh=mesh,
        in_specs=(
            P("ctx", "tp"),
            P(),
            P(),
            P(None, "tp"),
            P(None, "tp"),
            P("tp", None),
            P(None, "tp"),
            P(None, "tp"),
            P("tp", None),
            P("ctx", None, None),
            P(),
            P(),
            P("ctx"),
            P("ctx"),
        ),
        out_specs=(P("ctx", "tp"), P("ctx", "tp")),
        check_vma=False,
    )
```
